512 devices in a mesh: grp: 16 (over z, core), dev: 32 (over y, x).
Axes of the slice: x: 4, y: 8, z: 8, core: 2. Of those that a mesh axis runs over, the one named last changes fastest.
Arguments:
- desc: bfloat16 [2097152, 128], P(('grp', 'dev')), may hold values from -6 to 6
- positions: float32 [3, 2097152], P(None, ('grp', 'dev')), may hold values from -1 to 1
- species: int32 [2097152], P(('grp', 'dev')), may hold values from 0 to 5
- w_in: bfloat16 [128, 128], replicated, may hold values from -0.5 to 0.5
- w_mid: bfloat16 [128, 128], replicated, may hold values from -0.5 to 0.5
- w_head: float32 [128], replicated, may hold values from -0.5 to 0.5
- species_charge: float32 [6], replicated, may hold values from -1 to 1
- m2l_kernels: float32 [98, 16, 16], replicated, may hold values from -0.5 to 0.5
- expand_u: float32 [64, 16], replicated, may hold values from -1.5 to 1.5
- compress_v: float32 [64, 16], replicated, may hold values from -0.75 to 0.75
- send_list: int32 [16384, 256], P(('grp', 'dev')), may hold values from -1 to 4095, as said below
- slot_box: int32 [16384, 256], P(('grp', 'dev')), may hold values from 0 to 1023
Outputs:
- potential: float32 [2097152], P(('grp', 'dev'))
- grad_in: float32 [128, 128], replicated
- grad_mid: float32 [128, 128], replicated
- grad_head: float32 [128], replicated
- grad_species: float32 [6], replicated
The draws below stay inside these ranges and needn't reach their ends.
Inputs may be any that keep to these rules, and one draw needn't show every extreme that they name: `send_list`: each of a device's 4096 atoms stands in exactly one slot of the device's 32 rows; used slots come first in a row; in every device exactly one row has all 256 slots used and one row none.
All inputs are finite; a program needn't handle non-finite values.
Results may differ from the reference program's by a relative error of at most 0.002.
Values sent between devices are 32-bit elements; how exact they have to be, the bound alone decides.
No kernel may reach another device: no remote copies, remote signals or barrier semaphores. Data moves between devices by JAX's collectives and lax.ppermute only.
A program may use at most 64 MiB of HBM per device.

```python
import math
import jax
import jax.numpy as jnp
from jax import lax

FEAT = 128
HIDDEN_SIZE = 128
SPECIES = 6
NODES = 64
RANK = 16
OFFSETS = 98
A_DEV = 4096
BZ = 4
BX = 4
BY = 64
ATOMS = 2097152
CAP = 256
BOXES = 1024
NZ = 64
NX = 128
NY = 64
SEND_ROWS = 16384
N_DEV = 32


def draw_send_list(key, part):

    def device_list(device_key):
        key_counts, key_order, key_atoms = jax.random.split(device_key, 3)
        average = A_DEV // N_DEV
        pair_count = N_DEV // 2
        spread = jax.random.randint(key_counts, (pair_count - 1,), -(average // 2), average // 2 + 1)
        counts = jnp.concatenate([jnp.full((1,), 2 * average, jnp.int32), average + spread, jnp.zeros((1,), jnp.int32), average - spread]).astype(jnp.int32)
        counts = counts[jax.random.permutation(key_order, N_DEV)]
        starts = jnp.cumsum(counts) - counts
        ordering = jax.random.permutation(key_atoms, A_DEV).astype(jnp.int32)
        slot_index = jnp.arange(CAP, dtype=jnp.int32)[None, :]
        position = jnp.minimum(starts[:, None] + slot_index, A_DEV - 1)
        return jnp.where(slot_index < counts[:, None], ordering[position], -1).astype(jnp.int32)
    device_keys = jax.random.split(key, SEND_ROWS // N_DEV)
    return jax.vmap(device_list)(device_keys).reshape(SEND_ROWS, CAP)


def place_ends(entries, own_key, least, top_value):
    extent = entries.shape
    spot = [jax.random.randint(jax.random.fold_in(own_key, axis), (), 0, extent[axis]) for axis in range(len(extent))]
    entries = entries.at[tuple(spot)].set(least)
    longest = extent.index(max(extent))
    spot[longest] = (spot[longest] + 1) % extent[longest]
    return entries.at[tuple(spot)].set(top_value)


def block_levels(key, shape, shards, smallest, high):
    loudness = 1.0
    for axis_at, shards_of in shards:
        heights = jax.random.uniform(jax.random.fold_in(jax.random.fold_in(key, 6), axis_at), (shards_of,), jnp.float32, smallest / len(shards), high / len(shards))
        loudness = loudness * jnp.repeat(jnp.exp(heights), shape[axis_at] // shards_of).reshape((-1,) + (1,) * (len(shape) - 1 - axis_at))
    return loudness


def noise(key, shape, scale, reach, cuts=(), kind=jnp.bfloat16):
    result = jax.random.normal(key, shape, jnp.float32) * scale
    if len(cuts) > 0:
        result = block_levels(key, shape, cuts, -0.22, 0.18) * result
    return jnp.clip(result, min=-reach, max=reach).astype(kind)


def setup_inputs(seed: int = 0) -> dict:
    keys = jax.random.split(jax.random.key(seed), 13)
    return {
        "desc": noise(keys[0], (ATOMS, FEAT), 1.0, 6.0, ((0, 512),)),
        "positions": jnp.clip(jax.random.uniform(keys[1], (3, ATOMS), jnp.float32, -1.0, 1.0) * block_levels(keys[1], (3, ATOMS), ((1, 512),), -0.4, 0.0), -1.0, 1.0),
        "species": place_ends(jax.random.randint(keys[2], (ATOMS,), 0, SPECIES), jax.random.fold_in(keys[2], 1), 0, SPECIES - 1).astype(jnp.int32),
        "w_in": noise(keys[3], (FEAT, HIDDEN_SIZE), FEAT ** -0.5, 0.5),
        "w_mid": noise(keys[4], (HIDDEN_SIZE, HIDDEN_SIZE), HIDDEN_SIZE ** -0.5, 0.5),
        "w_head": noise(keys[5], (HIDDEN_SIZE,), HIDDEN_SIZE ** -0.5, 0.5, (), jnp.float32),
        "species_charge": jnp.clip(jax.random.uniform(keys[6], (SPECIES,), jnp.float32, -1.0, 1.0), -1.0, 1.0),
        "m2l_kernels": noise(keys[7], (OFFSETS, RANK, RANK), (RANK * 8) ** -0.5, 0.5, (), jnp.float32),
        "expand_u": noise(keys[8], (NODES, RANK), RANK ** -0.5, 1.5, (), jnp.float32),
        "compress_v": noise(keys[9], (NODES, RANK), NODES ** -0.5, 0.75, (), jnp.float32),
        "send_list": draw_send_list(jax.random.fold_in(keys[12], 71), 0),
        "slot_box": place_ends(jax.random.randint(keys[11], (SEND_ROWS, CAP), 0, BOXES), jax.random.fold_in(keys[11], 1), 0, BOXES - 1).astype(jnp.int32),
    }


NODE_POINTS = [math.cos((2 * node_number + 1) * math.pi / 8) for node_number in range(4)]

def chebyshev_rows(coordinate):
    order_one = coordinate
    order_two = 2.0 * coordinate * coordinate - 1.0
    order_three = 4.0 * coordinate * coordinate * coordinate - 3.0 * coordinate
    stacked = []
    for node_point in NODE_POINTS:
        cheb_two = 2.0 * node_point * node_point - 1.0
        cheb_three = 4.0 * node_point * node_point * node_point - 3.0 * node_point
        stacked.append(0.25 + 0.5 * (node_point * order_one + cheb_two * order_two + cheb_three * order_three))
    return jnp.stack(stacked, 0)

def node_weights(positions):
    along_z = chebyshev_rows(positions[0])
    along_x = chebyshev_rows(positions[1])
    along_y = chebyshev_rows(positions[2])
    product = along_z[:, None, None, :] * along_x[None, :, None, :] * along_y[None, None, :, :]
    return product.reshape(64, positions.shape[1])

def far_offsets():
    listed = []
    for shift_z in range(-2, 3):
        for shift_x in range(-2, 3):
            for shift_y in range(-2, 3):
                if max(abs(shift_z), abs(shift_x), abs(shift_y)) == 2:
                    listed.append((shift_z, shift_x, shift_y))
    return listed

def silu_slope(value):
    sigma = jax.nn.sigmoid(value)
    return sigma * (1.0 + value * (1.0 - sigma))

def reference(desc, positions, species, w_in, w_mid, w_head, species_charge, m2l_kernels, expand_u, compress_v, send_list, slot_box):
    pre_one = jnp.dot(desc, w_in, preferred_element_type=jnp.float32)
    hidden_one = jax.nn.silu(pre_one).astype(jnp.bfloat16)
    pre_two = jnp.dot(hidden_one, w_mid, preferred_element_type=jnp.float32)
    hidden_two = jax.nn.silu(pre_two)
    charge = lax.optimization_barrier(jnp.sum(hidden_two * w_head[None, :], axis=1)) + species_charge[species]
    row_number = jnp.arange(SEND_ROWS, dtype=jnp.int32)
    source = row_number // N_DEV
    target = row_number % N_DEV
    group_index = source // N_DEV
    is_used = send_list >= 0
    atom_index = jnp.where(is_used, source[:, None] * A_DEV + send_list, ATOMS).astype(jnp.int32)
    local_z = slot_box // (BX * BY)
    local_x = slot_box // BY % BX
    local_y = slot_box % BY
    global_box = ((group_index[:, None] * BZ + local_z) * NX + target[:, None] * BX + local_x) * NY + local_y
    atom_box = jnp.zeros((ATOMS,), jnp.int32).at[atom_index.reshape(-1)].set(global_box.reshape(-1).astype(jnp.int32), mode='drop')
    weight_table = node_weights(positions)
    moments = jnp.zeros((NODES, NZ * NX * NY), jnp.float32).at[:, atom_box].add(weight_table * charge[None, :])
    compressed = jnp.dot(compress_v.T, moments, precision=lax.Precision.HIGHEST).reshape(RANK, NZ, NX, NY)
    padded = jnp.pad(compressed, ((0, 0), (2, 2), (2, 2), (2, 2)))
    local_terms = jnp.zeros((RANK, NZ, NX, NY), jnp.float32)
    for offset_number, shift in enumerate(far_offsets()):
        window = padded[:, 2 + shift[0]:2 + shift[0] + NZ, 2 + shift[1]:2 + shift[1] + NX, 2 + shift[2]:2 + shift[2] + NY]
        local_terms = local_terms + jnp.einsum('ab,bzxy->azxy', m2l_kernels[offset_number], window, precision=lax.Precision.HIGHEST)
    expansion = jnp.dot(expand_u, local_terms.reshape(RANK, -1), precision=lax.Precision.HIGHEST)
    potential = lax.optimization_barrier(jnp.sum(weight_table * expansion[:, atom_box], axis=0))
    grad_scale = 1.0 / math.sqrt(ATOMS)
    grad_head = lax.optimization_barrier(jnp.sum(potential[:, None] * hidden_two, axis=0)) * grad_scale
    grad_species = jax.ops.segment_sum(potential, species, SPECIES) * grad_scale
    delta_two = (potential[:, None] * w_head[None, :] * silu_slope(pre_two)).astype(jnp.bfloat16)
    grad_mid = jnp.dot(hidden_one.T, delta_two, preferred_element_type=jnp.float32) * grad_scale
    back_one = jnp.dot(delta_two, w_mid.T, preferred_element_type=jnp.float32)
    delta_one = (back_one * silu_slope(pre_one)).astype(jnp.bfloat16)
    grad_in = jnp.dot(desc.T, delta_one, preferred_element_type=jnp.float32) * grad_scale
    return (potential, grad_in, grad_mid, grad_head, grad_species)
```

```python
import math

import jax
import jax.numpy as jnp
import numpy as np
from jax import lax
from jax.sharding import Mesh
from jax.sharding import PartitionSpec as P

NODES = 64
RANK = 16
BZ = 4
BX = 4
BY = 64
BOXES = 1024
GRP = ("grp_0", "grp_1")
DEV = ("dev_0", "dev_1")
GRP_DEV = ("grp_0", "grp_1", "dev_0", "dev_1")


NODE_POINTS = [math.cos((2 * node_number + 1) * math.pi / 8) for node_number in range(4)]


def extended_2(cells, sides, width):
    for axis, dim in sides:
        count = lax.axis_size(axis)
        ends = count - 1
        head = lax.slice_in_dim(cells, 0, width, axis=dim)
        tail = lax.slice_in_dim(cells, cells.shape[dim] - width, cells.shape[dim], axis=dim)
        cells = jnp.concatenate(
            [
                lax.ppermute(tail, axis, [(i, (i + 1) % count) for i in range(ends)]),
                cells,
                lax.ppermute(head, axis, [((i + 1) % count, i) for i in range(ends)]),
            ],
            axis=dim,
        )
    return cells


def in_blocks(x, dim, peers):
    before, after = (x.shape[:dim], x.shape[dim + 1 :])
    return jnp.moveaxis(x.reshape(*before, peers, -1, *after), dim, 0)


def sent_and_summed(x, axis, dim):
    blocks = in_blocks(x, dim, lax.axis_size(axis))
    arrived = lax.all_to_all(blocks, axis, split_axis=0, concat_axis=0, tiled=True)
    return arrived.sum(axis=0)


def sum_in_two_steps(x, axes, dim):
    far, near = axes
    blocks = in_blocks(x, dim, lax.axis_size(far))
    nearer = sent_and_summed(blocks, near, dim + 1)
    arrived = lax.all_to_all(nearer, far, split_axis=0, concat_axis=0, tiled=True)
    return arrived.sum(axis=0)


def padded_to(lines, peers):
    spare = -lines.shape[0] % peers
    if not spare:
        return lines
    return jnp.concatenate([lines, jnp.zeros((spare, *lines.shape[1:]), lines.dtype)])


def sent_to_all(x, axis):
    copies = jnp.broadcast_to(x, (lax.axis_size(axis), *x.shape))
    return lax.all_to_all(copies, axis, split_axis=0, concat_axis=0, tiled=True)


def laid_out(blocks, dim):
    dims = list(blocks.shape[1:])
    dims[dim] *= blocks.shape[0]
    return jnp.moveaxis(blocks, 0, dim).reshape(dims)


def whole_of(x, axes, dim):
    far, near = axes
    blocks = sent_to_all(sent_to_all(x, far), near)
    return laid_out(blocks.swapaxes(0, 1).reshape(-1, *x.shape), dim)


def nested_sum(x, axes):
    own = sum_in_two_steps(padded_to(x, lax.axis_size(axes[0]) * lax.axis_size(axes[1])), axes, 0)
    whole = whole_of(own, axes, 0)
    return whole[: len(x)].reshape(x.shape)


def together(arrays, axis):
    ends = [0]
    for a in arrays:
        ends.append(ends[-1] + a.size)
    total = nested_sum(jnp.concatenate([a.ravel() for a in arrays]), axis)
    return tuple((total[b:e].reshape(a.shape) for a, b, e in zip(arrays, ends, ends[1:])))


def summed_everywhere(arrays, axes):
    ends = [0]
    for a in arrays:
        ends.append(ends[-1] + a.size)
    total = lax.psum(jnp.concatenate([a.ravel() for a in arrays]), axes)
    return tuple((total[b:e].reshape(a.shape) for a, b, e in zip(arrays, ends, ends[1:])))


def shell_table():
    table = np.full((5, 5, 5), 98, dtype=np.int32)
    counter = 0
    for shift_z in range(-2, 3):
        for shift_x in range(-2, 3):
            for shift_y in range(-2, 3):
                if max(abs(shift_z), abs(shift_x), abs(shift_y)) == 2:
                    table[shift_z + 2, shift_x + 2, shift_y + 2] = counter
                    counter += 1
    return table


def chebyshev_rows(coordinate):
    order_two = 2.0 * coordinate * coordinate - 1.0
    order_three = 4.0 * coordinate * coordinate * coordinate - 3.0 * coordinate
    stacked = []
    for node_point in NODE_POINTS:
        cheb_two = 2.0 * node_point * node_point - 1.0
        cheb_three = 4.0 * node_point * node_point * node_point - 3.0 * node_point
        stacked.append(
            0.25 + 0.5 * (node_point * coordinate + cheb_two * order_two + cheb_three * order_three)
        )
    return jnp.stack(stacked, 0)


def node_weights(coords):
    along_z = chebyshev_rows(coords[0])
    along_x = chebyshev_rows(coords[1])
    along_y = chebyshev_rows(coords[2])
    product = along_z[:, None, None, :] * along_x[None, :, None, :] * along_y[None, None, :, :]
    return product.reshape(64, coords.shape[1])


def silu_slope(value):
    sigma = jax.nn.sigmoid(value)
    return sigma * (1.0 + value * (1.0 - sigma))


def translate(padded, m2l_kernels):
    rank_count = padded.shape[0]
    depth_z = padded.shape[1] - 4
    wide_x = padded.shape[2]
    depth_x = wide_x - 4
    length_y = padded.shape[3]
    y_source = jnp.arange(length_y, dtype=jnp.int32)[:, None]
    y_target = jnp.arange(length_y, dtype=jnp.int32)[None, :]
    shift_y = jnp.stack(
        [(y_source == y_target + step).astype(jnp.float32) for step in range(-2, 3)], 0
    )
    x_source = jnp.arange(wide_x, dtype=jnp.int32)[:, None]
    x_target = jnp.arange(depth_x, dtype=jnp.int32)[None, :]
    shift_x = jnp.stack(
        [(x_source == x_target + 2 + step).astype(jnp.float32) for step in range(-2, 3)], 0
    )
    shifted = jnp.einsum("gvy,bzxv->gbzxy", shift_y, padded, precision=lax.Precision.HIGHEST)
    extended = jnp.concatenate(
        [m2l_kernels, jnp.zeros((1, rank_count, rank_count), jnp.float32)], axis=0
    )
    stencil = extended[jnp.asarray(shell_table())]
    summed = jnp.zeros((rank_count, depth_z, depth_x, length_y), jnp.float32)
    for plane in range(5):
        slab = shifted[:, :, plane : plane + depth_z]
        partial_value = jnp.einsum(
            "fgab,gbzpy->afzpy", stencil[plane], slab, precision=lax.Precision.HIGHEST
        )
        summed = summed + jnp.einsum(
            "afzpy,fpq->azqy", partial_value, shift_x, precision=lax.Precision.HIGHEST
        )
    return summed


def shards(
    desc,
    positions,
    species,
    w_in,
    w_mid,
    w_head,
    species_charge,
    m2l_kernels,
    expand_u,
    compress_v,
    send_list,
    slot_box,
):
    atom_count = desc.shape[0]
    total_atoms = atom_count * lax.axis_size(GRP) * lax.axis_size(DEV)
    grad_scale = 1.0 / math.sqrt(total_atoms)
    pre_one = jnp.dot(desc, w_in, preferred_element_type=jnp.float32)
    hidden_one = jax.nn.silu(pre_one).astype(jnp.bfloat16)
    pre_two = jnp.dot(hidden_one, w_mid, preferred_element_type=jnp.float32)
    hidden_two = jax.nn.silu(pre_two)
    species_hot = (
        species[None, :] == jnp.arange(species_charge.shape[0], dtype=jnp.int32)[:, None]
    ).astype(jnp.float32)
    charge = jnp.sum(hidden_two * w_head[None, :], axis=1) + jnp.dot(
        species_charge, species_hot, precision=lax.Precision.HIGHEST
    )
    is_used = send_list >= 0
    safe_index = jnp.where(is_used, send_list, 0)
    packed = jnp.concatenate([charge[None, :], positions], axis=0)
    picked = jnp.where(is_used[None], packed[:, safe_index], 0.0)
    arrived, box_ids = (
        lax.all_to_all(picked, DEV, split_axis=1, concat_axis=1, tiled=True),
        lax.all_to_all(slot_box[None], DEV, split_axis=1, concat_axis=1, tiled=True),
    )
    arrived_charge = arrived[0].reshape(-1)
    arrived_coords = arrived[1:].reshape(3, -1)
    slot_boxes = box_ids.reshape(-1)
    weight_table = node_weights(arrived_coords)
    moments = (
        jnp.zeros((NODES, BOXES), jnp.float32)
        .at[:, slot_boxes]
        .add(weight_table * arrived_charge[None, :])
    )
    node_grid = moments.reshape(NODES, BZ, BX, BY)
    reduced = jnp.einsum("nr,nzxy->rzxy", compress_v, node_grid, precision=lax.Precision.HIGHEST)
    padded = extended_2(reduced, ((GRP, 1), (DEV, 2)), 2)
    local_terms = translate(padded, m2l_kernels)
    expansion = jnp.dot(expand_u, local_terms.reshape(RANK, BOXES), precision=lax.Precision.HIGHEST)
    slot_potential = jnp.sum(weight_table * expansion[:, slot_boxes], axis=0).reshape(
        send_list.shape
    )
    returned = lax.all_to_all(slot_potential, DEV, split_axis=0, concat_axis=0, tiled=True)
    target_rows = jnp.where(is_used, send_list, atom_count).reshape(-1)
    potential = (
        jnp.zeros((atom_count,), jnp.float32).at[target_rows].set(returned.reshape(-1), mode="drop")
    )
    head_part = jnp.sum(potential[:, None] * hidden_two, axis=0) * grad_scale
    species_part = jnp.dot(species_hot, potential, precision=lax.Precision.HIGHEST) * grad_scale
    delta_two = (potential[:, None] * w_head[None, :] * silu_slope(pre_two)).astype(jnp.bfloat16)
    mid_part = (
        lax.dot_general(
            hidden_one, delta_two, (((0,), (0,)), ((), ())), preferred_element_type=jnp.float32
        )
        * grad_scale
    )
    back_one = lax.dot_general(
        delta_two, w_mid, (((1,), (1,)), ((), ())), preferred_element_type=jnp.float32
    )
    delta_one = (back_one * silu_slope(pre_one)).astype(jnp.bfloat16)
    in_part = (
        lax.dot_general(
            desc, delta_one, (((0,), (0,)), ((), ())), preferred_element_type=jnp.float32
        )
        * grad_scale
    )
    grad_in, grad_mid, grad_head, grad_species = summed_everywhere(
        (in_part, mid_part, head_part, species_part), GRP_DEV
    )
    return (potential, grad_in, grad_mid, grad_head, grad_species)


def solution(mesh):
    torus = Mesh(mesh.devices.reshape(8, 2, 8, 4), ("grp_0", "grp_1", "dev_0", "dev_1"))
    placed = (
        P(GRP_DEV, None),
        P(None, GRP_DEV),
        P(GRP_DEV),
        P(),
        P(),
        P(),
        P(),
        P(),
        P(),
        P(),
        P(GRP_DEV, None),
        P(GRP_DEV, None),
    )
    return jax.shard_map(
        shards,
        mesh=torus,
        in_specs=placed,
        out_specs=(P(GRP_DEV), P(), P(), P(), P()),
        check_vma=False,
    )
```

```python
import math

import jax
import jax.numpy as jnp
import numpy as np
from jax import lax
from jax.experimental import pallas as pl
from jax.sharding import Mesh
from jax.sharding import PartitionSpec as P

NODES = 64
RANK = 16
BZ = 4
BX = 4
BY = 64
BOXES = 1024
GRP = ("grp_0", "grp_1")
DEV = ("dev_0", "dev_1")
GRP_DEV = ("grp_0", "grp_1", "dev_0", "dev_1")


NODE_POINTS = [math.cos((2 * node_number + 1) * math.pi / 8) for node_number in range(4)]


def extended_2(cells, sides, width):
    for axis, dim in sides:
        count = lax.axis_size(axis)
        ends = count - 1
        head = lax.slice_in_dim(cells, 0, width, axis=dim)
        tail = lax.slice_in_dim(cells, cells.shape[dim] - width, cells.shape[dim], axis=dim)
        cells = jnp.concatenate(
            [
                lax.ppermute(tail, axis, [(i, (i + 1) % count) for i in range(ends)]),
                cells,
                lax.ppermute(head, axis, [((i + 1) % count, i) for i in range(ends)]),
            ],
            axis=dim,
        )
    return cells


def in_blocks(x, dim, peers):
    before, after = (x.shape[:dim], x.shape[dim + 1 :])
    return jnp.moveaxis(x.reshape(*before, peers, -1, *after), dim, 0)


def sent_and_summed(x, axis, dim):
    blocks = in_blocks(x, dim, lax.axis_size(axis))
    arrived = lax.all_to_all(blocks, axis, split_axis=0, concat_axis=0, tiled=True)
    return arrived.sum(axis=0)


def sum_in_two_steps(x, axes, dim):
    far, near = axes
    blocks = in_blocks(x, dim, lax.axis_size(far))
    nearer = sent_and_summed(blocks, near, dim + 1)
    arrived = lax.all_to_all(nearer, far, split_axis=0, concat_axis=0, tiled=True)
    return arrived.sum(axis=0)


def padded_to(lines, peers):
    spare = -lines.shape[0] % peers
    if not spare:
        return lines
    return jnp.concatenate([lines, jnp.zeros((spare, *lines.shape[1:]), lines.dtype)])


def sent_to_all(x, axis):
    copies = jnp.broadcast_to(x, (lax.axis_size(axis), *x.shape))
    return lax.all_to_all(copies, axis, split_axis=0, concat_axis=0, tiled=True)


def laid_out(blocks, dim):
    dims = list(blocks.shape[1:])
    dims[dim] *= blocks.shape[0]
    return jnp.moveaxis(blocks, 0, dim).reshape(dims)


def whole_of(x, axes, dim):
    far, near = axes
    blocks = sent_to_all(sent_to_all(x, far), near)
    return laid_out(blocks.swapaxes(0, 1).reshape(-1, *x.shape), dim)


def nested_sum(x, axes):
    own = sum_in_two_steps(padded_to(x, lax.axis_size(axes[0]) * lax.axis_size(axes[1])), axes, 0)
    whole = whole_of(own, axes, 0)
    return whole[: len(x)].reshape(x.shape)


def together(arrays, axis):
    ends = [0]
    for a in arrays:
        ends.append(ends[-1] + a.size)
    total = nested_sum(jnp.concatenate([a.ravel() for a in arrays]), axis)
    return tuple((total[b:e].reshape(a.shape) for a, b, e in zip(arrays, ends, ends[1:])))


def summed_everywhere(arrays, axes):
    ends = [0]
    for a in arrays:
        ends.append(ends[-1] + a.size)
    total = lax.psum(jnp.concatenate([a.ravel() for a in arrays]), axes)
    return tuple((total[b:e].reshape(a.shape) for a, b, e in zip(arrays, ends, ends[1:])))


def split_three(x):
    high = lax.reduce_precision(x, exponent_bits=8, mantissa_bits=7)
    rest = x - high
    middle = lax.reduce_precision(rest, exponent_bits=8, mantissa_bits=7)
    return high, middle, rest - middle


def pieces_bf16(x, axis):
    return jnp.concatenate([p.astype(jnp.bfloat16) for p in split_three(x)], axis=axis)


def atoms_to_slots_kernel(table_ref, high_ref, low_ref, out_ref):
    rows, tile = out_ref.shape
    side = table_ref.shape[1]
    lines = lax.broadcasted_iota(jnp.int32, (side, tile), 0)
    low = (lines == low_ref[...]).astype(jnp.bfloat16)
    parts = jnp.dot(table_ref[...], low, preferred_element_type=jnp.float32)
    block = rows * side
    whole = parts[:block] + parts[block : 2 * block] + parts[2 * block :]
    high = (lines == high_ref[...]).astype(jnp.float32)
    for row in range(rows):
        out_ref[row : row + 1, :] = jnp.sum(
            whole[row * side : (row + 1) * side] * high, axis=0, keepdims=True
        )


def atoms_to_slots(values, high, low, tile=1024):
    rows, count = values.shape
    side = int(round(math.sqrt(count)))
    table = pieces_bf16(values.reshape(rows * side, side), 0)
    slots = high.shape[1]
    return pl.pallas_call(
        atoms_to_slots_kernel,
        grid=(slots // tile,),
        in_specs=[
            pl.BlockSpec(table.shape, lambda i: (0, 0)),
            pl.BlockSpec((1, tile), lambda i: (0, i)),
            pl.BlockSpec((1, tile), lambda i: (0, i)),
        ],
        out_specs=pl.BlockSpec((rows, tile), lambda i: (0, i)),
        out_shape=jax.ShapeDtypeStruct((rows, slots), jnp.float32),
    )(table, high, low)


def slots_to_atoms_kernel(value_ref, high_ref, low_ref, out_ref):
    @pl.when(pl.program_id(0) == 0)
    def _():
        out_ref[...] = jnp.zeros_like(out_ref)

    side = out_ref.shape[1]
    tile = high_ref.shape[1]
    lines = lax.broadcasted_iota(jnp.int32, (side, tile), 0)
    hit = lines == high_ref[...]
    low = (lines == low_ref[...]).astype(jnp.bfloat16)
    stacked = jnp.concatenate(
        [jnp.where(hit, value_ref[k : k + 1, :], 0.0).astype(jnp.bfloat16) for k in range(3)],
        axis=0,
    )
    out_ref[...] += lax.dot_general(
        stacked, low, (((1,), (1,)), ((), ())), preferred_element_type=jnp.float32
    )


def slots_to_atoms(values, high, low, count, tile=1024):
    side = int(round(math.sqrt(count)))
    pieces = jnp.stack(split_three(values), 0)
    slots = values.shape[0]
    parts = pl.pallas_call(
        slots_to_atoms_kernel,
        grid=(slots // tile,),
        in_specs=[
            pl.BlockSpec((3, tile), lambda i: (0, i)),
            pl.BlockSpec((1, tile), lambda i: (0, i)),
            pl.BlockSpec((1, tile), lambda i: (0, i)),
        ],
        out_specs=pl.BlockSpec((3 * side, side), lambda i: (0, 0)),
        out_shape=jax.ShapeDtypeStruct((3 * side, side), jnp.float32),
    )(pieces, high, low)
    return (parts[:side] + parts[side : 2 * side] + parts[2 * side :]).reshape(count)


def box_sum_kernel(value_ref, box_ref, out_ref):
    @pl.when(pl.program_id(0) == 0)
    def _():
        out_ref[...] = jnp.zeros_like(out_ref)

    boxes = out_ref.shape[1]
    tile = box_ref.shape[1]
    hot = (lax.broadcasted_iota(jnp.int32, (boxes, tile), 0) == box_ref[...]).astype(jnp.bfloat16)
    out_ref[...] += lax.dot_general(
        value_ref[...], hot, (((1,), (1,)), ((), ())), preferred_element_type=jnp.float32
    )


def box_sum(values, box, boxes, tile=1024):
    rows, slots = values.shape
    stacked = pieces_bf16(values, 0)
    parts = pl.pallas_call(
        box_sum_kernel,
        grid=(slots // tile,),
        in_specs=[
            pl.BlockSpec((3 * rows, tile), lambda i: (0, i)),
            pl.BlockSpec((1, tile), lambda i: (0, i)),
        ],
        out_specs=pl.BlockSpec((3 * rows, boxes), lambda i: (0, 0)),
        out_shape=jax.ShapeDtypeStruct((3 * rows, boxes), jnp.float32),
    )(stacked, box)
    return parts[:rows] + parts[rows : 2 * rows] + parts[2 * rows :]


def box_pick_kernel(table_ref, box_ref, weight_ref, out_ref):
    boxes = table_ref.shape[1]
    rows, tile = weight_ref.shape
    hot = (lax.broadcasted_iota(jnp.int32, (boxes, tile), 0) == box_ref[...]).astype(jnp.bfloat16)
    parts = jnp.dot(table_ref[...], hot, preferred_element_type=jnp.float32)
    picked = parts[:rows] + parts[rows : 2 * rows] + parts[2 * rows :]
    out_ref[...] = jnp.sum(weight_ref[...] * picked, axis=0, keepdims=True)


def box_pick(table, box, weights, tile=1024):
    rows, slots = weights.shape
    stacked = pieces_bf16(table, 0)
    return pl.pallas_call(
        box_pick_kernel,
        grid=(slots // tile,),
        in_specs=[
            pl.BlockSpec(stacked.shape, lambda i: (0, 0)),
            pl.BlockSpec((1, tile), lambda i: (0, i)),
            pl.BlockSpec((rows, tile), lambda i: (0, i)),
        ],
        out_specs=pl.BlockSpec((1, tile), lambda i: (0, i)),
        out_shape=jax.ShapeDtypeStruct((1, slots), jnp.float32),
    )(stacked, box, weights)[0]


def shell_table():
    table = np.full((5, 5, 5), 98, dtype=np.int32)
    counter = 0
    for shift_z in range(-2, 3):
        for shift_x in range(-2, 3):
            for shift_y in range(-2, 3):
                if max(abs(shift_z), abs(shift_x), abs(shift_y)) == 2:
                    table[shift_z + 2, shift_x + 2, shift_y + 2] = counter
                    counter += 1
    return table


def chebyshev_rows(coordinate):
    order_two = 2.0 * coordinate * coordinate - 1.0
    order_three = 4.0 * coordinate * coordinate * coordinate - 3.0 * coordinate
    stacked = []
    for node_point in NODE_POINTS:
        cheb_two = 2.0 * node_point * node_point - 1.0
        cheb_three = 4.0 * node_point * node_point * node_point - 3.0 * node_point
        stacked.append(
            0.25 + 0.5 * (node_point * coordinate + cheb_two * order_two + cheb_three * order_three)
        )
    return jnp.stack(stacked, 0)


def node_weights(coords):
    along_z = chebyshev_rows(coords[0])
    along_x = chebyshev_rows(coords[1])
    along_y = chebyshev_rows(coords[2])
    product = along_z[:, None, None, :] * along_x[None, :, None, :] * along_y[None, None, :, :]
    return product.reshape(64, coords.shape[1])


def silu_slope(value):
    sigma = jax.nn.sigmoid(value)
    return sigma * (1.0 + value * (1.0 - sigma))


def translate(padded, m2l_kernels):
    rank_count = padded.shape[0]
    depth_z = padded.shape[1] - 4
    wide_x = padded.shape[2]
    depth_x = wide_x - 4
    length_y = padded.shape[3]
    y_source = jnp.arange(length_y, dtype=jnp.int32)[:, None]
    y_target = jnp.arange(length_y, dtype=jnp.int32)[None, :]
    shift_y = jnp.stack(
        [(y_source == y_target + step).astype(jnp.float32) for step in range(-2, 3)], 0
    )
    x_source = jnp.arange(wide_x, dtype=jnp.int32)[:, None]
    x_target = jnp.arange(depth_x, dtype=jnp.int32)[None, :]
    shift_x = jnp.stack(
        [(x_source == x_target + 2 + step).astype(jnp.float32) for step in range(-2, 3)], 0
    )
    shifted = jnp.einsum("gvy,bzxv->gbzxy", shift_y, padded, precision=lax.Precision.HIGHEST)
    extended = jnp.concatenate(
        [m2l_kernels, jnp.zeros((1, rank_count, rank_count), jnp.float32)], axis=0
    )
    stencil = extended[jnp.asarray(shell_table())]
    summed = jnp.zeros((rank_count, depth_z, depth_x, length_y), jnp.float32)
    for plane in range(5):
        slab = shifted[:, :, plane : plane + depth_z]
        partial_value = jnp.einsum(
            "fgab,gbzpy->afzpy", stencil[plane], slab, precision=lax.Precision.HIGHEST
        )
        summed = summed + jnp.einsum(
            "afzpy,fpq->azqy", partial_value, shift_x, precision=lax.Precision.HIGHEST
        )
    return summed


def shards(
    desc,
    positions,
    species,
    w_in,
    w_mid,
    w_head,
    species_charge,
    m2l_kernels,
    expand_u,
    compress_v,
    send_list,
    slot_box,
):
    atom_count = desc.shape[0]
    total_atoms = atom_count * lax.axis_size(GRP) * lax.axis_size(DEV)
    grad_scale = 1.0 / math.sqrt(total_atoms)
    pre_one = jnp.dot(desc, w_in, preferred_element_type=jnp.float32)
    hidden_one = jax.nn.silu(pre_one).astype(jnp.bfloat16)
    pre_two = jnp.dot(hidden_one, w_mid, preferred_element_type=jnp.float32)
    hidden_two = jax.nn.silu(pre_two)
    species_hot = (
        species[None, :] == jnp.arange(species_charge.shape[0], dtype=jnp.int32)[:, None]
    ).astype(jnp.float32)
    charge = jnp.sum(hidden_two * w_head[None, :], axis=1) + jnp.dot(
        species_charge, species_hot, precision=lax.Precision.HIGHEST
    )
    is_used = send_list >= 0
    side = int(round(math.sqrt(atom_count)))
    atom_high = jnp.where(is_used, send_list // side, -1).reshape(1, -1)
    atom_low = (send_list % side).reshape(1, -1)
    packed = jnp.concatenate([charge[None, :], positions], axis=0)
    picked = atoms_to_slots(packed, atom_high, atom_low).reshape(4, *send_list.shape)
    arrived, box_ids = (
        lax.all_to_all(picked, DEV, split_axis=1, concat_axis=1, tiled=True),
        lax.all_to_all(slot_box[None], DEV, split_axis=1, concat_axis=1, tiled=True),
    )
    arrived_charge = arrived[0].reshape(-1)
    arrived_coords = arrived[1:].reshape(3, -1)
    slot_boxes = box_ids.reshape(-1)
    weight_table = node_weights(arrived_coords)
    moments = box_sum(weight_table * arrived_charge[None, :], slot_boxes[None, :], BOXES)
    node_grid = moments.reshape(NODES, BZ, BX, BY)
    reduced = jnp.einsum("nr,nzxy->rzxy", compress_v, node_grid, precision=lax.Precision.HIGHEST)
    padded = extended_2(reduced, ((GRP, 1), (DEV, 2)), 2)
    local_terms = translate(padded, m2l_kernels)
    expansion = jnp.dot(expand_u, local_terms.reshape(RANK, BOXES), precision=lax.Precision.HIGHEST)
    slot_potential = box_pick(expansion, slot_boxes[None, :], weight_table).reshape(
        send_list.shape
    )
    returned = lax.all_to_all(slot_potential, DEV, split_axis=0, concat_axis=0, tiled=True)
    potential = slots_to_atoms(returned.reshape(-1), atom_high, atom_low, atom_count)
    head_part = jnp.sum(potential[:, None] * hidden_two, axis=0) * grad_scale
    species_part = jnp.dot(species_hot, potential, precision=lax.Precision.HIGHEST) * grad_scale
    delta_two = (potential[:, None] * w_head[None, :] * silu_slope(pre_two)).astype(jnp.bfloat16)
    mid_part = (
        lax.dot_general(
            hidden_one, delta_two, (((0,), (0,)), ((), ())), preferred_element_type=jnp.float32
        )
        * grad_scale
    )
    back_one = lax.dot_general(
        delta_two, w_mid, (((1,), (1,)), ((), ())), preferred_element_type=jnp.float32
    )
    delta_one = (back_one * silu_slope(pre_one)).astype(jnp.bfloat16)
    in_part = (
        lax.dot_general(
            desc, delta_one, (((0,), (0,)), ((), ())), preferred_element_type=jnp.float32
        )
        * grad_scale
    )
    grad_in, grad_mid, grad_head, grad_species = together(
        (in_part, mid_part, head_part, species_part), ("grp_0", ("grp_1", "dev_0", "dev_1"))
    )
    return (potential, grad_in, grad_mid, grad_head, grad_species)


def solution(mesh):
    torus = Mesh(mesh.devices.reshape(8, 2, 8, 4), ("grp_0", "grp_1", "dev_0", "dev_1"))
    placed = (
        P(GRP_DEV, None),
        P(None, GRP_DEV),
        P(GRP_DEV),
        P(),
        P(),
        P(),
        P(),
        P(),
        P(),
        P(),
        P(GRP_DEV, None),
        P(GRP_DEV, None),
    )
    return jax.shard_map(
        shards,
        mesh=torus,
        in_specs=placed,
        out_specs=(P(GRP_DEV), P(), P(), P(), P()),
        check_vma=False,
    )
```

```python
import math

import jax
import jax.numpy as jnp
import numpy as np
from jax import lax
from jax.experimental import pallas as pl
from jax.sharding import Mesh
from jax.sharding import PartitionSpec as P

NODES = 64
RANK = 16
BZ = 4
BX = 4
BY = 64
BOXES = 1024
GRP = ("grp_0", "grp_1")
DEV = ("dev_0", "dev_1")
GRP_DEV = ("grp_0", "grp_1", "dev_0", "dev_1")


NODE_POINTS = [math.cos((2 * node_number + 1) * math.pi / 8) for node_number in range(4)]


def extended_2(cells, sides, width):
    for axis, dim in sides:
        count = lax.axis_size(axis)
        ends = count - 1
        head = lax.slice_in_dim(cells, 0, width, axis=dim)
        tail = lax.slice_in_dim(cells, cells.shape[dim] - width, cells.shape[dim], axis=dim)
        cells = jnp.concatenate(
            [
                lax.ppermute(tail, axis, [(i, (i + 1) % count) for i in range(ends)]),
                cells,
                lax.ppermute(head, axis, [((i + 1) % count, i) for i in range(ends)]),
            ],
            axis=dim,
        )
    return cells


def in_blocks(x, dim, peers):
    before, after = (x.shape[:dim], x.shape[dim + 1 :])
    return jnp.moveaxis(x.reshape(*before, peers, -1, *after), dim, 0)


def sent_and_summed(x, axis, dim):
    blocks = in_blocks(x, dim, lax.axis_size(axis))
    arrived = lax.all_to_all(blocks, axis, split_axis=0, concat_axis=0, tiled=True)
    return arrived.sum(axis=0)


def sum_in_two_steps(x, axes, dim):
    far, near = axes
    blocks = in_blocks(x, dim, lax.axis_size(far))
    nearer = sent_and_summed(blocks, near, dim + 1)
    arrived = lax.all_to_all(nearer, far, split_axis=0, concat_axis=0, tiled=True)
    return arrived.sum(axis=0)


def padded_to(lines, peers):
    spare = -lines.shape[0] % peers
    if not spare:
        return lines
    return jnp.concatenate([lines, jnp.zeros((spare, *lines.shape[1:]), lines.dtype)])


def sent_to_all(x, axis):
    copies = jnp.broadcast_to(x, (lax.axis_size(axis), *x.shape))
    return lax.all_to_all(copies, axis, split_axis=0, concat_axis=0, tiled=True)


def laid_out(blocks, dim):
    dims = list(blocks.shape[1:])
    dims[dim] *= blocks.shape[0]
    return jnp.moveaxis(blocks, 0, dim).reshape(dims)


def whole_of(x, axes, dim):
    far, near = axes
    blocks = sent_to_all(sent_to_all(x, far), near)
    return laid_out(blocks.swapaxes(0, 1).reshape(-1, *x.shape), dim)


def nested_sum(x, axes):
    own = sum_in_two_steps(padded_to(x, lax.axis_size(axes[0]) * lax.axis_size(axes[1])), axes, 0)
    whole = whole_of(own, axes, 0)
    return whole[: len(x)].reshape(x.shape)


def together(arrays, axis):
    ends = [0]
    for a in arrays:
        ends.append(ends[-1] + a.size)
    total = nested_sum(jnp.concatenate([a.ravel() for a in arrays]), axis)
    return tuple((total[b:e].reshape(a.shape) for a, b, e in zip(arrays, ends, ends[1:])))


def swapped(x, axis, step):
    count = lax.axis_size(axis)
    return lax.ppermute(x, axis, [(i, i ^ step) for i in range(count)])


def butterfly_sum(x, axis):
    step = 1
    while step < lax.axis_size(axis):
        x = x + swapped(x, axis, step)
        step *= 2
    return x


def hybrid_sum(x, pair, plane, stack):
    length = x.shape[0]
    x = butterfly_sum(x, pair)
    peers = lax.axis_size(plane)
    lines = padded_to(x, peers).reshape(peers, -1)
    own = lax.all_to_all(lines, plane, 0, 0, tiled=True).reshape(peers, -1).sum(axis=0)
    own = butterfly_sum(own, stack)
    copies = jnp.broadcast_to(own, (peers, *own.shape))
    return lax.all_to_all(copies, plane, 0, 0, tiled=True).reshape(-1)[:length]


def summed_everywhere(arrays):
    ends = [0]
    for a in arrays:
        ends.append(ends[-1] + a.size)
    flat = jnp.concatenate([a.ravel() for a in arrays])
    total = hybrid_sum(flat, "grp_1", DEV, "grp_0")
    return tuple((total[b:e].reshape(a.shape) for a, b, e in zip(arrays, ends, ends[1:])))


def split_three(x):
    high = lax.reduce_precision(x, exponent_bits=8, mantissa_bits=7)
    rest = x - high
    middle = lax.reduce_precision(rest, exponent_bits=8, mantissa_bits=7)
    return high, middle, rest - middle


def pieces_bf16(x, axis):
    return jnp.concatenate([p.astype(jnp.bfloat16) for p in split_three(x)], axis=axis)


def atoms_to_slots_kernel(table_ref, high_ref, low_ref, out_ref):
    rows, tile = out_ref.shape
    side = table_ref.shape[1]
    lines = lax.broadcasted_iota(jnp.int32, (side, tile), 0)
    low = (lines == low_ref[...]).astype(jnp.bfloat16)
    parts = jnp.dot(table_ref[...], low, preferred_element_type=jnp.float32)
    block = rows * side
    whole = parts[:block] + parts[block : 2 * block] + parts[2 * block :]
    high = (lines == high_ref[...]).astype(jnp.float32)
    for row in range(rows):
        out_ref[row : row + 1, :] = jnp.sum(
            whole[row * side : (row + 1) * side] * high, axis=0, keepdims=True
        )


def atoms_to_slots(values, high, low, tile=1024):
    rows, count = values.shape
    side = int(round(math.sqrt(count)))
    table = pieces_bf16(values.reshape(rows * side, side), 0)
    slots = high.shape[1]
    return pl.pallas_call(
        atoms_to_slots_kernel,
        grid=(slots // tile,),
        in_specs=[
            pl.BlockSpec(table.shape, lambda i: (0, 0)),
            pl.BlockSpec((1, tile), lambda i: (0, i)),
            pl.BlockSpec((1, tile), lambda i: (0, i)),
        ],
        out_specs=pl.BlockSpec((rows, tile), lambda i: (0, i)),
        out_shape=jax.ShapeDtypeStruct((rows, slots), jnp.float32),
    )(table, high, low)


def slots_to_atoms_kernel(value_ref, high_ref, low_ref, out_ref):
    @pl.when(pl.program_id(0) == 0)
    def _():
        out_ref[...] = jnp.zeros_like(out_ref)

    side = out_ref.shape[1]
    tile = high_ref.shape[1]
    lines = lax.broadcasted_iota(jnp.int32, (side, tile), 0)
    hit = lines == high_ref[...]
    low = (lines == low_ref[...]).astype(jnp.bfloat16)
    stacked = jnp.concatenate(
        [jnp.where(hit, value_ref[k : k + 1, :], 0.0).astype(jnp.bfloat16) for k in range(3)],
        axis=0,
    )
    out_ref[...] += lax.dot_general(
        stacked, low, (((1,), (1,)), ((), ())), preferred_element_type=jnp.float32
    )


def slots_to_atoms(values, high, low, count, tile=1024):
    side = int(round(math.sqrt(count)))
    pieces = jnp.stack(split_three(values), 0)
    slots = values.shape[0]
    parts = pl.pallas_call(
        slots_to_atoms_kernel,
        grid=(slots // tile,),
        in_specs=[
            pl.BlockSpec((3, tile), lambda i: (0, i)),
            pl.BlockSpec((1, tile), lambda i: (0, i)),
            pl.BlockSpec((1, tile), lambda i: (0, i)),
        ],
        out_specs=pl.BlockSpec((3 * side, side), lambda i: (0, 0)),
        out_shape=jax.ShapeDtypeStruct((3 * side, side), jnp.float32),
    )(pieces, high, low)
    return (parts[:side] + parts[side : 2 * side] + parts[2 * side :]).reshape(count)


def box_sum_kernel(value_ref, box_ref, out_ref):
    @pl.when(pl.program_id(0) == 0)
    def _():
        out_ref[...] = jnp.zeros_like(out_ref)

    boxes = out_ref.shape[1]
    tile = box_ref.shape[1]
    hot = (lax.broadcasted_iota(jnp.int32, (boxes, tile), 0) == box_ref[...]).astype(jnp.bfloat16)
    out_ref[...] += lax.dot_general(
        value_ref[...], hot, (((1,), (1,)), ((), ())), preferred_element_type=jnp.float32
    )


def box_sum(values, box, boxes, tile=1024):
    rows, slots = values.shape
    stacked = pieces_bf16(values, 0)
    parts = pl.pallas_call(
        box_sum_kernel,
        grid=(slots // tile,),
        in_specs=[
            pl.BlockSpec((3 * rows, tile), lambda i: (0, i)),
            pl.BlockSpec((1, tile), lambda i: (0, i)),
        ],
        out_specs=pl.BlockSpec((3 * rows, boxes), lambda i: (0, 0)),
        out_shape=jax.ShapeDtypeStruct((3 * rows, boxes), jnp.float32),
    )(stacked, box)
    return parts[:rows] + parts[rows : 2 * rows] + parts[2 * rows :]


def box_pick_kernel(table_ref, box_ref, weight_ref, out_ref):
    boxes = table_ref.shape[1]
    rows, tile = weight_ref.shape
    hot = (lax.broadcasted_iota(jnp.int32, (boxes, tile), 0) == box_ref[...]).astype(jnp.bfloat16)
    parts = jnp.dot(table_ref[...], hot, preferred_element_type=jnp.float32)
    picked = parts[:rows] + parts[rows : 2 * rows] + parts[2 * rows :]
    out_ref[...] = jnp.sum(weight_ref[...] * picked, axis=0, keepdims=True)


def box_pick(table, box, weights, tile=1024):
    rows, slots = weights.shape
    stacked = pieces_bf16(table, 0)
    return pl.pallas_call(
        box_pick_kernel,
        grid=(slots // tile,),
        in_specs=[
            pl.BlockSpec(stacked.shape, lambda i: (0, 0)),
            pl.BlockSpec((1, tile), lambda i: (0, i)),
            pl.BlockSpec((rows, tile), lambda i: (0, i)),
        ],
        out_specs=pl.BlockSpec((1, tile), lambda i: (0, i)),
        out_shape=jax.ShapeDtypeStruct((1, slots), jnp.float32),
    )(stacked, box, weights)[0]


def shell_table():
    table = np.full((5, 5, 5), 98, dtype=np.int32)
    counter = 0
    for shift_z in range(-2, 3):
        for shift_x in range(-2, 3):
            for shift_y in range(-2, 3):
                if max(abs(shift_z), abs(shift_x), abs(shift_y)) == 2:
                    table[shift_z + 2, shift_x + 2, shift_y + 2] = counter
                    counter += 1
    return table


def chebyshev_rows(coordinate):
    order_two = 2.0 * coordinate * coordinate - 1.0
    order_three = 4.0 * coordinate * coordinate * coordinate - 3.0 * coordinate
    stacked = []
    for node_point in NODE_POINTS:
        cheb_two = 2.0 * node_point * node_point - 1.0
        cheb_three = 4.0 * node_point * node_point * node_point - 3.0 * node_point
        stacked.append(
            0.25 + 0.5 * (node_point * coordinate + cheb_two * order_two + cheb_three * order_three)
        )
    return jnp.stack(stacked, 0)


def node_weights(coords):
    along_z = chebyshev_rows(coords[0])
    along_x = chebyshev_rows(coords[1])
    along_y = chebyshev_rows(coords[2])
    product = along_z[:, None, None, :] * along_x[None, :, None, :] * along_y[None, None, :, :]
    return product.reshape(64, coords.shape[1])


def silu_slope(value):
    sigma = jax.nn.sigmoid(value)
    return sigma * (1.0 + value * (1.0 - sigma))


def translate(padded, m2l_kernels):
    rank_count = padded.shape[0]
    depth_z = padded.shape[1] - 4
    wide_x = padded.shape[2]
    depth_x = wide_x - 4
    length_y = padded.shape[3]
    y_source = jnp.arange(length_y, dtype=jnp.int32)[:, None]
    y_target = jnp.arange(length_y, dtype=jnp.int32)[None, :]
    shift_y = jnp.stack(
        [(y_source == y_target + step).astype(jnp.float32) for step in range(-2, 3)], 0
    )
    x_source = jnp.arange(wide_x, dtype=jnp.int32)[:, None]
    x_target = jnp.arange(depth_x, dtype=jnp.int32)[None, :]
    shift_x = jnp.stack(
        [(x_source == x_target + 2 + step).astype(jnp.float32) for step in range(-2, 3)], 0
    )
    shifted = jnp.einsum("gvy,bzxv->gbzxy", shift_y, padded, precision=lax.Precision.HIGHEST)
    extended = jnp.concatenate(
        [m2l_kernels, jnp.zeros((1, rank_count, rank_count), jnp.float32)], axis=0
    )
    stencil = extended[jnp.asarray(shell_table())]
    summed = jnp.zeros((rank_count, depth_z, depth_x, length_y), jnp.float32)
    for plane in range(5):
        slab = shifted[:, :, plane : plane + depth_z]
        partial_value = jnp.einsum(
            "fgab,gbzpy->afzpy", stencil[plane], slab, precision=lax.Precision.HIGHEST
        )
        summed = summed + jnp.einsum(
            "afzpy,fpq->azqy", partial_value, shift_x, precision=lax.Precision.HIGHEST
        )
    return summed


def shards(
    desc,
    positions,
    species,
    w_in,
    w_mid,
    w_head,
    species_charge,
    m2l_kernels,
    expand_u,
    compress_v,
    send_list,
    slot_box,
):
    atom_count = desc.shape[0]
    total_atoms = atom_count * lax.axis_size(GRP) * lax.axis_size(DEV)
    grad_scale = 1.0 / math.sqrt(total_atoms)
    pre_one = jnp.dot(desc, w_in, preferred_element_type=jnp.float32)
    hidden_one = jax.nn.silu(pre_one).astype(jnp.bfloat16)
    pre_two = jnp.dot(hidden_one, w_mid, preferred_element_type=jnp.float32)
    hidden_two = jax.nn.silu(pre_two)
    species_hot = (
        species[None, :] == jnp.arange(species_charge.shape[0], dtype=jnp.int32)[:, None]
    ).astype(jnp.float32)
    charge = jnp.sum(hidden_two * w_head[None, :], axis=1) + jnp.dot(
        species_charge, species_hot, precision=lax.Precision.HIGHEST
    )
    is_used = send_list >= 0
    side = int(round(math.sqrt(atom_count)))
    atom_high = jnp.where(is_used, send_list // side, -1).reshape(1, -1)
    atom_low = (send_list % side).reshape(1, -1)
    packed = jnp.concatenate([charge[None, :], positions], axis=0)
    picked = atoms_to_slots(packed, atom_high, atom_low).reshape(4, *send_list.shape)
    outgoing = jnp.concatenate([picked, slot_box[None].astype(jnp.float32)], axis=0)
    arrived = lax.all_to_all(outgoing, DEV, split_axis=1, concat_axis=1, tiled=True)
    arrived_charge = arrived[0].reshape(-1)
    arrived_coords = arrived[1:4].reshape(3, -1)
    slot_boxes = arrived[4].reshape(-1).astype(jnp.int32)
    weight_table = node_weights(arrived_coords)
    moments = box_sum(weight_table * arrived_charge[None, :], slot_boxes[None, :], BOXES)
    node_grid = moments.reshape(NODES, BZ, BX, BY)
    reduced = jnp.einsum("nr,nzxy->rzxy", compress_v, node_grid, precision=lax.Precision.HIGHEST)
    padded = extended_2(reduced, ((GRP, 1), (DEV, 2)), 2)
    local_terms = translate(padded, m2l_kernels)
    expansion = jnp.dot(expand_u, local_terms.reshape(RANK, BOXES), precision=lax.Precision.HIGHEST)
    slot_potential = box_pick(expansion, slot_boxes[None, :], weight_table).reshape(
        send_list.shape
    )
    returned = lax.all_to_all(slot_potential, DEV, split_axis=0, concat_axis=0, tiled=True)
    potential = slots_to_atoms(returned.reshape(-1), atom_high, atom_low, atom_count)
    head_part = jnp.sum(potential[:, None] * hidden_two, axis=0) * grad_scale
    species_part = jnp.dot(species_hot, potential, precision=lax.Precision.HIGHEST) * grad_scale
    delta_two = (potential[:, None] * w_head[None, :] * silu_slope(pre_two)).astype(jnp.bfloat16)
    mid_part = (
        lax.dot_general(
            hidden_one, delta_two, (((0,), (0,)), ((), ())), preferred_element_type=jnp.float32
        )
        * grad_scale
    )
    back_one = lax.dot_general(
        delta_two, w_mid, (((1,), (1,)), ((), ())), preferred_element_type=jnp.float32
    )
    delta_one = (back_one * silu_slope(pre_one)).astype(jnp.bfloat16)
    in_part = (
        lax.dot_general(
            desc, delta_one, (((0,), (0,)), ((), ())), preferred_element_type=jnp.float32
        )
        * grad_scale
    )
    grad_in, grad_mid, grad_head, grad_species = summed_everywhere(
        (in_part, mid_part, head_part, species_part)
    )
    return (potential, grad_in, grad_mid, grad_head, grad_species)


def solution(mesh):
    torus = Mesh(mesh.devices.reshape(8, 2, 8, 4), ("grp_0", "grp_1", "dev_0", "dev_1"))
    placed = (
        P(GRP_DEV, None),
        P(None, GRP_DEV),
        P(GRP_DEV),
        P(),
        P(),
        P(),
        P(),
        P(),
        P(),
        P(),
        P(GRP_DEV, None),
        P(GRP_DEV, None),
    )
    return jax.shard_map(
        shards,
        mesh=torus,
        in_specs=placed,
        out_specs=(P(GRP_DEV), P(), P(), P(), P()),
        check_vma=False,
    )
```

```python
import math

import jax
import jax.numpy as jnp
import numpy as np
from jax import lax
from jax.experimental import pallas as pl
from jax.sharding import Mesh
from jax.sharding import PartitionSpec as P

NODES = 64
RANK = 16
BZ = 4
BX = 4
BY = 64
BOXES = 1024
GRP = ("grp_0", "grp_1")
DEV = ("dev_0", "dev_1")
GRP_DEV = ("grp_0", "grp_1", "dev_0", "dev_1")


NODE_POINTS = [math.cos((2 * node_number + 1) * math.pi / 8) for node_number in range(4)]


def extended_2(cells, sides, width):
    for axis, dim in sides:
        count = lax.axis_size(axis)
        ends = count - 1
        head = lax.slice_in_dim(cells, 0, width, axis=dim)
        tail = lax.slice_in_dim(cells, cells.shape[dim] - width, cells.shape[dim], axis=dim)
        cells = jnp.concatenate(
            [
                lax.ppermute(tail, axis, [(i, (i + 1) % count) for i in range(ends)]),
                cells,
                lax.ppermute(head, axis, [((i + 1) % count, i) for i in range(ends)]),
            ],
            axis=dim,
        )
    return cells


def in_blocks(x, dim, peers):
    before, after = (x.shape[:dim], x.shape[dim + 1 :])
    return jnp.moveaxis(x.reshape(*before, peers, -1, *after), dim, 0)


def sent_and_summed(x, axis, dim):
    blocks = in_blocks(x, dim, lax.axis_size(axis))
    arrived = lax.all_to_all(blocks, axis, split_axis=0, concat_axis=0, tiled=True)
    return arrived.sum(axis=0)


def sum_in_two_steps(x, axes, dim):
    far, near = axes
    blocks = in_blocks(x, dim, lax.axis_size(far))
    nearer = sent_and_summed(blocks, near, dim + 1)
    arrived = lax.all_to_all(nearer, far, split_axis=0, concat_axis=0, tiled=True)
    return arrived.sum(axis=0)


def padded_to(lines, peers):
    spare = -lines.shape[0] % peers
    if not spare:
        return lines
    return jnp.concatenate([lines, jnp.zeros((spare, *lines.shape[1:]), lines.dtype)])


def sent_to_all(x, axis):
    copies = jnp.broadcast_to(x, (lax.axis_size(axis), *x.shape))
    return lax.all_to_all(copies, axis, split_axis=0, concat_axis=0, tiled=True)


def laid_out(blocks, dim):
    dims = list(blocks.shape[1:])
    dims[dim] *= blocks.shape[0]
    return jnp.moveaxis(blocks, 0, dim).reshape(dims)


def whole_of(x, axes, dim):
    far, near = axes
    blocks = sent_to_all(sent_to_all(x, far), near)
    return laid_out(blocks.swapaxes(0, 1).reshape(-1, *x.shape), dim)


def nested_sum(x, axes):
    own = sum_in_two_steps(padded_to(x, lax.axis_size(axes[0]) * lax.axis_size(axes[1])), axes, 0)
    whole = whole_of(own, axes, 0)
    return whole[: len(x)].reshape(x.shape)


def together(arrays, axis):
    ends = [0]
    for a in arrays:
        ends.append(ends[-1] + a.size)
    total = nested_sum(jnp.concatenate([a.ravel() for a in arrays]), axis)
    return tuple((total[b:e].reshape(a.shape) for a, b, e in zip(arrays, ends, ends[1:])))


def swapped(x, axis, step):
    count = lax.axis_size(axis)
    return lax.ppermute(x, axis, [(i, i ^ step) for i in range(count)])


def butterfly_sum(x, axis):
    step = 1
    while step < lax.axis_size(axis):
        x = x + swapped(x, axis, step)
        step *= 2
    return x


def hybrid_sum(x, pair, plane, stack):
    length = x.shape[0]
    x = butterfly_sum(x, pair)
    peers = lax.axis_size(plane)
    lines = padded_to(x, peers).reshape(peers, -1)
    own = lax.all_to_all(lines, plane, 0, 0, tiled=True).reshape(peers, -1).sum(axis=0)
    own = butterfly_sum(own, stack)
    copies = jnp.broadcast_to(own, (peers, *own.shape))
    return lax.all_to_all(copies, plane, 0, 0, tiled=True).reshape(-1)[:length]


def summed_everywhere(arrays):
    ends = [0]
    for a in arrays:
        ends.append(ends[-1] + a.size)
    flat = jnp.concatenate([a.ravel() for a in arrays])
    total = hybrid_sum(flat, "grp_1", DEV, "grp_0")
    return tuple((total[b:e].reshape(a.shape) for a, b, e in zip(arrays, ends, ends[1:])))


def split_three(x):
    high = lax.reduce_precision(x, exponent_bits=8, mantissa_bits=7)
    rest = x - high
    middle = lax.reduce_precision(rest, exponent_bits=8, mantissa_bits=7)
    return high, middle, rest - middle


def pieces_bf16(x, axis):
    return jnp.concatenate([p.astype(jnp.bfloat16) for p in split_three(x)], axis=axis)


def atoms_to_slots_kernel(table_ref, high_ref, low_ref, out_ref):
    rows, tile = out_ref.shape
    side = table_ref.shape[1]
    lines = lax.broadcasted_iota(jnp.int32, (side, tile), 0)
    low = (lines == low_ref[...]).astype(jnp.bfloat16)
    parts = jnp.dot(table_ref[...], low, preferred_element_type=jnp.float32)
    block = rows * side
    whole = parts[:block] + parts[block : 2 * block] + parts[2 * block :]
    high = (lines == high_ref[...]).astype(jnp.float32)
    for row in range(rows):
        out_ref[row : row + 1, :] = jnp.sum(
            whole[row * side : (row + 1) * side] * high, axis=0, keepdims=True
        )


def atoms_to_slots(values, high, low, tile=1024):
    rows, count = values.shape
    side = int(round(math.sqrt(count)))
    table = pieces_bf16(values.reshape(rows * side, side), 0)
    slots = high.shape[1]
    return pl.pallas_call(
        atoms_to_slots_kernel,
        grid=(slots // tile,),
        in_specs=[
            pl.BlockSpec(table.shape, lambda i: (0, 0)),
            pl.BlockSpec((1, tile), lambda i: (0, i)),
            pl.BlockSpec((1, tile), lambda i: (0, i)),
        ],
        out_specs=pl.BlockSpec((rows, tile), lambda i: (0, i)),
        out_shape=jax.ShapeDtypeStruct((rows, slots), jnp.float32),
    )(table, high, low)


def slots_to_atoms_kernel(value_ref, high_ref, low_ref, out_ref):
    @pl.when(pl.program_id(0) == 0)
    def _():
        out_ref[...] = jnp.zeros_like(out_ref)

    side = out_ref.shape[1]
    tile = high_ref.shape[1]
    lines = lax.broadcasted_iota(jnp.int32, (side, tile), 0)
    hit = lines == high_ref[...]
    low = (lines == low_ref[...]).astype(jnp.bfloat16)
    stacked = jnp.concatenate(
        [jnp.where(hit, value_ref[k : k + 1, :], 0.0).astype(jnp.bfloat16) for k in range(3)],
        axis=0,
    )
    out_ref[...] += lax.dot_general(
        stacked, low, (((1,), (1,)), ((), ())), preferred_element_type=jnp.float32
    )


def slots_to_atoms(values, high, low, count, tile=1024):
    side = int(round(math.sqrt(count)))
    pieces = jnp.stack(split_three(values), 0)
    slots = values.shape[0]
    parts = pl.pallas_call(
        slots_to_atoms_kernel,
        grid=(slots // tile,),
        in_specs=[
            pl.BlockSpec((3, tile), lambda i: (0, i)),
            pl.BlockSpec((1, tile), lambda i: (0, i)),
            pl.BlockSpec((1, tile), lambda i: (0, i)),
        ],
        out_specs=pl.BlockSpec((3 * side, side), lambda i: (0, 0)),
        out_shape=jax.ShapeDtypeStruct((3 * side, side), jnp.float32),
    )(pieces, high, low)
    return (parts[:side] + parts[side : 2 * side] + parts[2 * side :]).reshape(count)


def node_rows(data_ref, tile):
    nodes = lax.broadcasted_iota(jnp.int32, (NODES, tile), 0)
    spread = []
    for axis, shift in ((0, 4), (1, 2), (2, 0)):
        u = data_ref[1 + axis : 2 + axis, :]
        order_two = 2.0 * u * u - 1.0
        order_three = 4.0 * u * u * u - 3.0 * u
        rows = []
        for node_point in NODE_POINTS:
            cheb_two = 2.0 * node_point * node_point - 1.0
            cheb_three = 4.0 * node_point * node_point * node_point - 3.0 * node_point
            rows.append(0.25 + 0.5 * (node_point * u + cheb_two * order_two + cheb_three * order_three))
        pick = jnp.bitwise_and(jnp.right_shift(nodes, shift), 3)
        full = jnp.broadcast_to(rows[3], (NODES, tile))
        for p in range(3):
            full = jnp.where(pick == p, rows[p], full)
        spread.append(full)
    return spread[0] * spread[1] * spread[2]


def bf16_pieces_in_kernel(x):
    high = x.astype(jnp.bfloat16)
    rest = x - high.astype(jnp.float32)
    middle = rest.astype(jnp.bfloat16)
    low = (rest - middle.astype(jnp.float32)).astype(jnp.bfloat16)
    return jnp.concatenate([high, middle, low], axis=0)


def box_sum_kernel(data_ref, out_ref):
    @pl.when(pl.program_id(0) == 0)
    def _():
        out_ref[...] = jnp.zeros_like(out_ref)

    boxes = out_ref.shape[1]
    tile = data_ref.shape[1]
    box = data_ref[4:5, :].astype(jnp.int32)
    weighted = node_rows(data_ref, tile) * data_ref[0:1, :]
    hot = (lax.broadcasted_iota(jnp.int32, (boxes, tile), 0) == box).astype(jnp.bfloat16)
    out_ref[...] += lax.dot_general(
        bf16_pieces_in_kernel(weighted), hot, (((1,), (1,)), ((), ())),
        preferred_element_type=jnp.float32,
    )


def box_sum(data, boxes, tile=1024):
    rows, slots = data.shape
    parts = pl.pallas_call(
        box_sum_kernel,
        grid=(slots // tile,),
        in_specs=[pl.BlockSpec((rows, tile), lambda i: (0, i))],
        out_specs=pl.BlockSpec((3 * NODES, boxes), lambda i: (0, 0)),
        out_shape=jax.ShapeDtypeStruct((3 * NODES, boxes), jnp.float32),
    )(data)
    return parts[:NODES] + parts[NODES : 2 * NODES] + parts[2 * NODES :]


def box_pick_kernel(table_ref, data_ref, out_ref):
    boxes = table_ref.shape[1]
    tile = data_ref.shape[1]
    box = data_ref[4:5, :].astype(jnp.int32)
    hot = (lax.broadcasted_iota(jnp.int32, (boxes, tile), 0) == box).astype(jnp.bfloat16)
    parts = jnp.dot(table_ref[...], hot, preferred_element_type=jnp.float32)
    picked = parts[:NODES] + parts[NODES : 2 * NODES] + parts[2 * NODES :]
    out_ref[...] = jnp.sum(node_rows(data_ref, tile) * picked, axis=0, keepdims=True)


def box_pick(table, data, tile=1024):
    rows, slots = data.shape
    stacked = pieces_bf16(table, 0)
    return pl.pallas_call(
        box_pick_kernel,
        grid=(slots // tile,),
        in_specs=[
            pl.BlockSpec(stacked.shape, lambda i: (0, 0)),
            pl.BlockSpec((rows, tile), lambda i: (0, i)),
        ],
        out_specs=pl.BlockSpec((1, tile), lambda i: (0, i)),
        out_shape=jax.ShapeDtypeStruct((1, slots), jnp.float32),
    )(stacked, data)[0]


def shell_table():
    table = np.full((5, 5, 5), 98, dtype=np.int32)
    counter = 0
    for shift_z in range(-2, 3):
        for shift_x in range(-2, 3):
            for shift_y in range(-2, 3):
                if max(abs(shift_z), abs(shift_x), abs(shift_y)) == 2:
                    table[shift_z + 2, shift_x + 2, shift_y + 2] = counter
                    counter += 1
    return table


def chebyshev_rows(coordinate):
    order_two = 2.0 * coordinate * coordinate - 1.0
    order_three = 4.0 * coordinate * coordinate * coordinate - 3.0 * coordinate
    stacked = []
    for node_point in NODE_POINTS:
        cheb_two = 2.0 * node_point * node_point - 1.0
        cheb_three = 4.0 * node_point * node_point * node_point - 3.0 * node_point
        stacked.append(
            0.25 + 0.5 * (node_point * coordinate + cheb_two * order_two + cheb_three * order_three)
        )
    return jnp.stack(stacked, 0)


def node_weights(coords):
    along_z = chebyshev_rows(coords[0])
    along_x = chebyshev_rows(coords[1])
    along_y = chebyshev_rows(coords[2])
    product = along_z[:, None, None, :] * along_x[None, :, None, :] * along_y[None, None, :, :]
    return product.reshape(64, coords.shape[1])


def silu_slope(value):
    sigma = jax.nn.sigmoid(value)
    return sigma * (1.0 + value * (1.0 - sigma))


def translate(padded, m2l_kernels):
    rank_count = padded.shape[0]
    depth_z = padded.shape[1] - 4
    wide_x = padded.shape[2]
    depth_x = wide_x - 4
    length_y = padded.shape[3]
    y_source = jnp.arange(length_y, dtype=jnp.int32)[:, None]
    y_target = jnp.arange(length_y, dtype=jnp.int32)[None, :]
    shift_y = jnp.stack(
        [(y_source == y_target + step).astype(jnp.float32) for step in range(-2, 3)], 0
    )
    x_source = jnp.arange(wide_x, dtype=jnp.int32)[:, None]
    x_target = jnp.arange(depth_x, dtype=jnp.int32)[None, :]
    shift_x = jnp.stack(
        [(x_source == x_target + 2 + step).astype(jnp.float32) for step in range(-2, 3)], 0
    )
    shifted = jnp.einsum("gvy,bzxv->gbzxy", shift_y, padded, precision=lax.Precision.HIGHEST)
    extended = jnp.concatenate(
        [m2l_kernels, jnp.zeros((1, rank_count, rank_count), jnp.float32)], axis=0
    )
    stencil = extended[jnp.asarray(shell_table())]
    summed = jnp.zeros((rank_count, depth_z, depth_x, length_y), jnp.float32)
    for plane in range(5):
        slab = shifted[:, :, plane : plane + depth_z]
        partial_value = jnp.einsum(
            "fgab,gbzpy->afzpy", stencil[plane], slab, precision=lax.Precision.HIGHEST
        )
        summed = summed + jnp.einsum(
            "afzpy,fpq->azqy", partial_value, shift_x, precision=lax.Precision.HIGHEST
        )
    return summed


def shards(
    desc,
    positions,
    species,
    w_in,
    w_mid,
    w_head,
    species_charge,
    m2l_kernels,
    expand_u,
    compress_v,
    send_list,
    slot_box,
):
    atom_count = desc.shape[0]
    total_atoms = atom_count * lax.axis_size(GRP) * lax.axis_size(DEV)
    grad_scale = 1.0 / math.sqrt(total_atoms)
    pre_one = jnp.dot(desc, w_in, preferred_element_type=jnp.float32)
    hidden_one = jax.nn.silu(pre_one).astype(jnp.bfloat16)
    pre_two = jnp.dot(hidden_one, w_mid, preferred_element_type=jnp.float32)
    hidden_two = jax.nn.silu(pre_two)
    species_hot = (
        species[None, :] == jnp.arange(species_charge.shape[0], dtype=jnp.int32)[:, None]
    ).astype(jnp.float32)
    charge = jnp.sum(hidden_two * w_head[None, :], axis=1) + jnp.dot(
        species_charge, species_hot, precision=lax.Precision.HIGHEST
    )
    is_used = send_list >= 0
    side = int(round(math.sqrt(atom_count)))
    atom_high = jnp.where(is_used, send_list // side, -1).reshape(1, -1)
    atom_low = (send_list % side).reshape(1, -1)
    packed = jnp.concatenate([charge[None, :], positions], axis=0)
    picked = atoms_to_slots(packed, atom_high, atom_low).reshape(4, *send_list.shape)
    outgoing = jnp.concatenate([picked, slot_box[None].astype(jnp.float32)], axis=0)
    arrived = lax.all_to_all(outgoing, DEV, split_axis=1, concat_axis=1, tiled=True)
    arrived = arrived.reshape(arrived.shape[0], -1)
    moments = box_sum(arrived, BOXES)
    node_grid = moments.reshape(NODES, BZ, BX, BY)
    reduced = jnp.einsum("nr,nzxy->rzxy", compress_v, node_grid, precision=lax.Precision.HIGHEST)
    padded = extended_2(reduced, ((GRP, 1), (DEV, 2)), 2)
    local_terms = translate(padded, m2l_kernels)
    expansion = jnp.dot(expand_u, local_terms.reshape(RANK, BOXES), precision=lax.Precision.HIGHEST)
    slot_potential = box_pick(expansion, arrived).reshape(send_list.shape)
    returned = lax.all_to_all(slot_potential, DEV, split_axis=0, concat_axis=0, tiled=True)
    potential = slots_to_atoms(returned.reshape(-1), atom_high, atom_low, atom_count)
    head_part = jnp.sum(potential[:, None] * hidden_two, axis=0) * grad_scale
    species_part = jnp.dot(species_hot, potential, precision=lax.Precision.HIGHEST) * grad_scale
    delta_two = (potential[:, None] * w_head[None, :] * silu_slope(pre_two)).astype(jnp.bfloat16)
    mid_part = (
        lax.dot_general(
            hidden_one, delta_two, (((0,), (0,)), ((), ())), preferred_element_type=jnp.float32
        )
        * grad_scale
    )
    back_one = lax.dot_general(
        delta_two, w_mid, (((1,), (1,)), ((), ())), preferred_element_type=jnp.float32
    )
    delta_one = (back_one * silu_slope(pre_one)).astype(jnp.bfloat16)
    in_part = (
        lax.dot_general(
            desc, delta_one, (((0,), (0,)), ((), ())), preferred_element_type=jnp.float32
        )
        * grad_scale
    )
    grad_in, grad_mid, grad_head, grad_species = summed_everywhere(
        (in_part, mid_part, head_part, species_part)
    )
    return (potential, grad_in, grad_mid, grad_head, grad_species)


def solution(mesh):
    torus = Mesh(mesh.devices.reshape(8, 2, 8, 4), ("grp_0", "grp_1", "dev_0", "dev_1"))
    placed = (
        P(GRP_DEV, None),
        P(None, GRP_DEV),
        P(GRP_DEV),
        P(),
        P(),
        P(),
        P(),
        P(),
        P(),
        P(),
        P(GRP_DEV, None),
        P(GRP_DEV, None),
    )
    return jax.shard_map(
        shards,
        mesh=torus,
        in_specs=placed,
        out_specs=(P(GRP_DEV), P(), P(), P(), P()),
        check_vma=False,
    )
```

```python
import math

import jax
import jax.numpy as jnp
import numpy as np
from jax import lax
from jax.experimental import pallas as pl
from jax.sharding import Mesh
from jax.sharding import PartitionSpec as P

NODES = 64
RANK = 16
BZ = 4
BX = 4
BY = 64
BOXES = 1024
GRP = ("grp_0", "grp_1")
DEV = ("dev_0", "dev_1")
GRP_DEV = ("grp_0", "grp_1", "dev_0", "dev_1")


NODE_POINTS = [math.cos((2 * node_number + 1) * math.pi / 8) for node_number in range(4)]


def extended_2(cells, sides, width):
    for axis, dim in sides:
        count = lax.axis_size(axis)
        ends = count - 1
        head = lax.slice_in_dim(cells, 0, width, axis=dim)
        tail = lax.slice_in_dim(cells, cells.shape[dim] - width, cells.shape[dim], axis=dim)
        cells = jnp.concatenate(
            [
                lax.ppermute(tail, axis, [(i, (i + 1) % count) for i in range(ends)]),
                cells,
                lax.ppermute(head, axis, [((i + 1) % count, i) for i in range(ends)]),
            ],
            axis=dim,
        )
    return cells


def in_blocks(x, dim, peers):
    before, after = (x.shape[:dim], x.shape[dim + 1 :])
    return jnp.moveaxis(x.reshape(*before, peers, -1, *after), dim, 0)


def sent_and_summed(x, axis, dim):
    blocks = in_blocks(x, dim, lax.axis_size(axis))
    arrived = lax.all_to_all(blocks, axis, split_axis=0, concat_axis=0, tiled=True)
    return arrived.sum(axis=0)


def sum_in_two_steps(x, axes, dim):
    far, near = axes
    blocks = in_blocks(x, dim, lax.axis_size(far))
    nearer = sent_and_summed(blocks, near, dim + 1)
    arrived = lax.all_to_all(nearer, far, split_axis=0, concat_axis=0, tiled=True)
    return arrived.sum(axis=0)


def padded_to(lines, peers):
    spare = -lines.shape[0] % peers
    if not spare:
        return lines
    return jnp.concatenate([lines, jnp.zeros((spare, *lines.shape[1:]), lines.dtype)])


def sent_to_all(x, axis):
    copies = jnp.broadcast_to(x, (lax.axis_size(axis), *x.shape))
    return lax.all_to_all(copies, axis, split_axis=0, concat_axis=0, tiled=True)


def laid_out(blocks, dim):
    dims = list(blocks.shape[1:])
    dims[dim] *= blocks.shape[0]
    return jnp.moveaxis(blocks, 0, dim).reshape(dims)


def whole_of(x, axes, dim):
    far, near = axes
    blocks = sent_to_all(sent_to_all(x, far), near)
    return laid_out(blocks.swapaxes(0, 1).reshape(-1, *x.shape), dim)


def nested_sum(x, axes):
    own = sum_in_two_steps(padded_to(x, lax.axis_size(axes[0]) * lax.axis_size(axes[1])), axes, 0)
    whole = whole_of(own, axes, 0)
    return whole[: len(x)].reshape(x.shape)


def together(arrays, axis):
    ends = [0]
    for a in arrays:
        ends.append(ends[-1] + a.size)
    total = nested_sum(jnp.concatenate([a.ravel() for a in arrays]), axis)
    return tuple((total[b:e].reshape(a.shape) for a, b, e in zip(arrays, ends, ends[1:])))


def swapped(x, axis, step):
    count = lax.axis_size(axis)
    return lax.ppermute(x, axis, [(i, i ^ step) for i in range(count)])


def butterfly_sum(x, axis):
    step = 1
    while step < lax.axis_size(axis):
        x = x + swapped(x, axis, step)
        step *= 2
    return x


def hybrid_sum(x, pair, plane, stack):
    length = x.shape[0]
    x = butterfly_sum(x, pair)
    peers = lax.axis_size(plane)
    lines = padded_to(x, peers).reshape(peers, -1)
    own = lax.all_to_all(lines, plane, 0, 0, tiled=True).reshape(peers, -1).sum(axis=0)
    own = butterfly_sum(own, stack)
    copies = jnp.broadcast_to(own, (peers, *own.shape))
    return lax.all_to_all(copies, plane, 0, 0, tiled=True).reshape(-1)[:length]


def summed_everywhere(arrays):
    ends = [0]
    for a in arrays:
        ends.append(ends[-1] + a.size)
    flat = jnp.concatenate([a.ravel() for a in arrays])
    total = hybrid_sum(flat, "grp_1", DEV, "grp_0")
    return tuple((total[b:e].reshape(a.shape) for a, b, e in zip(arrays, ends, ends[1:])))


def split_three(x):
    high = lax.reduce_precision(x, exponent_bits=8, mantissa_bits=7)
    rest = x - high
    middle = lax.reduce_precision(rest, exponent_bits=8, mantissa_bits=7)
    return high, middle, rest - middle


def pieces_bf16(x, axis):
    return jnp.concatenate([p.astype(jnp.bfloat16) for p in split_three(x)], axis=axis)


def atoms_to_slots_kernel(table_ref, high_ref, low_ref, box_ref, out_ref):
    rows, tile = out_ref.shape
    rows -= 1
    out_ref[rows : rows + 1, :] = box_ref[...].astype(jnp.float32)
    side = table_ref.shape[1]
    lines = lax.broadcasted_iota(jnp.int32, (side, tile), 0)
    low = (lines == low_ref[...]).astype(jnp.bfloat16)
    parts = jnp.dot(table_ref[...], low, preferred_element_type=jnp.float32)
    block = rows * side
    whole = parts[:block] + parts[block : 2 * block] + parts[2 * block :]
    high = (lines == high_ref[...]).astype(jnp.float32)
    for row in range(rows):
        out_ref[row : row + 1, :] = jnp.sum(
            whole[row * side : (row + 1) * side] * high, axis=0, keepdims=True
        )


def atoms_to_slots(values, high, low, box, tile=1024):
    rows, count = values.shape
    side = int(round(math.sqrt(count)))
    table = pieces_bf16(values.reshape(rows * side, side), 0)
    slots = high.shape[1]
    return pl.pallas_call(
        atoms_to_slots_kernel,
        grid=(slots // tile,),
        in_specs=[
            pl.BlockSpec(table.shape, lambda i: (0, 0)),
            pl.BlockSpec((1, tile), lambda i: (0, i)),
            pl.BlockSpec((1, tile), lambda i: (0, i)),
            pl.BlockSpec((1, tile), lambda i: (0, i)),
        ],
        out_specs=pl.BlockSpec((rows + 1, tile), lambda i: (0, i)),
        out_shape=jax.ShapeDtypeStruct((rows + 1, slots), jnp.float32),
    )(table, high, low, box)


def slots_to_atoms_kernel(value_ref, high_ref, low_ref, out_ref):
    @pl.when(pl.program_id(0) == 0)
    def _():
        out_ref[...] = jnp.zeros_like(out_ref)

    side = out_ref.shape[1]
    tile = high_ref.shape[1]
    lines = lax.broadcasted_iota(jnp.int32, (side, tile), 0)
    hit = lines == high_ref[...]
    low = (lines == low_ref[...]).astype(jnp.bfloat16)
    value = value_ref[...]
    high_part = value.astype(jnp.bfloat16).astype(jnp.float32)
    rest = value - high_part
    middle_part = rest.astype(jnp.bfloat16).astype(jnp.float32)
    low_part = rest - middle_part
    stacked = jnp.concatenate(
        [jnp.where(hit, p, 0.0).astype(jnp.bfloat16) for p in (high_part, middle_part, low_part)],
        axis=0,
    )
    out_ref[...] += lax.dot_general(
        stacked, low, (((1,), (1,)), ((), ())), preferred_element_type=jnp.float32
    )


def slots_to_atoms(values, high, low, count, tile=1024):
    side = int(round(math.sqrt(count)))
    pieces = values.reshape(1, -1)
    slots = values.shape[0]
    parts = pl.pallas_call(
        slots_to_atoms_kernel,
        grid=(slots // tile,),
        in_specs=[
            pl.BlockSpec((1, tile), lambda i: (0, i)),
            pl.BlockSpec((1, tile), lambda i: (0, i)),
            pl.BlockSpec((1, tile), lambda i: (0, i)),
        ],
        out_specs=pl.BlockSpec((3 * side, side), lambda i: (0, 0)),
        out_shape=jax.ShapeDtypeStruct((3 * side, side), jnp.float32),
    )(pieces, high, low)
    return (parts[:side] + parts[side : 2 * side] + parts[2 * side :]).reshape(count)


def node_rows(data_ref, tile):
    nodes = lax.broadcasted_iota(jnp.int32, (NODES, tile), 0)
    spread = []
    for axis, shift in ((0, 4), (1, 2), (2, 0)):
        u = data_ref[1 + axis : 2 + axis, :]
        order_two = 2.0 * u * u - 1.0
        order_three = 4.0 * u * u * u - 3.0 * u
        rows = []
        for node_point in NODE_POINTS:
            cheb_two = 2.0 * node_point * node_point - 1.0
            cheb_three = 4.0 * node_point * node_point * node_point - 3.0 * node_point
            rows.append(0.25 + 0.5 * (node_point * u + cheb_two * order_two + cheb_three * order_three))
        pick = jnp.bitwise_and(jnp.right_shift(nodes, shift), 3)
        full = jnp.broadcast_to(rows[3], (NODES, tile))
        for p in range(3):
            full = jnp.where(pick == p, rows[p], full)
        spread.append(full)
    return spread[0] * spread[1] * spread[2]


def bf16_pieces_in_kernel(x):
    high = x.astype(jnp.bfloat16)
    rest = x - high.astype(jnp.float32)
    middle = rest.astype(jnp.bfloat16)
    low = (rest - middle.astype(jnp.float32)).astype(jnp.bfloat16)
    return jnp.concatenate([high, middle, low], axis=0)


def box_sum_kernel(data_ref, out_ref):
    @pl.when(pl.program_id(0) == 0)
    def _():
        out_ref[...] = jnp.zeros_like(out_ref)

    boxes = out_ref.shape[1]
    tile = data_ref.shape[1]
    box = data_ref[4:5, :].astype(jnp.int32)
    weighted = node_rows(data_ref, tile) * data_ref[0:1, :]
    hot = (lax.broadcasted_iota(jnp.int32, (boxes, tile), 0) == box).astype(jnp.bfloat16)
    out_ref[...] += lax.dot_general(
        bf16_pieces_in_kernel(weighted), hot, (((1,), (1,)), ((), ())),
        preferred_element_type=jnp.float32,
    )


def box_sum(data, boxes, tile=1024):
    rows, slots = data.shape
    parts = pl.pallas_call(
        box_sum_kernel,
        grid=(slots // tile,),
        in_specs=[pl.BlockSpec((rows, tile), lambda i: (0, i))],
        out_specs=pl.BlockSpec((3 * NODES, boxes), lambda i: (0, 0)),
        out_shape=jax.ShapeDtypeStruct((3 * NODES, boxes), jnp.float32),
    )(data)
    return parts[:NODES] + parts[NODES : 2 * NODES] + parts[2 * NODES :]


def box_pick_kernel(table_ref, data_ref, out_ref):
    boxes = table_ref.shape[1]
    tile = data_ref.shape[1]
    box = data_ref[4:5, :].astype(jnp.int32)
    hot = (lax.broadcasted_iota(jnp.int32, (boxes, tile), 0) == box).astype(jnp.bfloat16)
    parts = jnp.dot(table_ref[...], hot, preferred_element_type=jnp.float32)
    picked = parts[:NODES] + parts[NODES : 2 * NODES] + parts[2 * NODES :]
    out_ref[...] = jnp.sum(node_rows(data_ref, tile) * picked, axis=0, keepdims=True)


def box_pick(table, data, tile=1024):
    rows, slots = data.shape
    stacked = pieces_bf16(table, 0)
    return pl.pallas_call(
        box_pick_kernel,
        grid=(slots // tile,),
        in_specs=[
            pl.BlockSpec(stacked.shape, lambda i: (0, 0)),
            pl.BlockSpec((rows, tile), lambda i: (0, i)),
        ],
        out_specs=pl.BlockSpec((1, tile), lambda i: (0, i)),
        out_shape=jax.ShapeDtypeStruct((1, slots), jnp.float32),
    )(stacked, data)[0]


def shell_table():
    table = np.full((5, 5, 5), 98, dtype=np.int32)
    counter = 0
    for shift_z in range(-2, 3):
        for shift_x in range(-2, 3):
            for shift_y in range(-2, 3):
                if max(abs(shift_z), abs(shift_x), abs(shift_y)) == 2:
                    table[shift_z + 2, shift_x + 2, shift_y + 2] = counter
                    counter += 1
    return table


def chebyshev_rows(coordinate):
    order_two = 2.0 * coordinate * coordinate - 1.0
    order_three = 4.0 * coordinate * coordinate * coordinate - 3.0 * coordinate
    stacked = []
    for node_point in NODE_POINTS:
        cheb_two = 2.0 * node_point * node_point - 1.0
        cheb_three = 4.0 * node_point * node_point * node_point - 3.0 * node_point
        stacked.append(
            0.25 + 0.5 * (node_point * coordinate + cheb_two * order_two + cheb_three * order_three)
        )
    return jnp.stack(stacked, 0)


def node_weights(coords):
    along_z = chebyshev_rows(coords[0])
    along_x = chebyshev_rows(coords[1])
    along_y = chebyshev_rows(coords[2])
    product = along_z[:, None, None, :] * along_x[None, :, None, :] * along_y[None, None, :, :]
    return product.reshape(64, coords.shape[1])


def silu_slope(value):
    sigma = jax.nn.sigmoid(value)
    return sigma * (1.0 + value * (1.0 - sigma))


def translate(padded, m2l_kernels):
    rank_count = padded.shape[0]
    depth_z = padded.shape[1] - 4
    wide_x = padded.shape[2]
    depth_x = wide_x - 4
    length_y = padded.shape[3]
    y_source = jnp.arange(length_y, dtype=jnp.int32)[:, None]
    y_target = jnp.arange(length_y, dtype=jnp.int32)[None, :]
    shift_y = jnp.stack(
        [(y_source == y_target + step).astype(jnp.float32) for step in range(-2, 3)], 0
    )
    x_source = jnp.arange(wide_x, dtype=jnp.int32)[:, None]
    x_target = jnp.arange(depth_x, dtype=jnp.int32)[None, :]
    shift_x = jnp.stack(
        [(x_source == x_target + 2 + step).astype(jnp.float32) for step in range(-2, 3)], 0
    )
    shifted = jnp.einsum("gvy,bzxv->gbzxy", shift_y, padded, precision=lax.Precision.HIGHEST)
    extended = jnp.concatenate(
        [m2l_kernels, jnp.zeros((1, rank_count, rank_count), jnp.float32)], axis=0
    )
    stencil = extended[jnp.asarray(shell_table())]
    summed = jnp.zeros((rank_count, depth_z, depth_x, length_y), jnp.float32)
    for plane in range(5):
        slab = shifted[:, :, plane : plane + depth_z]
        partial_value = jnp.einsum(
            "fgab,gbzpy->afzpy", stencil[plane], slab, precision=lax.Precision.HIGHEST
        )
        summed = summed + jnp.einsum(
            "afzpy,fpq->azqy", partial_value, shift_x, precision=lax.Precision.HIGHEST
        )
    return summed


def shards(
    desc,
    positions,
    species,
    w_in,
    w_mid,
    w_head,
    species_charge,
    m2l_kernels,
    expand_u,
    compress_v,
    send_list,
    slot_box,
):
    atom_count = desc.shape[0]
    total_atoms = atom_count * lax.axis_size(GRP) * lax.axis_size(DEV)
    grad_scale = 1.0 / math.sqrt(total_atoms)
    pre_one = jnp.dot(desc, w_in, preferred_element_type=jnp.float32)
    hidden_one = jax.nn.silu(pre_one).astype(jnp.bfloat16)
    pre_two = jnp.dot(hidden_one, w_mid, preferred_element_type=jnp.float32)
    hidden_two = jax.nn.silu(pre_two)
    species_hot = (
        species[None, :] == jnp.arange(species_charge.shape[0], dtype=jnp.int32)[:, None]
    ).astype(jnp.float32)
    charge = jnp.sum(hidden_two * w_head[None, :], axis=1) + jnp.dot(
        species_charge, species_hot, precision=lax.Precision.HIGHEST
    )
    is_used = send_list >= 0
    side = int(round(math.sqrt(atom_count)))
    atom_high = jnp.where(is_used, send_list // side, -1).reshape(1, -1)
    atom_low = (send_list % side).reshape(1, -1)
    packed = jnp.concatenate([charge[None, :], positions], axis=0)
    outgoing = atoms_to_slots(packed, atom_high, atom_low, slot_box.reshape(1, -1))
    outgoing = outgoing.reshape(outgoing.shape[0], *send_list.shape)
    arrived = lax.all_to_all(outgoing, DEV, split_axis=1, concat_axis=1, tiled=True)
    arrived = arrived.reshape(arrived.shape[0], -1)
    moments = box_sum(arrived, BOXES)
    node_grid = moments.reshape(NODES, BZ, BX, BY)
    reduced = jnp.einsum("nr,nzxy->rzxy", compress_v, node_grid, precision=lax.Precision.HIGHEST)
    padded = extended_2(reduced, ((GRP, 1), (DEV, 2)), 2)
    local_terms = translate(padded, m2l_kernels)
    expansion = jnp.dot(expand_u, local_terms.reshape(RANK, BOXES), precision=lax.Precision.HIGHEST)
    slot_potential = box_pick(expansion, arrived).reshape(send_list.shape)
    returned = lax.all_to_all(slot_potential, DEV, split_axis=0, concat_axis=0, tiled=True)
    potential = slots_to_atoms(returned.reshape(-1), atom_high, atom_low, atom_count)
    head_part = jnp.sum(potential[:, None] * hidden_two, axis=0) * grad_scale
    species_part = jnp.dot(species_hot, potential, precision=lax.Precision.HIGHEST) * grad_scale
    delta_two = (potential[:, None] * w_head[None, :] * silu_slope(pre_two)).astype(jnp.bfloat16)
    mid_part = (
        lax.dot_general(
            hidden_one, delta_two, (((0,), (0,)), ((), ())), preferred_element_type=jnp.float32
        )
        * grad_scale
    )
    back_one = lax.dot_general(
        delta_two, w_mid, (((1,), (1,)), ((), ())), preferred_element_type=jnp.float32
    )
    delta_one = (back_one * silu_slope(pre_one)).astype(jnp.bfloat16)
    in_part = (
        lax.dot_general(
            desc, delta_one, (((0,), (0,)), ((), ())), preferred_element_type=jnp.float32
        )
        * grad_scale
    )
    grad_in, grad_mid, grad_head, grad_species = summed_everywhere(
        (in_part, mid_part, head_part, species_part)
    )
    return (potential, grad_in, grad_mid, grad_head, grad_species)


def solution(mesh):
    torus = Mesh(mesh.devices.reshape(8, 2, 8, 4), ("grp_0", "grp_1", "dev_0", "dev_1"))
    placed = (
        P(GRP_DEV, None),
        P(None, GRP_DEV),
        P(GRP_DEV),
        P(),
        P(),
        P(),
        P(),
        P(),
        P(),
        P(),
        P(GRP_DEV, None),
        P(GRP_DEV, None),
    )
    return jax.shard_map(
        shards,
        mesh=torus,
        in_specs=placed,
        out_specs=(P(GRP_DEV), P(), P(), P(), P()),
        check_vma=False,
    )
```

```python
import math

import jax
import jax.numpy as jnp
import numpy as np
from jax import lax
from jax.experimental import pallas as pl
from jax.sharding import Mesh
from jax.sharding import PartitionSpec as P

NODES = 64
RANK = 16
BZ = 4
BX = 4
BY = 64
BOXES = 1024
GRP = ("grp_0", "grp_1")
DEV = ("dev_0", "dev_1")
GRP_DEV = ("grp_0", "grp_1", "dev_0", "dev_1")


NODE_POINTS = [math.cos((2 * node_number + 1) * math.pi / 8) for node_number in range(4)]


def extended_2(cells, sides, width):
    for axis, dim in sides:
        count = lax.axis_size(axis)
        ends = count - 1
        head = lax.slice_in_dim(cells, 0, width, axis=dim)
        tail = lax.slice_in_dim(cells, cells.shape[dim] - width, cells.shape[dim], axis=dim)
        cells = jnp.concatenate(
            [
                lax.ppermute(tail, axis, [(i, (i + 1) % count) for i in range(ends)]),
                cells,
                lax.ppermute(head, axis, [((i + 1) % count, i) for i in range(ends)]),
            ],
            axis=dim,
        )
    return cells


def in_blocks(x, dim, peers):
    before, after = (x.shape[:dim], x.shape[dim + 1 :])
    return jnp.moveaxis(x.reshape(*before, peers, -1, *after), dim, 0)


def sent_and_summed(x, axis, dim):
    blocks = in_blocks(x, dim, lax.axis_size(axis))
    arrived = lax.all_to_all(blocks, axis, split_axis=0, concat_axis=0, tiled=True)
    return arrived.sum(axis=0)


def sum_in_two_steps(x, axes, dim):
    far, near = axes
    blocks = in_blocks(x, dim, lax.axis_size(far))
    nearer = sent_and_summed(blocks, near, dim + 1)
    arrived = lax.all_to_all(nearer, far, split_axis=0, concat_axis=0, tiled=True)
    return arrived.sum(axis=0)


def padded_to(lines, peers):
    spare = -lines.shape[0] % peers
    if not spare:
        return lines
    return jnp.concatenate([lines, jnp.zeros((spare, *lines.shape[1:]), lines.dtype)])


def sent_to_all(x, axis):
    copies = jnp.broadcast_to(x, (lax.axis_size(axis), *x.shape))
    return lax.all_to_all(copies, axis, split_axis=0, concat_axis=0, tiled=True)


def laid_out(blocks, dim):
    dims = list(blocks.shape[1:])
    dims[dim] *= blocks.shape[0]
    return jnp.moveaxis(blocks, 0, dim).reshape(dims)


def whole_of(x, axes, dim):
    far, near = axes
    blocks = sent_to_all(sent_to_all(x, far), near)
    return laid_out(blocks.swapaxes(0, 1).reshape(-1, *x.shape), dim)


def nested_sum(x, axes):
    own = sum_in_two_steps(padded_to(x, lax.axis_size(axes[0]) * lax.axis_size(axes[1])), axes, 0)
    whole = whole_of(own, axes, 0)
    return whole[: len(x)].reshape(x.shape)


def together(arrays, axis):
    ends = [0]
    for a in arrays:
        ends.append(ends[-1] + a.size)
    total = nested_sum(jnp.concatenate([a.ravel() for a in arrays]), axis)
    return tuple((total[b:e].reshape(a.shape) for a, b, e in zip(arrays, ends, ends[1:])))


def swapped(x, axis, step):
    count = lax.axis_size(axis)
    return lax.ppermute(x, axis, [(i, i ^ step) for i in range(count)])


def butterfly_sum(x, axis):
    step = 1
    while step < lax.axis_size(axis):
        x = x + swapped(x, axis, step)
        step *= 2
    return x


def hybrid_sum(x, pair, plane, stack):
    length = x.shape[0]
    x = butterfly_sum(x, pair)
    peers = lax.axis_size(plane)
    lines = padded_to(x, peers).reshape(peers, -1)
    own = lax.all_to_all(lines, plane, 0, 0, tiled=True).reshape(peers, -1).sum(axis=0)
    own = butterfly_sum(own, stack)
    copies = jnp.broadcast_to(own, (peers, *own.shape))
    return lax.all_to_all(copies, plane, 0, 0, tiled=True).reshape(-1)[:length]


def summed_everywhere(arrays):
    ends = [0]
    for a in arrays:
        ends.append(ends[-1] + a.size)
    flat = jnp.concatenate([a.ravel() for a in arrays])
    total = hybrid_sum(flat, "grp_1", DEV, "grp_0")
    return tuple((total[b:e].reshape(a.shape) for a, b, e in zip(arrays, ends, ends[1:])))


def split_three(x):
    high = lax.reduce_precision(x, exponent_bits=8, mantissa_bits=7)
    rest = x - high
    middle = lax.reduce_precision(rest, exponent_bits=8, mantissa_bits=7)
    return high, middle, rest - middle


def pieces_bf16(x, axis):
    return jnp.concatenate([p.astype(jnp.bfloat16) for p in split_three(x)], axis=axis)


def atoms_to_slots_kernel(table_ref, high_ref, low_ref, box_ref, out_ref):
    rows, tile = out_ref.shape
    rows -= 1
    out_ref[rows : rows + 1, :] = box_ref[...].astype(jnp.float32)
    side = table_ref.shape[1]
    lines = lax.broadcasted_iota(jnp.int32, (side, tile), 0)
    low = (lines == low_ref[...]).astype(jnp.bfloat16)
    parts = jnp.dot(table_ref[...], low, preferred_element_type=jnp.float32)
    block = rows * side
    whole = parts[:block] + parts[block : 2 * block] + parts[2 * block :]
    high = (lines == high_ref[...]).astype(jnp.float32)
    for row in range(rows):
        out_ref[row : row + 1, :] = jnp.sum(
            whole[row * side : (row + 1) * side] * high, axis=0, keepdims=True
        )


def atoms_to_slots(values, high, low, box, tile=2048):
    rows, count = values.shape
    side = int(round(math.sqrt(count)))
    table = pieces_bf16(values.reshape(rows * side, side), 0)
    slots = high.shape[1]
    return pl.pallas_call(
        atoms_to_slots_kernel,
        grid=(slots // tile,),
        in_specs=[
            pl.BlockSpec(table.shape, lambda i: (0, 0)),
            pl.BlockSpec((1, tile), lambda i: (0, i)),
            pl.BlockSpec((1, tile), lambda i: (0, i)),
            pl.BlockSpec((1, tile), lambda i: (0, i)),
        ],
        out_specs=pl.BlockSpec((rows + 1, tile), lambda i: (0, i)),
        out_shape=jax.ShapeDtypeStruct((rows + 1, slots), jnp.float32),
    )(table, high, low, box)


def slots_to_atoms_kernel(value_ref, high_ref, low_ref, out_ref):
    @pl.when(pl.program_id(0) == 0)
    def _():
        out_ref[...] = jnp.zeros_like(out_ref)

    side = out_ref.shape[1]
    tile = high_ref.shape[1]
    lines = lax.broadcasted_iota(jnp.int32, (side, tile), 0)
    hit = lines == high_ref[...]
    low = (lines == low_ref[...]).astype(jnp.bfloat16)
    value = value_ref[...]
    high_part = value.astype(jnp.bfloat16).astype(jnp.float32)
    rest = value - high_part
    middle_part = rest.astype(jnp.bfloat16).astype(jnp.float32)
    low_part = rest - middle_part
    stacked = jnp.concatenate(
        [jnp.where(hit, p, 0.0).astype(jnp.bfloat16) for p in (high_part, middle_part, low_part)],
        axis=0,
    )
    out_ref[...] += lax.dot_general(
        stacked, low, (((1,), (1,)), ((), ())), preferred_element_type=jnp.float32
    )


def slots_to_atoms(values, high, low, count, tile=2048):
    side = int(round(math.sqrt(count)))
    pieces = values.reshape(1, -1)
    slots = values.shape[0]
    parts = pl.pallas_call(
        slots_to_atoms_kernel,
        grid=(slots // tile,),
        in_specs=[
            pl.BlockSpec((1, tile), lambda i: (0, i)),
            pl.BlockSpec((1, tile), lambda i: (0, i)),
            pl.BlockSpec((1, tile), lambda i: (0, i)),
        ],
        out_specs=pl.BlockSpec((3 * side, side), lambda i: (0, 0)),
        out_shape=jax.ShapeDtypeStruct((3 * side, side), jnp.float32),
    )(pieces, high, low)
    return (parts[:side] + parts[side : 2 * side] + parts[2 * side :]).reshape(count)


def node_rows(data_ref, tile):
    nodes = lax.broadcasted_iota(jnp.int32, (NODES, tile), 0)
    spread = []
    for axis, shift in ((0, 4), (1, 2), (2, 0)):
        u = data_ref[1 + axis : 2 + axis, :]
        order_two = 2.0 * u * u - 1.0
        order_three = 4.0 * u * u * u - 3.0 * u
        rows = []
        for node_point in NODE_POINTS:
            cheb_two = 2.0 * node_point * node_point - 1.0
            cheb_three = 4.0 * node_point * node_point * node_point - 3.0 * node_point
            rows.append(0.25 + 0.5 * (node_point * u + cheb_two * order_two + cheb_three * order_three))
        pick = jnp.bitwise_and(jnp.right_shift(nodes, shift), 3)
        full = jnp.broadcast_to(rows[3], (NODES, tile))
        for p in range(3):
            full = jnp.where(pick == p, rows[p], full)
        spread.append(full)
    return spread[0] * spread[1] * spread[2]


def bf16_pieces_in_kernel(x):
    high = x.astype(jnp.bfloat16)
    low = (x - high.astype(jnp.float32)).astype(jnp.bfloat16)
    return jnp.concatenate([high, low], axis=0)


def split_two(x):
    high = lax.reduce_precision(x, exponent_bits=8, mantissa_bits=7)
    return jnp.concatenate(
        [high.astype(jnp.bfloat16), (x - high).astype(jnp.bfloat16)], axis=0
    )


def box_sum_kernel(data_ref, out_ref):
    @pl.when(pl.program_id(0) == 0)
    def _():
        out_ref[...] = jnp.zeros_like(out_ref)

    boxes = out_ref.shape[1]
    tile = data_ref.shape[1]
    box = data_ref[4:5, :].astype(jnp.int32)
    weighted = node_rows(data_ref, tile) * data_ref[0:1, :]
    hot = (lax.broadcasted_iota(jnp.int32, (boxes, tile), 0) == box).astype(jnp.bfloat16)
    out_ref[...] += lax.dot_general(
        bf16_pieces_in_kernel(weighted), hot, (((1,), (1,)), ((), ())),
        preferred_element_type=jnp.float32,
    )


def box_sum(data, boxes, tile=2048):
    rows, slots = data.shape
    parts = pl.pallas_call(
        box_sum_kernel,
        grid=(slots // tile,),
        in_specs=[pl.BlockSpec((rows, tile), lambda i: (0, i))],
        out_specs=pl.BlockSpec((2 * NODES, boxes), lambda i: (0, 0)),
        out_shape=jax.ShapeDtypeStruct((2 * NODES, boxes), jnp.float32),
    )(data)
    return parts[:NODES] + parts[NODES:]


def box_pick_kernel(table_ref, data_ref, out_ref):
    boxes = table_ref.shape[1]
    tile = data_ref.shape[1]
    box = data_ref[4:5, :].astype(jnp.int32)
    hot = (lax.broadcasted_iota(jnp.int32, (boxes, tile), 0) == box).astype(jnp.bfloat16)
    parts = jnp.dot(table_ref[...], hot, preferred_element_type=jnp.float32)
    picked = parts[:NODES] + parts[NODES:]
    out_ref[...] = jnp.sum(node_rows(data_ref, tile) * picked, axis=0, keepdims=True)


def box_pick(table, data, tile=2048):
    rows, slots = data.shape
    stacked = split_two(table)
    return pl.pallas_call(
        box_pick_kernel,
        grid=(slots // tile,),
        in_specs=[
            pl.BlockSpec(stacked.shape, lambda i: (0, 0)),
            pl.BlockSpec((rows, tile), lambda i: (0, i)),
        ],
        out_specs=pl.BlockSpec((1, tile), lambda i: (0, i)),
        out_shape=jax.ShapeDtypeStruct((1, slots), jnp.float32),
    )(stacked, data)[0]


def shell_table():
    table = np.full((5, 5, 5), 98, dtype=np.int32)
    counter = 0
    for shift_z in range(-2, 3):
        for shift_x in range(-2, 3):
            for shift_y in range(-2, 3):
                if max(abs(shift_z), abs(shift_x), abs(shift_y)) == 2:
                    table[shift_z + 2, shift_x + 2, shift_y + 2] = counter
                    counter += 1
    return table


def chebyshev_rows(coordinate):
    order_two = 2.0 * coordinate * coordinate - 1.0
    order_three = 4.0 * coordinate * coordinate * coordinate - 3.0 * coordinate
    stacked = []
    for node_point in NODE_POINTS:
        cheb_two = 2.0 * node_point * node_point - 1.0
        cheb_three = 4.0 * node_point * node_point * node_point - 3.0 * node_point
        stacked.append(
            0.25 + 0.5 * (node_point * coordinate + cheb_two * order_two + cheb_three * order_three)
        )
    return jnp.stack(stacked, 0)


def node_weights(coords):
    along_z = chebyshev_rows(coords[0])
    along_x = chebyshev_rows(coords[1])
    along_y = chebyshev_rows(coords[2])
    product = along_z[:, None, None, :] * along_x[None, :, None, :] * along_y[None, None, :, :]
    return product.reshape(64, coords.shape[1])


def silu_slope(value):
    sigma = jax.nn.sigmoid(value)
    return sigma * (1.0 + value * (1.0 - sigma))


def translate(padded, m2l_kernels):
    rank_count = padded.shape[0]
    depth_z = padded.shape[1] - 4
    wide_x = padded.shape[2]
    depth_x = wide_x - 4
    length_y = padded.shape[3]
    y_source = jnp.arange(length_y, dtype=jnp.int32)[:, None]
    y_target = jnp.arange(length_y, dtype=jnp.int32)[None, :]
    shift_y = jnp.stack(
        [(y_source == y_target + step).astype(jnp.float32) for step in range(-2, 3)], 0
    )
    x_source = jnp.arange(wide_x, dtype=jnp.int32)[:, None]
    x_target = jnp.arange(depth_x, dtype=jnp.int32)[None, :]
    shift_x = jnp.stack(
        [(x_source == x_target + 2 + step).astype(jnp.float32) for step in range(-2, 3)], 0
    )
    shifted = jnp.einsum("gvy,bzxv->gbzxy", shift_y, padded, precision=lax.Precision.HIGHEST)
    extended = jnp.concatenate(
        [m2l_kernels, jnp.zeros((1, rank_count, rank_count), jnp.float32)], axis=0
    )
    stencil = extended[jnp.asarray(shell_table())]
    summed = jnp.zeros((rank_count, depth_z, depth_x, length_y), jnp.float32)
    for plane in range(5):
        slab = shifted[:, :, plane : plane + depth_z]
        partial_value = jnp.einsum(
            "fgab,gbzpy->afzpy", stencil[plane], slab, precision=lax.Precision.HIGHEST
        )
        summed = summed + jnp.einsum(
            "afzpy,fpq->azqy", partial_value, shift_x, precision=lax.Precision.HIGHEST
        )
    return summed


def shards(
    desc,
    positions,
    species,
    w_in,
    w_mid,
    w_head,
    species_charge,
    m2l_kernels,
    expand_u,
    compress_v,
    send_list,
    slot_box,
):
    atom_count = desc.shape[0]
    total_atoms = atom_count * lax.axis_size(GRP) * lax.axis_size(DEV)
    grad_scale = 1.0 / math.sqrt(total_atoms)
    pre_one = jnp.dot(desc, w_in, preferred_element_type=jnp.float32)
    hidden_one = jax.nn.silu(pre_one).astype(jnp.bfloat16)
    pre_two = jnp.dot(hidden_one, w_mid, preferred_element_type=jnp.float32)
    hidden_two = jax.nn.silu(pre_two)
    species_hot = (
        species[None, :] == jnp.arange(species_charge.shape[0], dtype=jnp.int32)[:, None]
    ).astype(jnp.float32)
    charge = jnp.sum(hidden_two * w_head[None, :], axis=1) + jnp.dot(
        species_charge, species_hot, precision=lax.Precision.HIGHEST
    )
    is_used = send_list >= 0
    side = int(round(math.sqrt(atom_count)))
    atom_high = jnp.where(is_used, send_list // side, -1).reshape(1, -1)
    atom_low = (send_list % side).reshape(1, -1)
    packed = jnp.concatenate([charge[None, :], positions], axis=0)
    outgoing = atoms_to_slots(packed, atom_high, atom_low, slot_box.reshape(1, -1))
    outgoing = outgoing.reshape(outgoing.shape[0], *send_list.shape)
    arrived = lax.all_to_all(outgoing, DEV, split_axis=1, concat_axis=1, tiled=True)
    arrived = arrived.reshape(arrived.shape[0], -1)
    moments = box_sum(arrived, BOXES)
    node_grid = moments.reshape(NODES, BZ, BX, BY)
    reduced = jnp.einsum("nr,nzxy->rzxy", compress_v, node_grid, precision=lax.Precision.HIGHEST)
    padded = extended_2(reduced, ((GRP, 1), (DEV, 2)), 2)
    local_terms = translate(padded, m2l_kernels)
    expansion = jnp.dot(expand_u, local_terms.reshape(RANK, BOXES), precision=lax.Precision.HIGHEST)
    slot_potential = box_pick(expansion, arrived).reshape(send_list.shape)
    returned = lax.all_to_all(slot_potential, DEV, split_axis=0, concat_axis=0, tiled=True)
    potential = slots_to_atoms(returned.reshape(-1), atom_high, atom_low, atom_count)
    head_part = jnp.sum(potential[:, None] * hidden_two, axis=0) * grad_scale
    species_part = jnp.dot(species_hot, potential, precision=lax.Precision.HIGHEST) * grad_scale
    delta_two = (potential[:, None] * w_head[None, :] * silu_slope(pre_two)).astype(jnp.bfloat16)
    mid_part = (
        lax.dot_general(
            hidden_one, delta_two, (((0,), (0,)), ((), ())), preferred_element_type=jnp.float32
        )
        * grad_scale
    )
    back_one = lax.dot_general(
        delta_two, w_mid, (((1,), (1,)), ((), ())), preferred_element_type=jnp.float32
    )
    delta_one = (back_one * silu_slope(pre_one)).astype(jnp.bfloat16)
    in_part = (
        lax.dot_general(
            desc, delta_one, (((0,), (0,)), ((), ())), preferred_element_type=jnp.float32
        )
        * grad_scale
    )
    grad_in, grad_mid, grad_head, grad_species = summed_everywhere(
        (in_part, mid_part, head_part, species_part)
    )
    return (potential, grad_in, grad_mid, grad_head, grad_species)


def solution(mesh):
    torus = Mesh(mesh.devices.reshape(8, 2, 8, 4), ("grp_0", "grp_1", "dev_0", "dev_1"))
    placed = (
        P(GRP_DEV, None),
        P(None, GRP_DEV),
        P(GRP_DEV),
        P(),
        P(),
        P(),
        P(),
        P(),
        P(),
        P(),
        P(GRP_DEV, None),
        P(GRP_DEV, None),
    )
    return jax.shard_map(
        shards,
        mesh=torus,
        in_specs=placed,
        out_specs=(P(GRP_DEV), P(), P(), P(), P()),
        check_vma=False,
    )
```

```python
import math

import jax
import jax.numpy as jnp
import numpy as np
from jax import lax
from jax.experimental import pallas as pl
from jax.sharding import Mesh
from jax.sharding import PartitionSpec as P

NODES = 64
RANK = 16
BZ = 4
BX = 4
BY = 64
BOXES = 1024
GRP = ("grp_0", "grp_1")
DEV = ("dev_0", "dev_1")
GRP_DEV = ("grp_0", "grp_1", "dev_0", "dev_1")


NODE_POINTS = [math.cos((2 * node_number + 1) * math.pi / 8) for node_number in range(4)]


def extended_2(cells, sides, width):
    for axis, dim in sides:
        count = lax.axis_size(axis)
        ends = count - 1
        head = lax.slice_in_dim(cells, 0, width, axis=dim)
        tail = lax.slice_in_dim(cells, cells.shape[dim] - width, cells.shape[dim], axis=dim)
        cells = jnp.concatenate(
            [
                lax.ppermute(tail, axis, [(i, (i + 1) % count) for i in range(ends)]),
                cells,
                lax.ppermute(head, axis, [((i + 1) % count, i) for i in range(ends)]),
            ],
            axis=dim,
        )
    return cells


def in_blocks(x, dim, peers):
    before, after = (x.shape[:dim], x.shape[dim + 1 :])
    return jnp.moveaxis(x.reshape(*before, peers, -1, *after), dim, 0)


def sent_and_summed(x, axis, dim):
    blocks = in_blocks(x, dim, lax.axis_size(axis))
    arrived = lax.all_to_all(blocks, axis, split_axis=0, concat_axis=0, tiled=True)
    return arrived.sum(axis=0)


def sum_in_two_steps(x, axes, dim):
    far, near = axes
    blocks = in_blocks(x, dim, lax.axis_size(far))
    nearer = sent_and_summed(blocks, near, dim + 1)
    arrived = lax.all_to_all(nearer, far, split_axis=0, concat_axis=0, tiled=True)
    return arrived.sum(axis=0)


def padded_to(lines, peers):
    spare = -lines.shape[0] % peers
    if not spare:
        return lines
    return jnp.concatenate([lines, jnp.zeros((spare, *lines.shape[1:]), lines.dtype)])


def sent_to_all(x, axis):
    copies = jnp.broadcast_to(x, (lax.axis_size(axis), *x.shape))
    return lax.all_to_all(copies, axis, split_axis=0, concat_axis=0, tiled=True)


def laid_out(blocks, dim):
    dims = list(blocks.shape[1:])
    dims[dim] *= blocks.shape[0]
    return jnp.moveaxis(blocks, 0, dim).reshape(dims)


def whole_of(x, axes, dim):
    far, near = axes
    blocks = sent_to_all(sent_to_all(x, far), near)
    return laid_out(blocks.swapaxes(0, 1).reshape(-1, *x.shape), dim)


def nested_sum(x, axes):
    own = sum_in_two_steps(padded_to(x, lax.axis_size(axes[0]) * lax.axis_size(axes[1])), axes, 0)
    whole = whole_of(own, axes, 0)
    return whole[: len(x)].reshape(x.shape)


def together(arrays, axis):
    ends = [0]
    for a in arrays:
        ends.append(ends[-1] + a.size)
    total = nested_sum(jnp.concatenate([a.ravel() for a in arrays]), axis)
    return tuple((total[b:e].reshape(a.shape) for a, b, e in zip(arrays, ends, ends[1:])))


def swapped(x, axis, step):
    count = lax.axis_size(axis)
    return lax.ppermute(x, axis, [(i, i ^ step) for i in range(count)])


def butterfly_sum(x, axis):
    step = 1
    while step < lax.axis_size(axis):
        x = x + swapped(x, axis, step)
        step *= 2
    return x


def hybrid_sum(x, pair, plane, stack):
    length = x.shape[0]
    x = butterfly_sum(x, pair)
    peers = lax.axis_size(plane)
    lines = padded_to(x, peers).reshape(peers, -1)
    own = lax.all_to_all(lines, plane, 0, 0, tiled=True).reshape(peers, -1).sum(axis=0)
    own = butterfly_sum(own, stack)
    copies = jnp.broadcast_to(own, (peers, *own.shape))
    return lax.all_to_all(copies, plane, 0, 0, tiled=True).reshape(-1)[:length]


def summed_everywhere(arrays):
    ends = [0]
    for a in arrays:
        ends.append(ends[-1] + a.size)
    flat = jnp.concatenate([a.ravel() for a in arrays])
    total = hybrid_sum(flat, "grp_1", DEV, "grp_0")
    return tuple((total[b:e].reshape(a.shape) for a, b, e in zip(arrays, ends, ends[1:])))


def split_three(x):
    high = lax.reduce_precision(x, exponent_bits=8, mantissa_bits=7)
    rest = x - high
    middle = lax.reduce_precision(rest, exponent_bits=8, mantissa_bits=7)
    return high, middle, rest - middle


def pieces_bf16(x, axis):
    return jnp.concatenate([p.astype(jnp.bfloat16) for p in split_three(x)], axis=axis)


def atoms_to_slots_kernel(table_ref, high_ref, low_ref, box_ref, out_ref):
    rows, tile = out_ref.shape
    rows -= 1
    out_ref[rows : rows + 1, :] = box_ref[...].astype(jnp.float32)
    side = table_ref.shape[1]
    lines = lax.broadcasted_iota(jnp.int32, (side, tile), 0)
    low = (lines == low_ref[...]).astype(jnp.bfloat16)
    parts = jnp.dot(table_ref[...], low, preferred_element_type=jnp.float32)
    block = rows * side
    whole = parts[:block] + parts[block : 2 * block] + parts[2 * block :]
    high = (lines == high_ref[...]).astype(jnp.float32)
    for row in range(rows):
        out_ref[row : row + 1, :] = jnp.sum(
            whole[row * side : (row + 1) * side] * high, axis=0, keepdims=True
        )


def atoms_to_slots(values, high, low, box, tile=4096):
    rows, count = values.shape
    side = int(round(math.sqrt(count)))
    table = pieces_bf16(values.reshape(rows * side, side), 0)
    slots = high.shape[1]
    return pl.pallas_call(
        atoms_to_slots_kernel,
        grid=(slots // tile,),
        in_specs=[
            pl.BlockSpec(table.shape, lambda i: (0, 0)),
            pl.BlockSpec((1, tile), lambda i: (0, i)),
            pl.BlockSpec((1, tile), lambda i: (0, i)),
            pl.BlockSpec((1, tile), lambda i: (0, i)),
        ],
        out_specs=pl.BlockSpec((rows + 1, tile), lambda i: (0, i)),
        out_shape=jax.ShapeDtypeStruct((rows + 1, slots), jnp.float32),
    )(table, high, low, box)


def slots_to_atoms_kernel(value_ref, high_ref, low_ref, out_ref):
    @pl.when(pl.program_id(0) == 0)
    def _():
        out_ref[...] = jnp.zeros_like(out_ref)

    side = out_ref.shape[1]
    tile = high_ref.shape[1]
    lines = lax.broadcasted_iota(jnp.int32, (side, tile), 0)
    hit = lines == high_ref[...]
    low = (lines == low_ref[...]).astype(jnp.bfloat16)
    value = value_ref[...]
    high_part = value.astype(jnp.bfloat16).astype(jnp.float32)
    rest = value - high_part
    middle_part = rest.astype(jnp.bfloat16).astype(jnp.float32)
    low_part = rest - middle_part
    stacked = jnp.concatenate(
        [jnp.where(hit, p, 0.0).astype(jnp.bfloat16) for p in (high_part, middle_part, low_part)],
        axis=0,
    )
    out_ref[...] += lax.dot_general(
        stacked, low, (((1,), (1,)), ((), ())), preferred_element_type=jnp.float32
    )


def slots_to_atoms(values, high, low, count, tile=8192):
    side = int(round(math.sqrt(count)))
    pieces = values.reshape(1, -1)
    slots = values.shape[0]
    parts = pl.pallas_call(
        slots_to_atoms_kernel,
        grid=(slots // tile,),
        in_specs=[
            pl.BlockSpec((1, tile), lambda i: (0, i)),
            pl.BlockSpec((1, tile), lambda i: (0, i)),
            pl.BlockSpec((1, tile), lambda i: (0, i)),
        ],
        out_specs=pl.BlockSpec((3 * side, side), lambda i: (0, 0)),
        out_shape=jax.ShapeDtypeStruct((3 * side, side), jnp.float32),
    )(pieces, high, low)
    return (parts[:side] + parts[side : 2 * side] + parts[2 * side :]).reshape(count)


def node_rows(data_ref, tile):
    nodes = lax.broadcasted_iota(jnp.int32, (NODES, tile), 0)
    spread = []
    for axis, shift in ((0, 4), (1, 2), (2, 0)):
        u = data_ref[1 + axis : 2 + axis, :]
        order_two = 2.0 * u * u - 1.0
        order_three = 4.0 * u * u * u - 3.0 * u
        rows = []
        for node_point in NODE_POINTS:
            cheb_two = 2.0 * node_point * node_point - 1.0
            cheb_three = 4.0 * node_point * node_point * node_point - 3.0 * node_point
            rows.append(0.25 + 0.5 * (node_point * u + cheb_two * order_two + cheb_three * order_three))
        pick = jnp.bitwise_and(jnp.right_shift(nodes, shift), 3)
        full = jnp.broadcast_to(rows[3], (NODES, tile))
        for p in range(3):
            full = jnp.where(pick == p, rows[p], full)
        spread.append(full)
    return spread[0] * spread[1] * spread[2]


def bf16_pieces_in_kernel(x):
    high = x.astype(jnp.bfloat16)
    low = (x - high.astype(jnp.float32)).astype(jnp.bfloat16)
    return jnp.concatenate([high, low], axis=0)


def split_two(x):
    high = lax.reduce_precision(x, exponent_bits=8, mantissa_bits=7)
    return jnp.concatenate(
        [high.astype(jnp.bfloat16), (x - high).astype(jnp.bfloat16)], axis=0
    )


def box_sum_kernel(data_ref, out_ref):
    @pl.when(pl.program_id(0) == 0)
    def _():
        out_ref[...] = jnp.zeros_like(out_ref)

    boxes = out_ref.shape[1]
    tile = data_ref.shape[1]
    box = data_ref[4:5, :].astype(jnp.int32)
    weighted = node_rows(data_ref, tile) * data_ref[0:1, :]
    hot = (lax.broadcasted_iota(jnp.int32, (boxes, tile), 0) == box).astype(jnp.bfloat16)
    out_ref[...] += lax.dot_general(
        bf16_pieces_in_kernel(weighted), hot, (((1,), (1,)), ((), ())),
        preferred_element_type=jnp.float32,
    )


def box_sum(data, boxes, tile=4096):
    rows, slots = data.shape
    parts = pl.pallas_call(
        box_sum_kernel,
        grid=(slots // tile,),
        in_specs=[pl.BlockSpec((rows, tile), lambda i: (0, i))],
        out_specs=pl.BlockSpec((2 * NODES, boxes), lambda i: (0, 0)),
        out_shape=jax.ShapeDtypeStruct((2 * NODES, boxes), jnp.float32),
    )(data)
    return parts[:NODES] + parts[NODES:]


def box_pick_kernel(table_ref, data_ref, out_ref):
    boxes = table_ref.shape[1]
    tile = data_ref.shape[1]
    box = data_ref[4:5, :].astype(jnp.int32)
    hot = (lax.broadcasted_iota(jnp.int32, (boxes, tile), 0) == box).astype(jnp.bfloat16)
    parts = jnp.dot(table_ref[...], hot, preferred_element_type=jnp.float32)
    picked = parts[:NODES] + parts[NODES:]
    out_ref[...] = jnp.sum(node_rows(data_ref, tile) * picked, axis=0, keepdims=True)


def box_pick(table, data, tile=4096):
    rows, slots = data.shape
    stacked = split_two(table)
    return pl.pallas_call(
        box_pick_kernel,
        grid=(slots // tile,),
        in_specs=[
            pl.BlockSpec(stacked.shape, lambda i: (0, 0)),
            pl.BlockSpec((rows, tile), lambda i: (0, i)),
        ],
        out_specs=pl.BlockSpec((1, tile), lambda i: (0, i)),
        out_shape=jax.ShapeDtypeStruct((1, slots), jnp.float32),
    )(stacked, data)[0]


def shell_table():
    table = np.full((5, 5, 5), 98, dtype=np.int32)
    counter = 0
    for shift_z in range(-2, 3):
        for shift_x in range(-2, 3):
            for shift_y in range(-2, 3):
                if max(abs(shift_z), abs(shift_x), abs(shift_y)) == 2:
                    table[shift_z + 2, shift_x + 2, shift_y + 2] = counter
                    counter += 1
    return table


def chebyshev_rows(coordinate):
    order_two = 2.0 * coordinate * coordinate - 1.0
    order_three = 4.0 * coordinate * coordinate * coordinate - 3.0 * coordinate
    stacked = []
    for node_point in NODE_POINTS:
        cheb_two = 2.0 * node_point * node_point - 1.0
        cheb_three = 4.0 * node_point * node_point * node_point - 3.0 * node_point
        stacked.append(
            0.25 + 0.5 * (node_point * coordinate + cheb_two * order_two + cheb_three * order_three)
        )
    return jnp.stack(stacked, 0)


def node_weights(coords):
    along_z = chebyshev_rows(coords[0])
    along_x = chebyshev_rows(coords[1])
    along_y = chebyshev_rows(coords[2])
    product = along_z[:, None, None, :] * along_x[None, :, None, :] * along_y[None, None, :, :]
    return product.reshape(64, coords.shape[1])


def silu_slope(value):
    sigma = jax.nn.sigmoid(value)
    return sigma * (1.0 + value * (1.0 - sigma))


def translate(padded, m2l_kernels):
    rank_count = padded.shape[0]
    depth_z = padded.shape[1] - 4
    wide_x = padded.shape[2]
    depth_x = wide_x - 4
    length_y = padded.shape[3]
    y_source = jnp.arange(length_y, dtype=jnp.int32)[:, None]
    y_target = jnp.arange(length_y, dtype=jnp.int32)[None, :]
    shift_y = jnp.stack(
        [(y_source == y_target + step).astype(jnp.float32) for step in range(-2, 3)], 0
    )
    x_source = jnp.arange(wide_x, dtype=jnp.int32)[:, None]
    x_target = jnp.arange(depth_x, dtype=jnp.int32)[None, :]
    shift_x = jnp.stack(
        [(x_source == x_target + 2 + step).astype(jnp.float32) for step in range(-2, 3)], 0
    )
    shifted = jnp.einsum("gvy,bzxv->gbzxy", shift_y, padded, precision=lax.Precision.HIGHEST)
    extended = jnp.concatenate(
        [m2l_kernels, jnp.zeros((1, rank_count, rank_count), jnp.float32)], axis=0
    )
    stencil = extended[jnp.asarray(shell_table())]
    summed = jnp.zeros((rank_count, depth_z, depth_x, length_y), jnp.float32)
    for plane in range(5):
        slab = shifted[:, :, plane : plane + depth_z]
        partial_value = jnp.einsum(
            "fgab,gbzpy->afzpy", stencil[plane], slab, precision=lax.Precision.HIGHEST
        )
        summed = summed + jnp.einsum(
            "afzpy,fpq->azqy", partial_value, shift_x, precision=lax.Precision.HIGHEST
        )
    return summed


def shards(
    desc,
    positions,
    species,
    w_in,
    w_mid,
    w_head,
    species_charge,
    m2l_kernels,
    expand_u,
    compress_v,
    send_list,
    slot_box,
):
    atom_count = desc.shape[0]
    total_atoms = atom_count * lax.axis_size(GRP) * lax.axis_size(DEV)
    grad_scale = 1.0 / math.sqrt(total_atoms)
    pre_one = jnp.dot(desc, w_in, preferred_element_type=jnp.float32)
    hidden_one = jax.nn.silu(pre_one).astype(jnp.bfloat16)
    pre_two = jnp.dot(hidden_one, w_mid, preferred_element_type=jnp.float32)
    hidden_two = jax.nn.silu(pre_two)
    species_hot = (
        species[None, :] == jnp.arange(species_charge.shape[0], dtype=jnp.int32)[:, None]
    ).astype(jnp.float32)
    charge = jnp.sum(hidden_two * w_head[None, :], axis=1) + jnp.dot(
        species_charge, species_hot, precision=lax.Precision.HIGHEST
    )
    is_used = send_list >= 0
    side = int(round(math.sqrt(atom_count)))
    atom_high = jnp.where(is_used, send_list // side, -1).reshape(1, -1)
    atom_low = (send_list % side).reshape(1, -1)
    packed = jnp.concatenate([charge[None, :], positions], axis=0)
    outgoing = atoms_to_slots(packed, atom_high, atom_low, slot_box.reshape(1, -1))
    outgoing = outgoing.reshape(outgoing.shape[0], *send_list.shape)
    arrived = lax.all_to_all(outgoing, DEV, split_axis=1, concat_axis=1, tiled=True)
    arrived = arrived.reshape(arrived.shape[0], -1)
    moments = box_sum(arrived, BOXES)
    node_grid = moments.reshape(NODES, BZ, BX, BY)
    reduced = jnp.einsum("nr,nzxy->rzxy", compress_v, node_grid, precision=lax.Precision.HIGHEST)
    padded = extended_2(reduced, ((GRP, 1), (DEV, 2)), 2)
    local_terms = translate(padded, m2l_kernels)
    expansion = jnp.dot(expand_u, local_terms.reshape(RANK, BOXES), precision=lax.Precision.HIGHEST)
    slot_potential = box_pick(expansion, arrived).reshape(send_list.shape)
    returned = lax.all_to_all(slot_potential, DEV, split_axis=0, concat_axis=0, tiled=True)
    potential = slots_to_atoms(returned.reshape(-1), atom_high, atom_low, atom_count)
    head_part = jnp.sum(potential[:, None] * hidden_two, axis=0) * grad_scale
    species_part = jnp.dot(species_hot, potential, precision=lax.Precision.HIGHEST) * grad_scale
    delta_two = (potential[:, None] * w_head[None, :] * silu_slope(pre_two)).astype(jnp.bfloat16)
    mid_part = (
        lax.dot_general(
            hidden_one, delta_two, (((0,), (0,)), ((), ())), preferred_element_type=jnp.float32
        )
        * grad_scale
    )
    back_one = lax.dot_general(
        delta_two, w_mid, (((1,), (1,)), ((), ())), preferred_element_type=jnp.float32
    )
    delta_one = (back_one * silu_slope(pre_one)).astype(jnp.bfloat16)
    in_part = (
        lax.dot_general(
            desc, delta_one, (((0,), (0,)), ((), ())), preferred_element_type=jnp.float32
        )
        * grad_scale
    )
    grad_in, grad_mid, grad_head, grad_species = summed_everywhere(
        (in_part, mid_part, head_part, species_part)
    )
    return (potential, grad_in, grad_mid, grad_head, grad_species)


def solution(mesh):
    torus = Mesh(mesh.devices.reshape(8, 2, 8, 4), ("grp_0", "grp_1", "dev_0", "dev_1"))
    placed = (
        P(GRP_DEV, None),
        P(None, GRP_DEV),
        P(GRP_DEV),
        P(),
        P(),
        P(),
        P(),
        P(),
        P(),
        P(),
        P(GRP_DEV, None),
        P(GRP_DEV, None),
    )
    return jax.shard_map(
        shards,
        mesh=torus,
        in_specs=placed,
        out_specs=(P(GRP_DEV), P(), P(), P(), P()),
        check_vma=False,
    )
```

```python
import math

import jax
import jax.numpy as jnp
import numpy as np
from jax import lax
from jax.experimental import pallas as pl
from jax.sharding import Mesh
from jax.sharding import PartitionSpec as P

NODES = 64
RANK = 16
BZ = 4
BX = 4
BY = 64
BOXES = 1024
GRP = ("grp_0", "grp_1")
DEV = ("dev_0", "dev_1")
GRP_DEV = ("grp_0", "grp_1", "dev_0", "dev_1")


NODE_POINTS = [math.cos((2 * node_number + 1) * math.pi / 8) for node_number in range(4)]


def extended_2(cells, sides, width):
    for axis, dim in sides:
        count = lax.axis_size(axis)
        ends = count - 1
        head = lax.slice_in_dim(cells, 0, width, axis=dim)
        tail = lax.slice_in_dim(cells, cells.shape[dim] - width, cells.shape[dim], axis=dim)
        cells = jnp.concatenate(
            [
                lax.ppermute(tail, axis, [(i, (i + 1) % count) for i in range(ends)]),
                cells,
                lax.ppermute(head, axis, [((i + 1) % count, i) for i in range(ends)]),
            ],
            axis=dim,
        )
    return cells


def in_blocks(x, dim, peers):
    before, after = (x.shape[:dim], x.shape[dim + 1 :])
    return jnp.moveaxis(x.reshape(*before, peers, -1, *after), dim, 0)


def sent_and_summed(x, axis, dim):
    blocks = in_blocks(x, dim, lax.axis_size(axis))
    arrived = lax.all_to_all(blocks, axis, split_axis=0, concat_axis=0, tiled=True)
    return arrived.sum(axis=0)


def sum_in_two_steps(x, axes, dim):
    far, near = axes
    blocks = in_blocks(x, dim, lax.axis_size(far))
    nearer = sent_and_summed(blocks, near, dim + 1)
    arrived = lax.all_to_all(nearer, far, split_axis=0, concat_axis=0, tiled=True)
    return arrived.sum(axis=0)


def padded_to(lines, peers):
    spare = -lines.shape[0] % peers
    if not spare:
        return lines
    return jnp.concatenate([lines, jnp.zeros((spare, *lines.shape[1:]), lines.dtype)])


def sent_to_all(x, axis):
    copies = jnp.broadcast_to(x, (lax.axis_size(axis), *x.shape))
    return lax.all_to_all(copies, axis, split_axis=0, concat_axis=0, tiled=True)


def laid_out(blocks, dim):
    dims = list(blocks.shape[1:])
    dims[dim] *= blocks.shape[0]
    return jnp.moveaxis(blocks, 0, dim).reshape(dims)


def whole_of(x, axes, dim):
    far, near = axes
    blocks = sent_to_all(sent_to_all(x, far), near)
    return laid_out(blocks.swapaxes(0, 1).reshape(-1, *x.shape), dim)


def nested_sum(x, axes):
    own = sum_in_two_steps(padded_to(x, lax.axis_size(axes[0]) * lax.axis_size(axes[1])), axes, 0)
    whole = whole_of(own, axes, 0)
    return whole[: len(x)].reshape(x.shape)


def together(arrays, axis):
    ends = [0]
    for a in arrays:
        ends.append(ends[-1] + a.size)
    total = nested_sum(jnp.concatenate([a.ravel() for a in arrays]), axis)
    return tuple((total[b:e].reshape(a.shape) for a, b, e in zip(arrays, ends, ends[1:])))


def swapped(x, axis, step):
    count = lax.axis_size(axis)
    return lax.ppermute(x, axis, [(i, i ^ step) for i in range(count)])


def butterfly_sum(x, axis):
    step = 1
    while step < lax.axis_size(axis):
        x = x + swapped(x, axis, step)
        step *= 2
    return x


def hybrid_sum(x, pair, plane, stack):
    length = x.shape[0]
    x = butterfly_sum(x, pair)
    peers = lax.axis_size(plane)
    lines = padded_to(x, peers).reshape(peers, -1)
    own = lax.all_to_all(lines, plane, 0, 0, tiled=True).reshape(peers, -1).sum(axis=0)
    own = butterfly_sum(own, stack)
    copies = jnp.broadcast_to(own, (peers, *own.shape))
    return lax.all_to_all(copies, plane, 0, 0, tiled=True).reshape(-1)[:length]


def summed_everywhere(arrays):
    ends = [0]
    for a in arrays:
        ends.append(ends[-1] + a.size)
    flat = jnp.concatenate([a.ravel() for a in arrays])
    total = hybrid_sum(flat, "grp_1", DEV, "grp_0")
    return tuple((total[b:e].reshape(a.shape) for a, b, e in zip(arrays, ends, ends[1:])))


def split_three(x):
    high = lax.reduce_precision(x, exponent_bits=8, mantissa_bits=7)
    rest = x - high
    middle = lax.reduce_precision(rest, exponent_bits=8, mantissa_bits=7)
    return high, middle, rest - middle


def pieces_bf16(x, axis):
    return jnp.concatenate([p.astype(jnp.bfloat16) for p in split_three(x)], axis=axis)


def atoms_to_slots_kernel(table_ref, high_ref, low_ref, box_ref, out_ref):
    rows, tile = out_ref.shape
    rows -= 1
    out_ref[rows : rows + 1, :] = box_ref[...].astype(jnp.float32)
    side = table_ref.shape[1]
    lines = lax.broadcasted_iota(jnp.int32, (side, tile), 0)
    low = (lines == low_ref[...]).astype(jnp.bfloat16)
    parts = jnp.dot(table_ref[...], low, preferred_element_type=jnp.float32)
    block = rows * side
    whole = parts[:block] + parts[block : 2 * block] + parts[2 * block :]
    high = (lines == high_ref[...]).astype(jnp.float32)
    for row in range(rows):
        out_ref[row : row + 1, :] = jnp.sum(
            whole[row * side : (row + 1) * side] * high, axis=0, keepdims=True
        )


def atoms_to_slots(values, high, low, box, tile=4096):
    rows, count = values.shape
    side = int(round(math.sqrt(count)))
    table = pieces_bf16(values.reshape(rows * side, side), 0)
    slots = high.shape[1]
    return pl.pallas_call(
        atoms_to_slots_kernel,
        grid=(slots // tile,),
        in_specs=[
            pl.BlockSpec(table.shape, lambda i: (0, 0)),
            pl.BlockSpec((1, tile), lambda i: (0, i)),
            pl.BlockSpec((1, tile), lambda i: (0, i)),
            pl.BlockSpec((1, tile), lambda i: (0, i)),
        ],
        out_specs=pl.BlockSpec((rows + 1, tile), lambda i: (0, i)),
        out_shape=jax.ShapeDtypeStruct((rows + 1, slots), jnp.float32),
    )(table, high, low, box)


def slots_to_atoms_kernel(value_ref, high_ref, low_ref, out_ref):
    @pl.when(pl.program_id(0) == 0)
    def _():
        out_ref[...] = jnp.zeros_like(out_ref)

    side = out_ref.shape[1]
    tile = high_ref.shape[1]
    lines = lax.broadcasted_iota(jnp.int32, (side, tile), 0)
    hit = lines == high_ref[...]
    low = (lines == low_ref[...]).astype(jnp.bfloat16)
    value = value_ref[...]
    high_part = value.astype(jnp.bfloat16).astype(jnp.float32)
    rest = value - high_part
    middle_part = rest.astype(jnp.bfloat16).astype(jnp.float32)
    low_part = rest - middle_part
    stacked = jnp.concatenate(
        [jnp.where(hit, p, 0.0).astype(jnp.bfloat16) for p in (high_part, middle_part, low_part)],
        axis=0,
    )
    out_ref[...] += lax.dot_general(
        stacked, low, (((1,), (1,)), ((), ())), preferred_element_type=jnp.float32
    )


def slots_to_atoms(values, high, low, count, tile=8192):
    side = int(round(math.sqrt(count)))
    pieces = values.reshape(1, -1)
    slots = values.shape[0]
    parts = pl.pallas_call(
        slots_to_atoms_kernel,
        grid=(slots // tile,),
        in_specs=[
            pl.BlockSpec((1, tile), lambda i: (0, i)),
            pl.BlockSpec((1, tile), lambda i: (0, i)),
            pl.BlockSpec((1, tile), lambda i: (0, i)),
        ],
        out_specs=pl.BlockSpec((3 * side, side), lambda i: (0, 0)),
        out_shape=jax.ShapeDtypeStruct((3 * side, side), jnp.float32),
    )(pieces, high, low)
    return (parts[:side] + parts[side : 2 * side] + parts[2 * side :]).reshape(count)


def node_rows(data_ref, tile):
    nodes = lax.broadcasted_iota(jnp.int32, (NODES, tile), 0)
    spread = []
    for axis, shift in ((0, 4), (1, 2), (2, 0)):
        u = data_ref[1 + axis : 2 + axis, :]
        order_two = 2.0 * u * u - 1.0
        order_three = 4.0 * u * u * u - 3.0 * u
        rows = []
        for node_point in NODE_POINTS:
            cheb_two = 2.0 * node_point * node_point - 1.0
            cheb_three = 4.0 * node_point * node_point * node_point - 3.0 * node_point
            rows.append(0.25 + 0.5 * (node_point * u + cheb_two * order_two + cheb_three * order_three))
        pick = jnp.bitwise_and(jnp.right_shift(nodes, shift), 3)
        full = jnp.broadcast_to(rows[3], (NODES, tile))
        for p in range(3):
            full = jnp.where(pick == p, rows[p], full)
        spread.append(full)
    return spread[0] * spread[1] * spread[2]


def bf16_pieces_in_kernel(x):
    high = x.astype(jnp.bfloat16)
    low = (x - high.astype(jnp.float32)).astype(jnp.bfloat16)
    return jnp.concatenate([high, low], axis=0)


def split_two(x):
    high = lax.reduce_precision(x, exponent_bits=8, mantissa_bits=7)
    return jnp.concatenate(
        [high.astype(jnp.bfloat16), (x - high).astype(jnp.bfloat16)], axis=0
    )


def box_sum_kernel(data_ref, out_ref):
    @pl.when(pl.program_id(0) == 0)
    def _():
        out_ref[...] = jnp.zeros_like(out_ref)

    boxes = out_ref.shape[1]
    tile = data_ref.shape[1]
    box = data_ref[4:5, :].astype(jnp.int32)
    weighted = node_rows(data_ref, tile) * data_ref[0:1, :]
    hot = (lax.broadcasted_iota(jnp.int32, (boxes, tile), 0) == box).astype(jnp.bfloat16)
    out_ref[...] += lax.dot_general(
        bf16_pieces_in_kernel(weighted), hot, (((1,), (1,)), ((), ())),
        preferred_element_type=jnp.float32,
    )


def box_sum(data, boxes, tile=4096):
    rows, slots = data.shape
    parts = pl.pallas_call(
        box_sum_kernel,
        grid=(slots // tile,),
        in_specs=[pl.BlockSpec((rows, tile), lambda i: (0, i))],
        out_specs=pl.BlockSpec((2 * NODES, boxes), lambda i: (0, 0)),
        out_shape=jax.ShapeDtypeStruct((2 * NODES, boxes), jnp.float32),
    )(data)
    return parts[:NODES] + parts[NODES:]


def box_pick_kernel(table_ref, data_ref, out_ref):
    boxes = table_ref.shape[1]
    tile = data_ref.shape[1]
    box = data_ref[4:5, :].astype(jnp.int32)
    hot = (lax.broadcasted_iota(jnp.int32, (boxes, tile), 0) == box).astype(jnp.bfloat16)
    parts = jnp.dot(table_ref[...], hot, preferred_element_type=jnp.float32)
    picked = parts[:NODES] + parts[NODES:]
    out_ref[...] = jnp.sum(node_rows(data_ref, tile) * picked, axis=0, keepdims=True)


def box_pick(table, data, tile=4096):
    rows, slots = data.shape
    stacked = split_two(table)
    return pl.pallas_call(
        box_pick_kernel,
        grid=(slots // tile,),
        in_specs=[
            pl.BlockSpec(stacked.shape, lambda i: (0, 0)),
            pl.BlockSpec((rows, tile), lambda i: (0, i)),
        ],
        out_specs=pl.BlockSpec((1, tile), lambda i: (0, i)),
        out_shape=jax.ShapeDtypeStruct((1, slots), jnp.float32),
    )(stacked, data)[0]


def shell_table():
    table = np.full((5, 5, 5), 98, dtype=np.int32)
    counter = 0
    for shift_z in range(-2, 3):
        for shift_x in range(-2, 3):
            for shift_y in range(-2, 3):
                if max(abs(shift_z), abs(shift_x), abs(shift_y)) == 2:
                    table[shift_z + 2, shift_x + 2, shift_y + 2] = counter
                    counter += 1
    return table


def chebyshev_rows(coordinate):
    order_two = 2.0 * coordinate * coordinate - 1.0
    order_three = 4.0 * coordinate * coordinate * coordinate - 3.0 * coordinate
    stacked = []
    for node_point in NODE_POINTS:
        cheb_two = 2.0 * node_point * node_point - 1.0
        cheb_three = 4.0 * node_point * node_point * node_point - 3.0 * node_point
        stacked.append(
            0.25 + 0.5 * (node_point * coordinate + cheb_two * order_two + cheb_three * order_three)
        )
    return jnp.stack(stacked, 0)


def node_weights(coords):
    along_z = chebyshev_rows(coords[0])
    along_x = chebyshev_rows(coords[1])
    along_y = chebyshev_rows(coords[2])
    product = along_z[:, None, None, :] * along_x[None, :, None, :] * along_y[None, None, :, :]
    return product.reshape(64, coords.shape[1])


def silu_slope(value):
    sigma = jax.nn.sigmoid(value)
    return sigma * (1.0 + value * (1.0 - sigma))


def translate(padded, m2l_kernels):
    rank_count = padded.shape[0]
    depth_z = padded.shape[1] - 4
    wide_x = padded.shape[2]
    depth_x = wide_x - 4
    length_y = padded.shape[3]
    y_source = jnp.arange(length_y, dtype=jnp.int32)[:, None]
    y_target = jnp.arange(length_y, dtype=jnp.int32)[None, :]
    shift_y = jnp.stack(
        [(y_source == y_target + step).astype(jnp.float32) for step in range(-2, 3)], 0
    )
    x_source = jnp.arange(wide_x, dtype=jnp.int32)[:, None]
    x_target = jnp.arange(depth_x, dtype=jnp.int32)[None, :]
    shift_x = jnp.stack(
        [(x_source == x_target + 2 + step).astype(jnp.float32) for step in range(-2, 3)], 0
    )
    shifted = jnp.einsum("gvy,bzxv->gbzxy", shift_y, padded, precision=lax.Precision.HIGHEST)
    extended = jnp.concatenate(
        [m2l_kernels, jnp.zeros((1, rank_count, rank_count), jnp.float32)], axis=0
    )
    stencil = extended[jnp.asarray(shell_table())]
    summed = jnp.zeros((rank_count, depth_z, depth_x, length_y), jnp.float32)
    for plane in range(5):
        slab = shifted[:, :, plane : plane + depth_z]
        partial_value = jnp.einsum(
            "fgab,gbzpy->afzpy", stencil[plane], slab, precision=lax.Precision.HIGHEST
        )
        summed = summed + jnp.einsum(
            "afzpy,fpq->azqy", partial_value, shift_x, precision=lax.Precision.HIGHEST
        )
    return summed


def shards(
    desc,
    positions,
    species,
    w_in,
    w_mid,
    w_head,
    species_charge,
    m2l_kernels,
    expand_u,
    compress_v,
    send_list,
    slot_box,
):
    atom_count = desc.shape[0]
    total_atoms = atom_count * lax.axis_size(GRP) * lax.axis_size(DEV)
    grad_scale = 1.0 / math.sqrt(total_atoms)
    pre_one = jnp.dot(desc, w_in, preferred_element_type=jnp.float32)
    hidden_one = jax.nn.silu(pre_one).astype(jnp.bfloat16)
    pre_two = jnp.dot(hidden_one, w_mid, preferred_element_type=jnp.float32)
    hidden_two = jax.nn.silu(pre_two)
    species_hot = (
        species[None, :] == jnp.arange(species_charge.shape[0], dtype=jnp.int32)[:, None]
    ).astype(jnp.float32)
    charge = jnp.sum(hidden_two * w_head[None, :], axis=1) + jnp.dot(
        species_charge, species_hot, precision=lax.Precision.HIGHEST
    )
    is_used = send_list >= 0
    side = int(round(math.sqrt(atom_count)))
    atom_high = jnp.where(is_used, send_list // side, -1).reshape(1, -1)
    atom_low = (send_list % side).reshape(1, -1)
    packed = jnp.concatenate([charge[None, :], positions], axis=0)
    outgoing = atoms_to_slots(packed, atom_high, atom_low, slot_box.reshape(1, -1))
    outgoing = outgoing.reshape(outgoing.shape[0], *send_list.shape)
    arrived = lax.all_to_all(outgoing, DEV, split_axis=1, concat_axis=1, tiled=True)
    arrived = arrived.reshape(arrived.shape[0], -1)
    moments = box_sum(arrived, BOXES)
    node_grid = moments.reshape(NODES, BZ, BX, BY)
    reduced = jnp.einsum("nr,nzxy->rzxy", compress_v, node_grid, precision=lax.Precision.HIGHEST)
    padded = extended_2(reduced, ((GRP, 1), (DEV, 2)), 2)
    padded, hidden_two, slope_two, slope_one = lax.optimization_barrier(
        (padded, hidden_two, silu_slope(pre_two), silu_slope(pre_one))
    )
    local_terms = translate(padded, m2l_kernels)
    expansion = jnp.dot(expand_u, local_terms.reshape(RANK, BOXES), precision=lax.Precision.HIGHEST)
    slot_potential = box_pick(expansion, arrived).reshape(send_list.shape)
    returned = lax.all_to_all(slot_potential, DEV, split_axis=0, concat_axis=0, tiled=True)
    potential = slots_to_atoms(returned.reshape(-1), atom_high, atom_low, atom_count)
    head_part = jnp.sum(potential[:, None] * hidden_two, axis=0) * grad_scale
    species_part = jnp.dot(species_hot, potential, precision=lax.Precision.HIGHEST) * grad_scale
    delta_two = (potential[:, None] * w_head[None, :] * slope_two).astype(jnp.bfloat16)
    mid_part = (
        lax.dot_general(
            hidden_one, delta_two, (((0,), (0,)), ((), ())), preferred_element_type=jnp.float32
        )
        * grad_scale
    )
    back_one = lax.dot_general(
        delta_two, w_mid, (((1,), (1,)), ((), ())), preferred_element_type=jnp.float32
    )
    delta_one = (back_one * slope_one).astype(jnp.bfloat16)
    in_part = (
        lax.dot_general(
            desc, delta_one, (((0,), (0,)), ((), ())), preferred_element_type=jnp.float32
        )
        * grad_scale
    )
    grad_in, grad_mid, grad_head, grad_species = summed_everywhere(
        (in_part, mid_part, head_part, species_part)
    )
    return (potential, grad_in, grad_mid, grad_head, grad_species)


def solution(mesh):
    torus = Mesh(mesh.devices.reshape(8, 2, 8, 4), ("grp_0", "grp_1", "dev_0", "dev_1"))
    placed = (
        P(GRP_DEV, None),
        P(None, GRP_DEV),
        P(GRP_DEV),
        P(),
        P(),
        P(),
        P(),
        P(),
        P(),
        P(),
        P(GRP_DEV, None),
        P(GRP_DEV, None),
    )
    return jax.shard_map(
        shards,
        mesh=torus,
        in_specs=placed,
        out_specs=(P(GRP_DEV), P(), P(), P(), P()),
        check_vma=False,
    )
```

```python
import math

import jax
import jax.numpy as jnp
import numpy as np
from jax import lax
from jax.experimental import pallas as pl
from jax.sharding import Mesh
from jax.sharding import PartitionSpec as P

NODES = 64
RANK = 16
BZ = 4
BX = 4
BY = 64
BOXES = 1024
GRP = ("grp_0", "grp_1")
DEV = ("dev_0", "dev_1")
GRP_DEV = ("grp_0", "grp_1", "dev_0", "dev_1")


NODE_POINTS = [math.cos((2 * node_number + 1) * math.pi / 8) for node_number in range(4)]


def extended_2(cells, sides, width):
    for axis, dim in sides:
        count = lax.axis_size(axis)
        ends = count - 1
        head = lax.slice_in_dim(cells, 0, width, axis=dim)
        tail = lax.slice_in_dim(cells, cells.shape[dim] - width, cells.shape[dim], axis=dim)
        cells = jnp.concatenate(
            [
                lax.ppermute(tail, axis, [(i, (i + 1) % count) for i in range(ends)]),
                cells,
                lax.ppermute(head, axis, [((i + 1) % count, i) for i in range(ends)]),
            ],
            axis=dim,
        )
    return cells


def shifted_pairs(counts, steps):
    pairs = []
    total = 1
    for count in counts:
        total *= count
    for source in range(total):
        place = []
        rest = source
        for count in reversed(counts):
            place.append(rest % count)
            rest //= count
        place = place[::-1]
        target = [p + s for p, s in zip(place, steps)]
        if all(0 <= t < c for t, c in zip(target, counts)):
            linear = 0
            for t, c in zip(target, counts):
                linear = linear * c + t
            pairs.append((source, linear))
    return pairs


def extended_at_once(cells, width):
    grp_count = lax.axis_size(GRP)
    dev_count = lax.axis_size(DEV)
    both = GRP + DEV

    def moved(block, axes, counts, steps):
        return lax.ppermute(block, axes, shifted_pairs(counts, steps))

    head_z, tail_z = cells[:, :width], cells[:, -width:]
    head_x, tail_x = cells[:, :, :width], cells[:, :, -width:]
    counts = (grp_count, dev_count)
    top = moved(tail_z, GRP, (grp_count,), (1,))
    bottom = moved(head_z, GRP, (grp_count,), (-1,))
    left = moved(tail_x, DEV, (dev_count,), (1,))
    right = moved(head_x, DEV, (dev_count,), (-1,))
    top_left = moved(tail_z[:, :, -width:], both, counts, (1, 1))
    top_right = moved(tail_z[:, :, :width], both, counts, (1, -1))
    bottom_left = moved(head_z[:, :, -width:], both, counts, (-1, 1))
    bottom_right = moved(head_z[:, :, :width], both, counts, (-1, -1))
    return jnp.concatenate(
        [
            jnp.concatenate([top_left, top, top_right], axis=2),
            jnp.concatenate([left, cells, right], axis=2),
            jnp.concatenate([bottom_left, bottom, bottom_right], axis=2),
        ],
        axis=1,
    )


def in_blocks(x, dim, peers):
    before, after = (x.shape[:dim], x.shape[dim + 1 :])
    return jnp.moveaxis(x.reshape(*before, peers, -1, *after), dim, 0)


def sent_and_summed(x, axis, dim):
    blocks = in_blocks(x, dim, lax.axis_size(axis))
    arrived = lax.all_to_all(blocks, axis, split_axis=0, concat_axis=0, tiled=True)
    return arrived.sum(axis=0)


def sum_in_two_steps(x, axes, dim):
    far, near = axes
    blocks = in_blocks(x, dim, lax.axis_size(far))
    nearer = sent_and_summed(blocks, near, dim + 1)
    arrived = lax.all_to_all(nearer, far, split_axis=0, concat_axis=0, tiled=True)
    return arrived.sum(axis=0)


def padded_to(lines, peers):
    spare = -lines.shape[0] % peers
    if not spare:
        return lines
    return jnp.concatenate([lines, jnp.zeros((spare, *lines.shape[1:]), lines.dtype)])


def sent_to_all(x, axis):
    copies = jnp.broadcast_to(x, (lax.axis_size(axis), *x.shape))
    return lax.all_to_all(copies, axis, split_axis=0, concat_axis=0, tiled=True)


def laid_out(blocks, dim):
    dims = list(blocks.shape[1:])
    dims[dim] *= blocks.shape[0]
    return jnp.moveaxis(blocks, 0, dim).reshape(dims)


def whole_of(x, axes, dim):
    far, near = axes
    blocks = sent_to_all(sent_to_all(x, far), near)
    return laid_out(blocks.swapaxes(0, 1).reshape(-1, *x.shape), dim)


def nested_sum(x, axes):
    own = sum_in_two_steps(padded_to(x, lax.axis_size(axes[0]) * lax.axis_size(axes[1])), axes, 0)
    whole = whole_of(own, axes, 0)
    return whole[: len(x)].reshape(x.shape)


def together(arrays, axis):
    ends = [0]
    for a in arrays:
        ends.append(ends[-1] + a.size)
    total = nested_sum(jnp.concatenate([a.ravel() for a in arrays]), axis)
    return tuple((total[b:e].reshape(a.shape) for a, b, e in zip(arrays, ends, ends[1:])))


def swapped(x, axis, step):
    count = lax.axis_size(axis)
    return lax.ppermute(x, axis, [(i, i ^ step) for i in range(count)])


def butterfly_sum(x, axis):
    step = 1
    while step < lax.axis_size(axis):
        x = x + swapped(x, axis, step)
        step *= 2
    return x


def hybrid_sum(x, pair, plane, stack):
    length = x.shape[0]
    x = butterfly_sum(x, pair)
    peers = lax.axis_size(plane)
    lines = padded_to(x, peers).reshape(peers, -1)
    own = lax.all_to_all(lines, plane, 0, 0, tiled=True).reshape(peers, -1).sum(axis=0)
    own = butterfly_sum(own, stack)
    copies = jnp.broadcast_to(own, (peers, *own.shape))
    return lax.all_to_all(copies, plane, 0, 0, tiled=True).reshape(-1)[:length]


def summed_everywhere(arrays):
    ends = [0]
    for a in arrays:
        ends.append(ends[-1] + a.size)
    flat = jnp.concatenate([a.ravel() for a in arrays])
    total = hybrid_sum(flat, "grp_1", DEV, "grp_0")
    return tuple((total[b:e].reshape(a.shape) for a, b, e in zip(arrays, ends, ends[1:])))


def split_three(x):
    high = lax.reduce_precision(x, exponent_bits=8, mantissa_bits=7)
    rest = x - high
    middle = lax.reduce_precision(rest, exponent_bits=8, mantissa_bits=7)
    return high, middle, rest - middle


def pieces_bf16(x, axis):
    return jnp.concatenate([p.astype(jnp.bfloat16) for p in split_three(x)], axis=axis)


def atoms_to_slots_kernel(table_ref, high_ref, low_ref, box_ref, out_ref):
    rows, tile = out_ref.shape
    rows -= 1
    out_ref[rows : rows + 1, :] = box_ref[...].astype(jnp.float32)
    side = table_ref.shape[1]
    lines = lax.broadcasted_iota(jnp.int32, (side, tile), 0)
    low = (lines == low_ref[...]).astype(jnp.bfloat16)
    parts = jnp.dot(table_ref[...], low, preferred_element_type=jnp.float32)
    block = rows * side
    whole = parts[:block] + parts[block : 2 * block] + parts[2 * block :]
    high = (lines == high_ref[...]).astype(jnp.float32)
    for row in range(rows):
        out_ref[row : row + 1, :] = jnp.sum(
            whole[row * side : (row + 1) * side] * high, axis=0, keepdims=True
        )


def atoms_to_slots(values, high, low, box, tile=4096):
    rows, count = values.shape
    side = int(round(math.sqrt(count)))
    table = pieces_bf16(values.reshape(rows * side, side), 0)
    slots = high.shape[1]
    return pl.pallas_call(
        atoms_to_slots_kernel,
        grid=(slots // tile,),
        in_specs=[
            pl.BlockSpec(table.shape, lambda i: (0, 0)),
            pl.BlockSpec((1, tile), lambda i: (0, i)),
            pl.BlockSpec((1, tile), lambda i: (0, i)),
            pl.BlockSpec((1, tile), lambda i: (0, i)),
        ],
        out_specs=pl.BlockSpec((rows + 1, tile), lambda i: (0, i)),
        out_shape=jax.ShapeDtypeStruct((rows + 1, slots), jnp.float32),
    )(table, high, low, box)


def slots_to_atoms_kernel(value_ref, high_ref, low_ref, out_ref):
    @pl.when(pl.program_id(0) == 0)
    def _():
        out_ref[...] = jnp.zeros_like(out_ref)

    side = out_ref.shape[1]
    tile = high_ref.shape[1]
    lines = lax.broadcasted_iota(jnp.int32, (side, tile), 0)
    hit = lines == high_ref[...]
    low = (lines == low_ref[...]).astype(jnp.bfloat16)
    value = value_ref[...]
    high_part = value.astype(jnp.bfloat16).astype(jnp.float32)
    rest = value - high_part
    middle_part = rest.astype(jnp.bfloat16).astype(jnp.float32)
    low_part = rest - middle_part
    stacked = jnp.concatenate(
        [jnp.where(hit, p, 0.0).astype(jnp.bfloat16) for p in (high_part, middle_part, low_part)],
        axis=0,
    )
    out_ref[...] += lax.dot_general(
        stacked, low, (((1,), (1,)), ((), ())), preferred_element_type=jnp.float32
    )


def slots_to_atoms(values, high, low, count, tile=8192):
    side = int(round(math.sqrt(count)))
    pieces = values.reshape(1, -1)
    slots = values.shape[0]
    parts = pl.pallas_call(
        slots_to_atoms_kernel,
        grid=(slots // tile,),
        in_specs=[
            pl.BlockSpec((1, tile), lambda i: (0, i)),
            pl.BlockSpec((1, tile), lambda i: (0, i)),
            pl.BlockSpec((1, tile), lambda i: (0, i)),
        ],
        out_specs=pl.BlockSpec((3 * side, side), lambda i: (0, 0)),
        out_shape=jax.ShapeDtypeStruct((3 * side, side), jnp.float32),
    )(pieces, high, low)
    return (parts[:side] + parts[side : 2 * side] + parts[2 * side :]).reshape(count)


def node_rows(data_ref, tile):
    nodes = lax.broadcasted_iota(jnp.int32, (NODES, tile), 0)
    spread = []
    for axis, shift in ((0, 4), (1, 2), (2, 0)):
        u = data_ref[1 + axis : 2 + axis, :]
        order_two = 2.0 * u * u - 1.0
        order_three = 4.0 * u * u * u - 3.0 * u
        rows = []
        for node_point in NODE_POINTS:
            cheb_two = 2.0 * node_point * node_point - 1.0
            cheb_three = 4.0 * node_point * node_point * node_point - 3.0 * node_point
            rows.append(0.25 + 0.5 * (node_point * u + cheb_two * order_two + cheb_three * order_three))
        pick = jnp.bitwise_and(jnp.right_shift(nodes, shift), 3)
        full = jnp.broadcast_to(rows[3], (NODES, tile))
        for p in range(3):
            full = jnp.where(pick == p, rows[p], full)
        spread.append(full)
    return spread[0] * spread[1] * spread[2]


def bf16_pieces_in_kernel(x):
    high = x.astype(jnp.bfloat16)
    low = (x - high.astype(jnp.float32)).astype(jnp.bfloat16)
    return jnp.concatenate([high, low], axis=0)


def split_two(x):
    high = lax.reduce_precision(x, exponent_bits=8, mantissa_bits=7)
    return jnp.concatenate(
        [high.astype(jnp.bfloat16), (x - high).astype(jnp.bfloat16)], axis=0
    )


def box_sum_kernel(data_ref, out_ref):
    @pl.when(pl.program_id(0) == 0)
    def _():
        out_ref[...] = jnp.zeros_like(out_ref)

    boxes = out_ref.shape[1]
    tile = data_ref.shape[1]
    box = data_ref[4:5, :].astype(jnp.int32)
    weighted = node_rows(data_ref, tile) * data_ref[0:1, :]
    hot = (lax.broadcasted_iota(jnp.int32, (boxes, tile), 0) == box).astype(jnp.bfloat16)
    out_ref[...] += lax.dot_general(
        bf16_pieces_in_kernel(weighted), hot, (((1,), (1,)), ((), ())),
        preferred_element_type=jnp.float32,
    )


def box_sum(data, boxes, tile=4096):
    rows, slots = data.shape
    parts = pl.pallas_call(
        box_sum_kernel,
        grid=(slots // tile,),
        in_specs=[pl.BlockSpec((rows, tile), lambda i: (0, i))],
        out_specs=pl.BlockSpec((2 * NODES, boxes), lambda i: (0, 0)),
        out_shape=jax.ShapeDtypeStruct((2 * NODES, boxes), jnp.float32),
    )(data)
    return parts[:NODES] + parts[NODES:]


def box_pick_kernel(table_ref, data_ref, out_ref):
    boxes = table_ref.shape[1]
    tile = data_ref.shape[1]
    box = data_ref[4:5, :].astype(jnp.int32)
    hot = (lax.broadcasted_iota(jnp.int32, (boxes, tile), 0) == box).astype(jnp.bfloat16)
    parts = jnp.dot(table_ref[...], hot, preferred_element_type=jnp.float32)
    picked = parts[:NODES] + parts[NODES:]
    out_ref[...] = jnp.sum(node_rows(data_ref, tile) * picked, axis=0, keepdims=True)


def box_pick(table, data, tile=4096):
    rows, slots = data.shape
    stacked = split_two(table)
    return pl.pallas_call(
        box_pick_kernel,
        grid=(slots // tile,),
        in_specs=[
            pl.BlockSpec(stacked.shape, lambda i: (0, 0)),
            pl.BlockSpec((rows, tile), lambda i: (0, i)),
        ],
        out_specs=pl.BlockSpec((1, tile), lambda i: (0, i)),
        out_shape=jax.ShapeDtypeStruct((1, slots), jnp.float32),
    )(stacked, data)[0]


def shell_table():
    table = np.full((5, 5, 5), 98, dtype=np.int32)
    counter = 0
    for shift_z in range(-2, 3):
        for shift_x in range(-2, 3):
            for shift_y in range(-2, 3):
                if max(abs(shift_z), abs(shift_x), abs(shift_y)) == 2:
                    table[shift_z + 2, shift_x + 2, shift_y + 2] = counter
                    counter += 1
    return table


def chebyshev_rows(coordinate):
    order_two = 2.0 * coordinate * coordinate - 1.0
    order_three = 4.0 * coordinate * coordinate * coordinate - 3.0 * coordinate
    stacked = []
    for node_point in NODE_POINTS:
        cheb_two = 2.0 * node_point * node_point - 1.0
        cheb_three = 4.0 * node_point * node_point * node_point - 3.0 * node_point
        stacked.append(
            0.25 + 0.5 * (node_point * coordinate + cheb_two * order_two + cheb_three * order_three)
        )
    return jnp.stack(stacked, 0)


def node_weights(coords):
    along_z = chebyshev_rows(coords[0])
    along_x = chebyshev_rows(coords[1])
    along_y = chebyshev_rows(coords[2])
    product = along_z[:, None, None, :] * along_x[None, :, None, :] * along_y[None, None, :, :]
    return product.reshape(64, coords.shape[1])


def silu_slope(value):
    sigma = jax.nn.sigmoid(value)
    return sigma * (1.0 + value * (1.0 - sigma))


def translate(padded, m2l_kernels):
    rank_count = padded.shape[0]
    depth_z = padded.shape[1] - 4
    wide_x = padded.shape[2]
    depth_x = wide_x - 4
    length_y = padded.shape[3]
    y_source = jnp.arange(length_y, dtype=jnp.int32)[:, None]
    y_target = jnp.arange(length_y, dtype=jnp.int32)[None, :]
    shift_y = jnp.stack(
        [(y_source == y_target + step).astype(jnp.float32) for step in range(-2, 3)], 0
    )
    x_source = jnp.arange(wide_x, dtype=jnp.int32)[:, None]
    x_target = jnp.arange(depth_x, dtype=jnp.int32)[None, :]
    shift_x = jnp.stack(
        [(x_source == x_target + 2 + step).astype(jnp.float32) for step in range(-2, 3)], 0
    )
    shifted = jnp.einsum("gvy,bzxv->gbzxy", shift_y, padded, precision=lax.Precision.HIGHEST)
    extended = jnp.concatenate(
        [m2l_kernels, jnp.zeros((1, rank_count, rank_count), jnp.float32)], axis=0
    )
    stencil = extended[jnp.asarray(shell_table())]
    summed = jnp.zeros((rank_count, depth_z, depth_x, length_y), jnp.float32)
    for plane in range(5):
        slab = shifted[:, :, plane : plane + depth_z]
        partial_value = jnp.einsum(
            "fgab,gbzpy->afzpy", stencil[plane], slab, precision=lax.Precision.HIGHEST
        )
        summed = summed + jnp.einsum(
            "afzpy,fpq->azqy", partial_value, shift_x, precision=lax.Precision.HIGHEST
        )
    return summed


def shards(
    desc,
    positions,
    species,
    w_in,
    w_mid,
    w_head,
    species_charge,
    m2l_kernels,
    expand_u,
    compress_v,
    send_list,
    slot_box,
):
    atom_count = desc.shape[0]
    total_atoms = atom_count * lax.axis_size(GRP) * lax.axis_size(DEV)
    grad_scale = 1.0 / math.sqrt(total_atoms)
    pre_one = jnp.dot(desc, w_in, preferred_element_type=jnp.float32)
    hidden_one = jax.nn.silu(pre_one).astype(jnp.bfloat16)
    pre_two = jnp.dot(hidden_one, w_mid, preferred_element_type=jnp.float32)
    hidden_two = jax.nn.silu(pre_two)
    species_hot = (
        species[None, :] == jnp.arange(species_charge.shape[0], dtype=jnp.int32)[:, None]
    ).astype(jnp.float32)
    charge = jnp.sum(hidden_two * w_head[None, :], axis=1) + jnp.dot(
        species_charge, species_hot, precision=lax.Precision.HIGHEST
    )
    is_used = send_list >= 0
    side = int(round(math.sqrt(atom_count)))
    atom_high = jnp.where(is_used, send_list // side, -1).reshape(1, -1)
    atom_low = (send_list % side).reshape(1, -1)
    packed = jnp.concatenate([charge[None, :], positions], axis=0)
    outgoing = atoms_to_slots(packed, atom_high, atom_low, slot_box.reshape(1, -1))
    outgoing = outgoing.reshape(outgoing.shape[0], *send_list.shape)
    arrived = lax.all_to_all(outgoing, DEV, split_axis=1, concat_axis=1, tiled=True)
    arrived = arrived.reshape(arrived.shape[0], -1)
    moments = box_sum(arrived, BOXES)
    node_grid = moments.reshape(NODES, BZ, BX, BY)
    reduced = jnp.einsum("nr,nzxy->rzxy", compress_v, node_grid, precision=lax.Precision.HIGHEST)
    padded = extended_at_once(reduced, 2)
    local_terms = translate(padded, m2l_kernels)
    expansion = jnp.dot(expand_u, local_terms.reshape(RANK, BOXES), precision=lax.Precision.HIGHEST)
    slot_potential = box_pick(expansion, arrived).reshape(send_list.shape)
    returned = lax.all_to_all(slot_potential, DEV, split_axis=0, concat_axis=0, tiled=True)
    potential = slots_to_atoms(returned.reshape(-1), atom_high, atom_low, atom_count)
    head_part = jnp.sum(potential[:, None] * hidden_two, axis=0) * grad_scale
    species_part = jnp.dot(species_hot, potential, precision=lax.Precision.HIGHEST) * grad_scale
    delta_two = (potential[:, None] * w_head[None, :] * silu_slope(pre_two)).astype(jnp.bfloat16)
    mid_part = (
        lax.dot_general(
            hidden_one, delta_two, (((0,), (0,)), ((), ())), preferred_element_type=jnp.float32
        )
        * grad_scale
    )
    back_one = lax.dot_general(
        delta_two, w_mid, (((1,), (1,)), ((), ())), preferred_element_type=jnp.float32
    )
    delta_one = (back_one * silu_slope(pre_one)).astype(jnp.bfloat16)
    in_part = (
        lax.dot_general(
            desc, delta_one, (((0,), (0,)), ((), ())), preferred_element_type=jnp.float32
        )
        * grad_scale
    )
    grad_in, grad_mid, grad_head, grad_species = summed_everywhere(
        (in_part, mid_part, head_part, species_part)
    )
    return (potential, grad_in, grad_mid, grad_head, grad_species)


def solution(mesh):
    torus = Mesh(mesh.devices.reshape(8, 2, 8, 4), ("grp_0", "grp_1", "dev_0", "dev_1"))
    placed = (
        P(GRP_DEV, None),
        P(None, GRP_DEV),
        P(GRP_DEV),
        P(),
        P(),
        P(),
        P(),
        P(),
        P(),
        P(),
        P(GRP_DEV, None),
        P(GRP_DEV, None),
    )
    return jax.shard_map(
        shards,
        mesh=torus,
        in_specs=placed,
        out_specs=(P(GRP_DEV), P(), P(), P(), P()),
        check_vma=False,
    )
```

```python
import math

import jax
import jax.numpy as jnp
import numpy as np
from jax import lax
from jax.experimental import pallas as pl
from jax.sharding import Mesh
from jax.sharding import PartitionSpec as P

NODES = 64
RANK = 16
BZ = 4
BX = 4
BY = 64
BOXES = 1024
GRP = ("grp_0", "grp_1")
DEV = ("dev_0", "dev_1")
GRP_DEV = ("grp_0", "grp_1", "dev_0", "dev_1")


NODE_POINTS = [math.cos((2 * node_number + 1) * math.pi / 8) for node_number in range(4)]


def extended_2(cells, sides, width):
    for axis, dim in sides:
        count = lax.axis_size(axis)
        ends = count - 1
        head = lax.slice_in_dim(cells, 0, width, axis=dim)
        tail = lax.slice_in_dim(cells, cells.shape[dim] - width, cells.shape[dim], axis=dim)
        cells = jnp.concatenate(
            [
                lax.ppermute(tail, axis, [(i, (i + 1) % count) for i in range(ends)]),
                cells,
                lax.ppermute(head, axis, [((i + 1) % count, i) for i in range(ends)]),
            ],
            axis=dim,
        )
    return cells


def in_blocks(x, dim, peers):
    before, after = (x.shape[:dim], x.shape[dim + 1 :])
    return jnp.moveaxis(x.reshape(*before, peers, -1, *after), dim, 0)


def sent_and_summed(x, axis, dim):
    blocks = in_blocks(x, dim, lax.axis_size(axis))
    arrived = lax.all_to_all(blocks, axis, split_axis=0, concat_axis=0, tiled=True)
    return arrived.sum(axis=0)


def sum_in_two_steps(x, axes, dim):
    far, near = axes
    blocks = in_blocks(x, dim, lax.axis_size(far))
    nearer = sent_and_summed(blocks, near, dim + 1)
    arrived = lax.all_to_all(nearer, far, split_axis=0, concat_axis=0, tiled=True)
    return arrived.sum(axis=0)


def padded_to(lines, peers):
    spare = -lines.shape[0] % peers
    if not spare:
        return lines
    return jnp.concatenate([lines, jnp.zeros((spare, *lines.shape[1:]), lines.dtype)])


def sent_to_all(x, axis):
    copies = jnp.broadcast_to(x, (lax.axis_size(axis), *x.shape))
    return lax.all_to_all(copies, axis, split_axis=0, concat_axis=0, tiled=True)


def laid_out(blocks, dim):
    dims = list(blocks.shape[1:])
    dims[dim] *= blocks.shape[0]
    return jnp.moveaxis(blocks, 0, dim).reshape(dims)


def whole_of(x, axes, dim):
    far, near = axes
    blocks = sent_to_all(sent_to_all(x, far), near)
    return laid_out(blocks.swapaxes(0, 1).reshape(-1, *x.shape), dim)


def nested_sum(x, axes):
    own = sum_in_two_steps(padded_to(x, lax.axis_size(axes[0]) * lax.axis_size(axes[1])), axes, 0)
    whole = whole_of(own, axes, 0)
    return whole[: len(x)].reshape(x.shape)


def together(arrays, axis):
    ends = [0]
    for a in arrays:
        ends.append(ends[-1] + a.size)
    total = nested_sum(jnp.concatenate([a.ravel() for a in arrays]), axis)
    return tuple((total[b:e].reshape(a.shape) for a, b, e in zip(arrays, ends, ends[1:])))


def swapped(x, axis, step):
    count = lax.axis_size(axis)
    return lax.ppermute(x, axis, [(i, i ^ step) for i in range(count)])


def butterfly_sum(x, axis):
    step = 1
    while step < lax.axis_size(axis):
        x = x + swapped(x, axis, step)
        step *= 2
    return x


def hybrid_sum(x, pair, plane, stack):
    length = x.shape[0]
    x = butterfly_sum(x, pair)
    peers = lax.axis_size(plane)
    lines = padded_to(x, peers).reshape(peers, -1)
    own = lax.all_to_all(lines, plane, 0, 0, tiled=True).reshape(peers, -1).sum(axis=0)
    own = butterfly_sum(own, stack)
    copies = jnp.broadcast_to(own, (peers, *own.shape))
    return lax.all_to_all(copies, plane, 0, 0, tiled=True).reshape(-1)[:length]


def summed_everywhere(arrays):
    ends = [0]
    for a in arrays:
        ends.append(ends[-1] + a.size)
    flat = jnp.concatenate([a.ravel() for a in arrays])
    total = hybrid_sum(flat, "grp_1", DEV, "grp_0")
    return tuple((total[b:e].reshape(a.shape) for a, b, e in zip(arrays, ends, ends[1:])))


def split_three(x):
    high = lax.reduce_precision(x, exponent_bits=8, mantissa_bits=7)
    rest = x - high
    middle = lax.reduce_precision(rest, exponent_bits=8, mantissa_bits=7)
    return high, middle, rest - middle


def pieces_bf16(x, axis):
    return jnp.concatenate([p.astype(jnp.bfloat16) for p in split_three(x)], axis=axis)


def atoms_to_slots_kernel(table_ref, high_ref, low_ref, box_ref, out_ref):
    rows, tile = out_ref.shape
    rows -= 1
    out_ref[rows : rows + 1, :] = box_ref[...].astype(jnp.float32)
    side = table_ref.shape[1]
    lines = lax.broadcasted_iota(jnp.int32, (side, tile), 0)
    low = (lines == low_ref[...]).astype(jnp.bfloat16)
    parts = jnp.dot(table_ref[...], low, preferred_element_type=jnp.float32)
    block = rows * side
    whole = parts[:block] + parts[block : 2 * block] + parts[2 * block :]
    high = (lines == high_ref[...]).astype(jnp.float32)
    for row in range(rows):
        out_ref[row : row + 1, :] = jnp.sum(
            whole[row * side : (row + 1) * side] * high, axis=0, keepdims=True
        )


def atoms_to_slots(values, high, low, box, tile=8192):
    rows, count = values.shape
    side = int(round(math.sqrt(count)))
    table = pieces_bf16(values.reshape(rows * side, side), 0)
    slots = high.shape[1]
    return pl.pallas_call(
        atoms_to_slots_kernel,
        grid=(slots // tile,),
        in_specs=[
            pl.BlockSpec(table.shape, lambda i: (0, 0)),
            pl.BlockSpec((1, tile), lambda i: (0, i)),
            pl.BlockSpec((1, tile), lambda i: (0, i)),
            pl.BlockSpec((1, tile), lambda i: (0, i)),
        ],
        out_specs=pl.BlockSpec((rows + 1, tile), lambda i: (0, i)),
        out_shape=jax.ShapeDtypeStruct((rows + 1, slots), jnp.float32),
    )(table, high, low, box)


def slots_to_atoms_kernel(value_ref, high_ref, low_ref, out_ref):
    @pl.when(pl.program_id(0) == 0)
    def _():
        out_ref[...] = jnp.zeros_like(out_ref)

    side = out_ref.shape[1]
    tile = high_ref.shape[1]
    lines = lax.broadcasted_iota(jnp.int32, (side, tile), 0)
    hit = lines == high_ref[...]
    low = (lines == low_ref[...]).astype(jnp.bfloat16)
    value = value_ref[...]
    high_part = value.astype(jnp.bfloat16).astype(jnp.float32)
    rest = value - high_part
    middle_part = rest.astype(jnp.bfloat16).astype(jnp.float32)
    low_part = rest - middle_part
    stacked = jnp.concatenate(
        [jnp.where(hit, p, 0.0).astype(jnp.bfloat16) for p in (high_part, middle_part, low_part)],
        axis=0,
    )
    out_ref[...] += lax.dot_general(
        stacked, low, (((1,), (1,)), ((), ())), preferred_element_type=jnp.float32
    )


def slots_to_atoms(values, high, low, count, tile=8192):
    side = int(round(math.sqrt(count)))
    pieces = values.reshape(1, -1)
    slots = values.shape[0]
    parts = pl.pallas_call(
        slots_to_atoms_kernel,
        grid=(slots // tile,),
        in_specs=[
            pl.BlockSpec((1, tile), lambda i: (0, i)),
            pl.BlockSpec((1, tile), lambda i: (0, i)),
            pl.BlockSpec((1, tile), lambda i: (0, i)),
        ],
        out_specs=pl.BlockSpec((3 * side, side), lambda i: (0, 0)),
        out_shape=jax.ShapeDtypeStruct((3 * side, side), jnp.float32),
    )(pieces, high, low)
    return (parts[:side] + parts[side : 2 * side] + parts[2 * side :]).reshape(count)


def node_rows(data_ref, tile):
    nodes = lax.broadcasted_iota(jnp.int32, (NODES, tile), 0)
    spread = []
    for axis, shift in ((0, 4), (1, 2), (2, 0)):
        u = data_ref[1 + axis : 2 + axis, :]
        order_two = 2.0 * u * u - 1.0
        order_three = 4.0 * u * u * u - 3.0 * u
        rows = []
        for node_point in NODE_POINTS:
            cheb_two = 2.0 * node_point * node_point - 1.0
            cheb_three = 4.0 * node_point * node_point * node_point - 3.0 * node_point
            rows.append(0.25 + 0.5 * (node_point * u + cheb_two * order_two + cheb_three * order_three))
        pick = jnp.bitwise_and(jnp.right_shift(nodes, shift), 3)
        full = jnp.broadcast_to(rows[3], (NODES, tile))
        for p in range(3):
            full = jnp.where(pick == p, rows[p], full)
        spread.append(full)
    return spread[0] * spread[1] * spread[2]


def bf16_pieces_in_kernel(x):
    high = x.astype(jnp.bfloat16)
    low = (x - high.astype(jnp.float32)).astype(jnp.bfloat16)
    return jnp.concatenate([high, low], axis=0)


def split_two(x):
    high = lax.reduce_precision(x, exponent_bits=8, mantissa_bits=7)
    return jnp.concatenate(
        [high.astype(jnp.bfloat16), (x - high).astype(jnp.bfloat16)], axis=0
    )


def box_sum_kernel(data_ref, out_ref):
    @pl.when(pl.program_id(0) == 0)
    def _():
        out_ref[...] = jnp.zeros_like(out_ref)

    boxes = out_ref.shape[1]
    tile = data_ref.shape[1]
    box = data_ref[4:5, :].astype(jnp.int32)
    weighted = node_rows(data_ref, tile) * data_ref[0:1, :]
    hot = (lax.broadcasted_iota(jnp.int32, (boxes, tile), 0) == box).astype(jnp.bfloat16)
    out_ref[...] += lax.dot_general(
        bf16_pieces_in_kernel(weighted), hot, (((1,), (1,)), ((), ())),
        preferred_element_type=jnp.float32,
    )


def box_sum(data, boxes, tile=4096):
    rows, slots = data.shape
    parts = pl.pallas_call(
        box_sum_kernel,
        grid=(slots // tile,),
        in_specs=[pl.BlockSpec((rows, tile), lambda i: (0, i))],
        out_specs=pl.BlockSpec((2 * NODES, boxes), lambda i: (0, 0)),
        out_shape=jax.ShapeDtypeStruct((2 * NODES, boxes), jnp.float32),
    )(data)
    return parts[:NODES] + parts[NODES:]


def box_pick_kernel(table_ref, data_ref, out_ref):
    boxes = table_ref.shape[1]
    tile = data_ref.shape[1]
    box = data_ref[4:5, :].astype(jnp.int32)
    hot = (lax.broadcasted_iota(jnp.int32, (boxes, tile), 0) == box).astype(jnp.bfloat16)
    parts = jnp.dot(table_ref[...], hot, preferred_element_type=jnp.float32)
    picked = parts[:NODES] + parts[NODES:]
    out_ref[...] = jnp.sum(node_rows(data_ref, tile) * picked, axis=0, keepdims=True)


def box_pick(table, data, tile=4096):
    rows, slots = data.shape
    stacked = split_two(table)
    return pl.pallas_call(
        box_pick_kernel,
        grid=(slots // tile,),
        in_specs=[
            pl.BlockSpec(stacked.shape, lambda i: (0, 0)),
            pl.BlockSpec((rows, tile), lambda i: (0, i)),
        ],
        out_specs=pl.BlockSpec((1, tile), lambda i: (0, i)),
        out_shape=jax.ShapeDtypeStruct((1, slots), jnp.float32),
    )(stacked, data)[0]


def shell_table():
    table = np.full((5, 5, 5), 98, dtype=np.int32)
    counter = 0
    for shift_z in range(-2, 3):
        for shift_x in range(-2, 3):
            for shift_y in range(-2, 3):
                if max(abs(shift_z), abs(shift_x), abs(shift_y)) == 2:
                    table[shift_z + 2, shift_x + 2, shift_y + 2] = counter
                    counter += 1
    return table


def chebyshev_rows(coordinate):
    order_two = 2.0 * coordinate * coordinate - 1.0
    order_three = 4.0 * coordinate * coordinate * coordinate - 3.0 * coordinate
    stacked = []
    for node_point in NODE_POINTS:
        cheb_two = 2.0 * node_point * node_point - 1.0
        cheb_three = 4.0 * node_point * node_point * node_point - 3.0 * node_point
        stacked.append(
            0.25 + 0.5 * (node_point * coordinate + cheb_two * order_two + cheb_three * order_three)
        )
    return jnp.stack(stacked, 0)


def node_weights(coords):
    along_z = chebyshev_rows(coords[0])
    along_x = chebyshev_rows(coords[1])
    along_y = chebyshev_rows(coords[2])
    product = along_z[:, None, None, :] * along_x[None, :, None, :] * along_y[None, None, :, :]
    return product.reshape(64, coords.shape[1])


def silu_slope(value):
    sigma = jax.nn.sigmoid(value)
    return sigma * (1.0 + value * (1.0 - sigma))


def translate(padded, m2l_kernels):
    rank_count = padded.shape[0]
    depth_z = padded.shape[1] - 4
    wide_x = padded.shape[2]
    depth_x = wide_x - 4
    length_y = padded.shape[3]
    y_source = jnp.arange(length_y, dtype=jnp.int32)[:, None]
    y_target = jnp.arange(length_y, dtype=jnp.int32)[None, :]
    shift_y = jnp.stack(
        [(y_source == y_target + step).astype(jnp.float32) for step in range(-2, 3)], 0
    )
    x_source = jnp.arange(wide_x, dtype=jnp.int32)[:, None]
    x_target = jnp.arange(depth_x, dtype=jnp.int32)[None, :]
    shift_x = jnp.stack(
        [(x_source == x_target + 2 + step).astype(jnp.float32) for step in range(-2, 3)], 0
    )
    shifted = jnp.einsum("gvy,bzxv->gbzxy", shift_y, padded, precision=lax.Precision.HIGHEST)
    extended = jnp.concatenate(
        [m2l_kernels, jnp.zeros((1, rank_count, rank_count), jnp.float32)], axis=0
    )
    stencil = extended[jnp.asarray(shell_table())]
    summed = jnp.zeros((rank_count, depth_z, depth_x, length_y), jnp.float32)
    for plane in range(5):
        slab = shifted[:, :, plane : plane + depth_z]
        partial_value = jnp.einsum(
            "fgab,gbzpy->afzpy", stencil[plane], slab, precision=lax.Precision.HIGHEST
        )
        summed = summed + jnp.einsum(
            "afzpy,fpq->azqy", partial_value, shift_x, precision=lax.Precision.HIGHEST
        )
    return summed


def shards(
    desc,
    positions,
    species,
    w_in,
    w_mid,
    w_head,
    species_charge,
    m2l_kernels,
    expand_u,
    compress_v,
    send_list,
    slot_box,
):
    atom_count = desc.shape[0]
    total_atoms = atom_count * lax.axis_size(GRP) * lax.axis_size(DEV)
    grad_scale = 1.0 / math.sqrt(total_atoms)
    pre_one = jnp.dot(desc, w_in, preferred_element_type=jnp.float32)
    hidden_one = jax.nn.silu(pre_one).astype(jnp.bfloat16)
    pre_two = jnp.dot(hidden_one, w_mid, preferred_element_type=jnp.float32)
    hidden_two = jax.nn.silu(pre_two)
    species_hot = (
        species[None, :] == jnp.arange(species_charge.shape[0], dtype=jnp.int32)[:, None]
    ).astype(jnp.float32)
    charge = jnp.sum(hidden_two * w_head[None, :], axis=1) + jnp.dot(
        species_charge, species_hot, precision=lax.Precision.HIGHEST
    )
    is_used = send_list >= 0
    side = int(round(math.sqrt(atom_count)))
    atom_high = jnp.where(is_used, send_list // side, -1).reshape(1, -1)
    atom_low = (send_list % side).reshape(1, -1)
    packed = jnp.concatenate([charge[None, :], positions], axis=0)
    outgoing = atoms_to_slots(packed, atom_high, atom_low, slot_box.reshape(1, -1))
    outgoing = outgoing.reshape(outgoing.shape[0], *send_list.shape)
    arrived = lax.all_to_all(outgoing, DEV, split_axis=1, concat_axis=1, tiled=True)
    arrived = arrived.reshape(arrived.shape[0], -1)
    moments = box_sum(arrived, BOXES)
    node_grid = moments.reshape(NODES, BZ, BX, BY)
    reduced = jnp.einsum("nr,nzxy->rzxy", compress_v, node_grid, precision=lax.Precision.HIGHEST)
    padded = extended_2(reduced, ((GRP, 1), (DEV, 2)), 2)
    local_terms = translate(padded, m2l_kernels)
    expansion = jnp.dot(expand_u, local_terms.reshape(RANK, BOXES), precision=lax.Precision.HIGHEST)
    slot_potential = box_pick(expansion, arrived).reshape(send_list.shape)
    returned = lax.all_to_all(slot_potential, DEV, split_axis=0, concat_axis=0, tiled=True)
    potential = slots_to_atoms(returned.reshape(-1), atom_high, atom_low, atom_count)
    head_part = jnp.sum(potential[:, None] * hidden_two, axis=0) * grad_scale
    species_part = jnp.dot(species_hot, potential, precision=lax.Precision.HIGHEST) * grad_scale
    delta_two = (potential[:, None] * w_head[None, :] * silu_slope(pre_two)).astype(jnp.bfloat16)
    mid_part = (
        lax.dot_general(
            hidden_one, delta_two, (((0,), (0,)), ((), ())), preferred_element_type=jnp.float32
        )
        * grad_scale
    )
    back_one = lax.dot_general(
        delta_two, w_mid, (((1,), (1,)), ((), ())), preferred_element_type=jnp.float32
    )
    delta_one = (back_one * silu_slope(pre_one)).astype(jnp.bfloat16)
    in_part = (
        lax.dot_general(
            desc, delta_one, (((0,), (0,)), ((), ())), preferred_element_type=jnp.float32
        )
        * grad_scale
    )
    grad_in, grad_mid, grad_head, grad_species = summed_everywhere(
        (in_part, mid_part, head_part, species_part)
    )
    return (potential, grad_in, grad_mid, grad_head, grad_species)


def solution(mesh):
    torus = Mesh(mesh.devices.reshape(8, 2, 8, 4), ("grp_0", "grp_1", "dev_0", "dev_1"))
    placed = (
        P(GRP_DEV, None),
        P(None, GRP_DEV),
        P(GRP_DEV),
        P(),
        P(),
        P(),
        P(),
        P(),
        P(),
        P(),
        P(GRP_DEV, None),
        P(GRP_DEV, None),
    )
    return jax.shard_map(
        shards,
        mesh=torus,
        in_specs=placed,
        out_specs=(P(GRP_DEV), P(), P(), P(), P()),
        check_vma=False,
    )
```

```python
import math

import jax
import jax.numpy as jnp
import numpy as np
from jax import lax
from jax.experimental import pallas as pl
from jax.sharding import Mesh
from jax.sharding import PartitionSpec as P

NODES = 64
RANK = 16
BZ = 4
BX = 4
BY = 64
BOXES = 1024
GRP = ("grp_0", "grp_1")
DEV = ("dev_0", "dev_1")
GRP_DEV = ("grp_0", "grp_1", "dev_0", "dev_1")


NODE_POINTS = [math.cos((2 * node_number + 1) * math.pi / 8) for node_number in range(4)]


def extended_2(cells, sides, width):
    for axis, dim in sides:
        count = lax.axis_size(axis)
        ends = count - 1
        head = lax.slice_in_dim(cells, 0, width, axis=dim)
        tail = lax.slice_in_dim(cells, cells.shape[dim] - width, cells.shape[dim], axis=dim)
        cells = jnp.concatenate(
            [
                lax.ppermute(tail, axis, [(i, (i + 1) % count) for i in range(ends)]),
                cells,
                lax.ppermute(head, axis, [((i + 1) % count, i) for i in range(ends)]),
            ],
            axis=dim,
        )
    return cells


def in_blocks(x, dim, peers):
    before, after = (x.shape[:dim], x.shape[dim + 1 :])
    return jnp.moveaxis(x.reshape(*before, peers, -1, *after), dim, 0)


def sent_and_summed(x, axis, dim):
    blocks = in_blocks(x, dim, lax.axis_size(axis))
    arrived = lax.all_to_all(blocks, axis, split_axis=0, concat_axis=0, tiled=True)
    return arrived.sum(axis=0)


def sum_in_two_steps(x, axes, dim):
    far, near = axes
    blocks = in_blocks(x, dim, lax.axis_size(far))
    nearer = sent_and_summed(blocks, near, dim + 1)
    arrived = lax.all_to_all(nearer, far, split_axis=0, concat_axis=0, tiled=True)
    return arrived.sum(axis=0)


def padded_to(lines, peers):
    spare = -lines.shape[0] % peers
    if not spare:
        return lines
    return jnp.concatenate([lines, jnp.zeros((spare, *lines.shape[1:]), lines.dtype)])


def sent_to_all(x, axis):
    copies = jnp.broadcast_to(x, (lax.axis_size(axis), *x.shape))
    return lax.all_to_all(copies, axis, split_axis=0, concat_axis=0, tiled=True)


def laid_out(blocks, dim):
    dims = list(blocks.shape[1:])
    dims[dim] *= blocks.shape[0]
    return jnp.moveaxis(blocks, 0, dim).reshape(dims)


def whole_of(x, axes, dim):
    far, near = axes
    blocks = sent_to_all(sent_to_all(x, far), near)
    return laid_out(blocks.swapaxes(0, 1).reshape(-1, *x.shape), dim)


def nested_sum(x, axes):
    own = sum_in_two_steps(padded_to(x, lax.axis_size(axes[0]) * lax.axis_size(axes[1])), axes, 0)
    whole = whole_of(own, axes, 0)
    return whole[: len(x)].reshape(x.shape)


def together(arrays, axis):
    ends = [0]
    for a in arrays:
        ends.append(ends[-1] + a.size)
    total = nested_sum(jnp.concatenate([a.ravel() for a in arrays]), axis)
    return tuple((total[b:e].reshape(a.shape) for a, b, e in zip(arrays, ends, ends[1:])))


def swapped(x, axis, step):
    count = lax.axis_size(axis)
    return lax.ppermute(x, axis, [(i, i ^ step) for i in range(count)])


def butterfly_sum(x, axis):
    step = 1
    while step < lax.axis_size(axis):
        x = x + swapped(x, axis, step)
        step *= 2
    return x


def hybrid_sum(x, pair, plane, stack):
    length = x.shape[0]
    x = butterfly_sum(x, pair)
    peers = lax.axis_size(plane)
    lines = padded_to(x, peers).reshape(peers, -1)
    own = lax.all_to_all(lines, plane, 0, 0, tiled=True).reshape(peers, -1).sum(axis=0)
    own = butterfly_sum(own, stack)
    copies = jnp.broadcast_to(own, (peers, *own.shape))
    return lax.all_to_all(copies, plane, 0, 0, tiled=True).reshape(-1)[:length]


def summed_everywhere(arrays):
    ends = [0]
    for a in arrays:
        ends.append(ends[-1] + a.size)
    flat = jnp.concatenate([a.ravel() for a in arrays])
    total = hybrid_sum(flat, "grp_1", DEV, "grp_0")
    return tuple((total[b:e].reshape(a.shape) for a, b, e in zip(arrays, ends, ends[1:])))


def split_three(x):
    high = lax.reduce_precision(x, exponent_bits=8, mantissa_bits=7)
    rest = x - high
    middle = lax.reduce_precision(rest, exponent_bits=8, mantissa_bits=7)
    return high, middle, rest - middle


def pieces_bf16(x, axis):
    return jnp.concatenate([p.astype(jnp.bfloat16) for p in split_three(x)], axis=axis)


def atoms_to_slots_kernel(table_ref, high_ref, low_ref, box_ref, out_ref):
    rows, tile = out_ref.shape
    rows -= 1
    out_ref[rows : rows + 1, :] = box_ref[...].astype(jnp.float32)
    side = table_ref.shape[1]
    lines = lax.broadcasted_iota(jnp.int32, (side, tile), 0)
    low = (lines == low_ref[...]).astype(jnp.bfloat16)
    parts = jnp.dot(table_ref[...], low, preferred_element_type=jnp.float32)
    block = rows * side
    whole = parts[:block] + parts[block : 2 * block] + parts[2 * block :]
    high = (lines == high_ref[...]).astype(jnp.float32)
    for row in range(rows):
        out_ref[row : row + 1, :] = jnp.sum(
            whole[row * side : (row + 1) * side] * high, axis=0, keepdims=True
        )


def atoms_to_slots(values, high, low, box, tile=4096):
    rows, count = values.shape
    side = int(round(math.sqrt(count)))
    table = pieces_bf16(values.reshape(rows * side, side), 0)
    slots = high.shape[1]
    return pl.pallas_call(
        atoms_to_slots_kernel,
        grid=(slots // tile,),
        in_specs=[
            pl.BlockSpec(table.shape, lambda i: (0, 0)),
            pl.BlockSpec((1, tile), lambda i: (0, i)),
            pl.BlockSpec((1, tile), lambda i: (0, i)),
            pl.BlockSpec((1, tile), lambda i: (0, i)),
        ],
        out_specs=pl.BlockSpec((rows + 1, tile), lambda i: (0, i)),
        out_shape=jax.ShapeDtypeStruct((rows + 1, slots), jnp.float32),
    )(table, high, low, box)


def slots_to_atoms_kernel(value_ref, high_ref, low_ref, out_ref):
    @pl.when(pl.program_id(0) == 0)
    def _():
        out_ref[...] = jnp.zeros_like(out_ref)

    side = out_ref.shape[1]
    tile = high_ref.shape[1]
    lines = lax.broadcasted_iota(jnp.int32, (side, tile), 0)
    hit = lines == high_ref[...]
    low = (lines == low_ref[...]).astype(jnp.bfloat16)
    value = value_ref[...]
    high_part = value.astype(jnp.bfloat16).astype(jnp.float32)
    rest = value - high_part
    middle_part = rest.astype(jnp.bfloat16).astype(jnp.float32)
    low_part = rest - middle_part
    stacked = jnp.concatenate(
        [jnp.where(hit, p, 0.0).astype(jnp.bfloat16) for p in (high_part, middle_part, low_part)],
        axis=0,
    )
    out_ref[...] += lax.dot_general(
        stacked, low, (((1,), (1,)), ((), ())), preferred_element_type=jnp.float32
    )


def slots_to_atoms(values, high, low, count, tile=8192):
    side = int(round(math.sqrt(count)))
    pieces = values.reshape(1, -1)
    slots = values.shape[0]
    parts = pl.pallas_call(
        slots_to_atoms_kernel,
        grid=(slots // tile,),
        in_specs=[
            pl.BlockSpec((1, tile), lambda i: (0, i)),
            pl.BlockSpec((1, tile), lambda i: (0, i)),
            pl.BlockSpec((1, tile), lambda i: (0, i)),
        ],
        out_specs=pl.BlockSpec((3 * side, side), lambda i: (0, 0)),
        out_shape=jax.ShapeDtypeStruct((3 * side, side), jnp.float32),
    )(pieces, high, low)
    return (parts[:side] + parts[side : 2 * side] + parts[2 * side :]).reshape(count)


def node_rows(data_ref, tile):
    nodes = lax.broadcasted_iota(jnp.int32, (NODES, tile), 0)
    spread = []
    for axis, shift in ((0, 4), (1, 2), (2, 0)):
        u = data_ref[1 + axis : 2 + axis, :]
        order_two = 2.0 * u * u - 1.0
        order_three = 4.0 * u * u * u - 3.0 * u
        rows = []
        for node_point in NODE_POINTS:
            cheb_two = 2.0 * node_point * node_point - 1.0
            cheb_three = 4.0 * node_point * node_point * node_point - 3.0 * node_point
            rows.append(0.25 + 0.5 * (node_point * u + cheb_two * order_two + cheb_three * order_three))
        pick = jnp.bitwise_and(jnp.right_shift(nodes, shift), 3)
        full = jnp.broadcast_to(rows[3], (NODES, tile))
        for p in range(3):
            full = jnp.where(pick == p, rows[p], full)
        spread.append(full)
    return spread[0] * spread[1] * spread[2]


def bf16_pieces_in_kernel(x):
    high = x.astype(jnp.bfloat16)
    low = (x - high.astype(jnp.float32)).astype(jnp.bfloat16)
    return jnp.concatenate([high, low], axis=0)


def split_two(x):
    high = lax.reduce_precision(x, exponent_bits=8, mantissa_bits=7)
    return jnp.concatenate(
        [high.astype(jnp.bfloat16), (x - high).astype(jnp.bfloat16)], axis=0
    )


def box_sum_kernel(data_ref, out_ref):
    @pl.when(pl.program_id(0) == 0)
    def _():
        out_ref[...] = jnp.zeros_like(out_ref)

    boxes = out_ref.shape[1]
    tile = data_ref.shape[1]
    box = data_ref[4:5, :].astype(jnp.int32)
    weighted = node_rows(data_ref, tile) * data_ref[0:1, :]
    hot = (lax.broadcasted_iota(jnp.int32, (boxes, tile), 0) == box).astype(jnp.bfloat16)
    out_ref[...] += lax.dot_general(
        bf16_pieces_in_kernel(weighted), hot, (((1,), (1,)), ((), ())),
        preferred_element_type=jnp.float32,
    )


def box_sum(data, boxes, tile=8192):
    rows, slots = data.shape
    parts = pl.pallas_call(
        box_sum_kernel,
        grid=(slots // tile,),
        in_specs=[pl.BlockSpec((rows, tile), lambda i: (0, i))],
        out_specs=pl.BlockSpec((2 * NODES, boxes), lambda i: (0, 0)),
        out_shape=jax.ShapeDtypeStruct((2 * NODES, boxes), jnp.float32),
    )(data)
    return parts[:NODES] + parts[NODES:]


def box_pick_kernel(table_ref, data_ref, out_ref):
    boxes = table_ref.shape[1]
    tile = data_ref.shape[1]
    box = data_ref[4:5, :].astype(jnp.int32)
    hot = (lax.broadcasted_iota(jnp.int32, (boxes, tile), 0) == box).astype(jnp.bfloat16)
    parts = jnp.dot(table_ref[...], hot, preferred_element_type=jnp.float32)
    picked = parts[:NODES] + parts[NODES:]
    out_ref[...] = jnp.sum(node_rows(data_ref, tile) * picked, axis=0, keepdims=True)


def box_pick(table, data, tile=4096):
    rows, slots = data.shape
    stacked = split_two(table)
    return pl.pallas_call(
        box_pick_kernel,
        grid=(slots // tile,),
        in_specs=[
            pl.BlockSpec(stacked.shape, lambda i: (0, 0)),
            pl.BlockSpec((rows, tile), lambda i: (0, i)),
        ],
        out_specs=pl.BlockSpec((1, tile), lambda i: (0, i)),
        out_shape=jax.ShapeDtypeStruct((1, slots), jnp.float32),
    )(stacked, data)[0]


def shell_table():
    table = np.full((5, 5, 5), 98, dtype=np.int32)
    counter = 0
    for shift_z in range(-2, 3):
        for shift_x in range(-2, 3):
            for shift_y in range(-2, 3):
                if max(abs(shift_z), abs(shift_x), abs(shift_y)) == 2:
                    table[shift_z + 2, shift_x + 2, shift_y + 2] = counter
                    counter += 1
    return table


def chebyshev_rows(coordinate):
    order_two = 2.0 * coordinate * coordinate - 1.0
    order_three = 4.0 * coordinate * coordinate * coordinate - 3.0 * coordinate
    stacked = []
    for node_point in NODE_POINTS:
        cheb_two = 2.0 * node_point * node_point - 1.0
        cheb_three = 4.0 * node_point * node_point * node_point - 3.0 * node_point
        stacked.append(
            0.25 + 0.5 * (node_point * coordinate + cheb_two * order_two + cheb_three * order_three)
        )
    return jnp.stack(stacked, 0)


def node_weights(coords):
    along_z = chebyshev_rows(coords[0])
    along_x = chebyshev_rows(coords[1])
    along_y = chebyshev_rows(coords[2])
    product = along_z[:, None, None, :] * along_x[None, :, None, :] * along_y[None, None, :, :]
    return product.reshape(64, coords.shape[1])


def silu_slope(value):
    sigma = jax.nn.sigmoid(value)
    return sigma * (1.0 + value * (1.0 - sigma))


def translate(padded, m2l_kernels):
    rank_count = padded.shape[0]
    depth_z = padded.shape[1] - 4
    wide_x = padded.shape[2]
    depth_x = wide_x - 4
    length_y = padded.shape[3]
    y_source = jnp.arange(length_y, dtype=jnp.int32)[:, None]
    y_target = jnp.arange(length_y, dtype=jnp.int32)[None, :]
    shift_y = jnp.stack(
        [(y_source == y_target + step).astype(jnp.float32) for step in range(-2, 3)], 0
    )
    x_source = jnp.arange(wide_x, dtype=jnp.int32)[:, None]
    x_target = jnp.arange(depth_x, dtype=jnp.int32)[None, :]
    shift_x = jnp.stack(
        [(x_source == x_target + 2 + step).astype(jnp.float32) for step in range(-2, 3)], 0
    )
    shifted = jnp.einsum("gvy,bzxv->gbzxy", shift_y, padded, precision=lax.Precision.HIGHEST)
    extended = jnp.concatenate(
        [m2l_kernels, jnp.zeros((1, rank_count, rank_count), jnp.float32)], axis=0
    )
    stencil = extended[jnp.asarray(shell_table())]
    summed = jnp.zeros((rank_count, depth_z, depth_x, length_y), jnp.float32)
    for plane in range(5):
        slab = shifted[:, :, plane : plane + depth_z]
        partial_value = jnp.einsum(
            "fgab,gbzpy->afzpy", stencil[plane], slab, precision=lax.Precision.HIGHEST
        )
        summed = summed + jnp.einsum(
            "afzpy,fpq->azqy", partial_value, shift_x, precision=lax.Precision.HIGHEST
        )
    return summed


def shards(
    desc,
    positions,
    species,
    w_in,
    w_mid,
    w_head,
    species_charge,
    m2l_kernels,
    expand_u,
    compress_v,
    send_list,
    slot_box,
):
    atom_count = desc.shape[0]
    total_atoms = atom_count * lax.axis_size(GRP) * lax.axis_size(DEV)
    grad_scale = 1.0 / math.sqrt(total_atoms)
    pre_one = jnp.dot(desc, w_in, preferred_element_type=jnp.float32)
    hidden_one = jax.nn.silu(pre_one).astype(jnp.bfloat16)
    pre_two = jnp.dot(hidden_one, w_mid, preferred_element_type=jnp.float32)
    hidden_two = jax.nn.silu(pre_two)
    species_hot = (
        species[None, :] == jnp.arange(species_charge.shape[0], dtype=jnp.int32)[:, None]
    ).astype(jnp.float32)
    charge = jnp.sum(hidden_two * w_head[None, :], axis=1) + jnp.dot(
        species_charge, species_hot, precision=lax.Precision.HIGHEST
    )
    is_used = send_list >= 0
    side = int(round(math.sqrt(atom_count)))
    atom_high = jnp.where(is_used, send_list // side, -1).reshape(1, -1)
    atom_low = (send_list % side).reshape(1, -1)
    packed = jnp.concatenate([charge[None, :], positions], axis=0)
    outgoing = atoms_to_slots(packed, atom_high, atom_low, slot_box.reshape(1, -1))
    outgoing = outgoing.reshape(outgoing.shape[0], *send_list.shape)
    arrived = lax.all_to_all(outgoing, DEV, split_axis=1, concat_axis=1, tiled=True)
    arrived = arrived.reshape(arrived.shape[0], -1)
    moments = box_sum(arrived, BOXES)
    node_grid = moments.reshape(NODES, BZ, BX, BY)
    reduced = jnp.einsum("nr,nzxy->rzxy", compress_v, node_grid, precision=lax.Precision.HIGHEST)
    padded = extended_2(reduced, ((GRP, 1), (DEV, 2)), 2)
    local_terms = translate(padded, m2l_kernels)
    expansion = jnp.dot(expand_u, local_terms.reshape(RANK, BOXES), precision=lax.Precision.HIGHEST)
    slot_potential = box_pick(expansion, arrived).reshape(send_list.shape)
    returned = lax.all_to_all(slot_potential, DEV, split_axis=0, concat_axis=0, tiled=True)
    potential = slots_to_atoms(returned.reshape(-1), atom_high, atom_low, atom_count)
    head_part = jnp.sum(potential[:, None] * hidden_two, axis=0) * grad_scale
    species_part = jnp.dot(species_hot, potential, precision=lax.Precision.HIGHEST) * grad_scale
    delta_two = (potential[:, None] * w_head[None, :] * silu_slope(pre_two)).astype(jnp.bfloat16)
    mid_part = (
        lax.dot_general(
            hidden_one, delta_two, (((0,), (0,)), ((), ())), preferred_element_type=jnp.float32
        )
        * grad_scale
    )
    back_one = lax.dot_general(
        delta_two, w_mid, (((1,), (1,)), ((), ())), preferred_element_type=jnp.float32
    )
    delta_one = (back_one * silu_slope(pre_one)).astype(jnp.bfloat16)
    in_part = (
        lax.dot_general(
            desc, delta_one, (((0,), (0,)), ((), ())), preferred_element_type=jnp.float32
        )
        * grad_scale
    )
    grad_in, grad_mid, grad_head, grad_species = summed_everywhere(
        (in_part, mid_part, head_part, species_part)
    )
    return (potential, grad_in, grad_mid, grad_head, grad_species)


def solution(mesh):
    torus = Mesh(mesh.devices.reshape(8, 2, 8, 4), ("grp_0", "grp_1", "dev_0", "dev_1"))
    placed = (
        P(GRP_DEV, None),
        P(None, GRP_DEV),
        P(GRP_DEV),
        P(),
        P(),
        P(),
        P(),
        P(),
        P(),
        P(),
        P(GRP_DEV, None),
        P(GRP_DEV, None),
    )
    return jax.shard_map(
        shards,
        mesh=torus,
        in_specs=placed,
        out_specs=(P(GRP_DEV), P(), P(), P(), P()),
        check_vma=False,
    )
```
